32 devices in a mesh: wide: 4 (over y, core), narrow: 8 (over z, x).
Axes of the slice: x: 2, y: 2, z: 4, core: 2. Of those that a mesh axis runs over, the one named last changes fastest.
Arguments:
- tokens: bfloat16 [16384, 1024], P(('wide', 'narrow')), may hold values from -6 to 6
- cotangent: bfloat16 [16384, 1024], P(('wide', 'narrow')), may hold values from -6 to 6
- corpus_ids: int32 [8], P('wide'), may hold values from 0 to 7
- corpus_weights: float32 [8], replicated, may hold values from 0.3 to 3
- qkv_weight: bfloat16 [3, 1024, 1024], P(None, None, 'narrow'), may hold values from -0.1875 to 0.1875
- qkv_bias: float32 [3, 1024], P(None, 'narrow'), may hold values from -2 to 2
- out_weight: bfloat16 [1024, 1024], P('narrow'), may hold values from -0.75 to 0.75
- out_bias: float32 [1024], replicated, may hold values from -2 to 2
- up_weight: bfloat16 [1024, 4096], P(None, 'narrow'), may hold values from -0.1875 to 0.1875
- up_bias: float32 [4096], P('narrow'), may hold values from -3 to 3
- down_weight: bfloat16 [4096, 1024], P('narrow'), may hold values from -0.09375 to 0.09375
- down_bias: float32 [1024], replicated, may hold values from -2 to 2
- norm_gains: float32 [4, 1024], replicated, may hold values from 0.5 to 1.5
- norm_biases: float32 [4, 1024], replicated, may hold values from -2 to 2
Outputs:
- layer_out: bfloat16 [16384, 1024], P(('wide', 'narrow'))
- input_grad: bfloat16 [16384, 1024], P(('wide', 'narrow'))
- qkv_wgrad: float32 [3, 1024, 1024], P(None, None, 'narrow')
- qkv_bgrad: float32 [3, 1024], P(None, 'narrow')
- out_wgrad: float32 [1024, 1024], P('narrow')
- out_bgrad: float32 [1024], replicated
- up_wgrad: float32 [1024, 4096], P(None, 'narrow')
- up_bgrad: float32 [4096], P('narrow')
- down_wgrad: float32 [4096, 1024], P('narrow')
- down_bgrad: float32 [1024], replicated
- gain_grads: float32 [4, 1024], replicated
- bias_grads: float32 [4, 1024], replicated
The draws below stay inside these ranges and needn't reach their ends.
All inputs are finite; a program needn't handle non-finite values.
Results may differ from the reference program's by a relative error of at most 0.023.
Values may be sent and summed in bfloat16 or wider, within the bound.
No kernel may reach another device: no remote copies, remote signals or barrier semaphores. Data moves between devices by JAX's collectives and lax.ppermute only.
A program may use at most 256 MiB of HBM per device.

```python
import math
import jax
import jax.numpy as jnp
from jax import lax

D = 1024
HEADS = 16
HEAD = 64
FF = 4096
SEQ = 2048
CORPORA = 8
SEQS = 8
TOKENS = 16384
N_NARROW = 8


def touch_ends(entries, own_key, smallest, top_value):
    shape = entries.shape
    index_at = [jax.random.randint(jax.random.fold_in(own_key, axis), (), 0, shape[axis]) for axis in range(len(shape))]
    entries = entries.at[tuple(index_at)].set(smallest)
    longest = shape.index(max(shape))
    index_at[longest] = (index_at[longest] + 1) % shape[longest]
    return entries.at[tuple(index_at)].set(top_value)


def block_levels(own_key, dims, shards, least, high):
    level, own = 1.0, jax.random.fold_in(own_key, 6)
    for axis_at, shards_of in shards:
        steps = jnp.exp(jax.random.uniform(jax.random.fold_in(own, axis_at), (shards_of,), jnp.float32, least / len(shards), high / len(shards)))
        level = level * jnp.repeat(steps, dims[axis_at] // shards_of).reshape([-1 if axis == axis_at else 1 for axis in range(len(dims))])
    return level


def scatter_about(stream_key, extent, scale, most, shards=(), held_as=jnp.bfloat16):
    result = scale * jax.random.normal(stream_key, extent, jnp.float32)
    if shards:
        result = result * block_levels(stream_key, extent, shards, -0.22, 0.18)
    return jnp.clip(result, -most, most).astype(held_as)


def setup_inputs(seed: int = 0) -> dict:
    key_of = jax.random.split(jax.random.key(seed), 15)
    return {
        "tokens": scatter_about(key_of[0], (TOKENS, D), 1.0, 6.0, ((0, 32),)),
        "cotangent": scatter_about(key_of[1], (TOKENS, D), 1.0, 6.0, ((0, 32),)),
        "corpus_ids": touch_ends(jax.random.randint(key_of[2], (SEQS,), 0, CORPORA), jax.random.fold_in(key_of[2], 1), 0, CORPORA - 1).astype(jnp.int32),
        "corpus_weights": jnp.clip(jnp.exp(jax.random.uniform(key_of[3], (CORPORA,), jnp.float32, math.log(0.3), math.log(3.0))), 0.3, 3.0),
        "qkv_weight": scatter_about(key_of[4], (3, D, D), D ** -0.5, 0.1875, ((2, 8),)),
        "qkv_bias": scatter_about(key_of[5], (3, D), 0.3, 2.0, ((1, 8),), jnp.float32),
        "out_weight": scatter_about(key_of[6], (D, D), HEAD ** -0.5, 0.75, ((0, 8),)),
        "out_bias": scatter_about(key_of[7], (D,), 0.3, 2.0, (), jnp.float32),
        "up_weight": scatter_about(key_of[8], (D, FF), D ** -0.5, 0.1875, ((1, 8),)),
        "up_bias": scatter_about(key_of[9], (FF,), 0.5, 3.0, ((0, 8),), jnp.float32),
        "down_weight": scatter_about(key_of[10], (FF, D), FF ** -0.5, 0.09375, ((0, 8),)),
        "down_bias": scatter_about(key_of[11], (D,), 0.3, 2.0, (), jnp.float32),
        "norm_gains": jnp.clip(1.0 + 0.1 * jax.random.normal(key_of[12], (4, D), jnp.float32), 0.5, 1.5),
        "norm_biases": scatter_about(key_of[13], (4, D), 0.3, 2.0, (), jnp.float32),
    }


epsilon = 1e-05
root_half = 0.7071067811865476
masked_score = -1e+30
highest = lax.Precision.HIGHEST

@jax.custom_vjp
def low(v):
    return lax.optimization_barrier(v.astype(jnp.bfloat16)).astype(jnp.float32)

@jax.custom_vjp
def low_back(v):
    return v

def low_keep(v):
    return (low(v), None)

def low_pass(kept, grad):
    return (grad,)

def back_keep(v):
    return (v, None)

def back_low(kept, grad):
    return (low(grad),)
low.defvjp(low_keep, low_pass)
low_back.defvjp(back_keep, back_low)

def layer_norm(vec_in, gain_row, bias_row):
    center = vec_in - lax.optimization_barrier(jnp.mean(vec_in, axis=-1, keepdims=True))
    inverse = lax.rsqrt(lax.optimization_barrier(jnp.mean(center * center, axis=-1, keepdims=True)) + epsilon)
    return center * inverse * gain_row + bias_row

def rotary_tables(length, head_size):
    half_size = head_size // 2
    inv_freq = jnp.exp(jnp.arange(half_size, dtype=jnp.float32) * (-math.log(10000.0) / half_size))
    angles = jnp.arange(length, dtype=jnp.float32)[:, None] * inv_freq[None, :]
    return (jnp.cos(angles), jnp.sin(angles))

def rotate(vectors, cos_table, sine_table):
    half_size = vectors.shape[-1] // 2
    front_half = vectors[..., :half_size]
    back_half = vectors[..., half_size:]
    cos_grid = cos_table[:, None, :]
    sin_grid = sine_table[:, None, :]
    return jnp.concatenate([front_half * cos_grid - back_half * sin_grid, front_half * sin_grid + back_half * cos_grid], axis=-1)

def gelu_value(hidden):
    return 0.5 * hidden * (1.0 + lax.erf(hidden * root_half))

def attend(query, key_rows, values):
    block_rows = min(512, SEQ)
    score_scale = 1.0 / math.sqrt(HEAD)
    key_pos = jnp.arange(SEQ, dtype=jnp.int32)

    def one_block(block_index):
        row_start = (block_index * block_rows).astype(jnp.int32)
        query_block = lax.dynamic_slice_in_dim(query, row_start, block_rows, 0)
        scores = low_back(jnp.einsum('qhd,khd->hqk', query_block, key_rows, precision=highest) * score_scale)
        query_pos = row_start + jnp.arange(block_rows, dtype=jnp.int32)
        scores = jnp.where(key_pos[None, None, :] <= query_pos[None, :, None], scores, masked_score)
        row_max = lax.optimization_barrier(jnp.max(scores, axis=-1, keepdims=True))
        log_total = row_max + jnp.log(lax.optimization_barrier(jnp.sum(jnp.exp(scores - row_max), axis=-1, keepdims=True)))
        probs_low = low(jnp.exp(scores - log_total))
        return jnp.einsum('hqk,khd->qhd', probs_low, values, precision=highest)
    blocks = lax.map(jax.checkpoint(one_block), jnp.arange(SEQ // block_rows, dtype=jnp.int32))
    return blocks.reshape(SEQ, query.shape[1], HEAD)

def layer_forward(layer_in, qkv_weight, qkv_bias, out_weight, out_bias, up_weight, up_bias, down_weight, down_bias, norm_gains, norm_biases):
    cos_table, sine_table = rotary_tables(SEQ, HEAD)
    inner = D // N_NARROW
    unit_count = FF // N_NARROW
    heads_group = HEADS // N_NARROW
    normed_first = low(layer_norm(layer_in, norm_gains[0], norm_biases[0]))
    branch_sum = jnp.zeros((SEQ, D), jnp.float32)
    for group in range(N_NARROW):
        col_start = group * inner
        col_stop = col_start + inner
        group_in = low_back(normed_first)
        qkv_pre = jnp.einsum('sd,tde->tse', group_in, qkv_weight[:, :, col_start:col_stop], precision=highest)
        qkv_pre = low_back(qkv_pre + qkv_bias[:, None, col_start:col_stop])
        shaped = qkv_pre.reshape(3, SEQ, heads_group, HEAD)
        query = low(rotate(shaped[0], cos_table, sine_table))
        key_rows = low(rotate(shaped[1], cos_table, sine_table))
        values = low(shaped[2])
        attn_out = low(low_back(attend(query, key_rows, values).reshape(SEQ, inner)))
        branch_sum = branch_sum + low(jnp.dot(attn_out, out_weight[col_start:col_stop], precision=highest, preferred_element_type=jnp.float32))
    pre_attn = low_back(branch_sum + out_bias)
    residual = layer_in + layer_norm(pre_attn, norm_gains[1], norm_biases[1])
    normed_third = low(layer_norm(residual, norm_gains[2], norm_biases[2]))
    mlp_sum = jnp.zeros((SEQ, D), jnp.float32)
    for group in range(N_NARROW):
        unit_start = group * unit_count
        unit_stop = unit_start + unit_count
        group_in = low_back(normed_third)
        hidden = jnp.dot(group_in, up_weight[:, unit_start:unit_stop], precision=highest, preferred_element_type=jnp.float32)
        hidden = low_back(hidden + up_bias[unit_start:unit_stop])
        act_low = low(gelu_value(hidden))
        mlp_sum = mlp_sum + low(jnp.dot(act_low, down_weight[unit_start:unit_stop], precision=highest, preferred_element_type=jnp.float32))
    pre_mlp = low_back(mlp_sum + down_bias)
    return residual + layer_norm(pre_mlp, norm_gains[3], norm_biases[3])

def reference(tokens, cotangent, corpus_ids, corpus_weights, qkv_weight, qkv_bias, out_weight, out_bias, up_weight, up_bias, down_weight, down_bias, norm_gains, norm_biases):
    params = (qkv_weight.astype(jnp.float32), qkv_bias.astype(jnp.float32), out_weight.astype(jnp.float32), out_bias.astype(jnp.float32), up_weight.astype(jnp.float32), up_bias.astype(jnp.float32), down_weight.astype(jnp.float32), down_bias.astype(jnp.float32), norm_gains.astype(jnp.float32), norm_biases.astype(jnp.float32))
    layer_in = tokens.astype(jnp.float32).reshape(SEQS, SEQ, D)
    upstream = cotangent.astype(jnp.float32).reshape(SEQS, SEQ, D)
    seq_weight = lax.optimization_barrier(jnp.sum(jnp.where(corpus_ids[:, None] == jnp.arange(CORPORA, dtype=jnp.int32)[None, :], corpus_weights[None, :], 0.0), axis=1))

    def per_sequence(running, item):
        seq_in, seq_up, weight_one = item
        seq_out, pull_back = jax.vjp(layer_forward, seq_in, *params)
        grads_all = pull_back(seq_up * weight_one)
        running = tuple((total_part + fresh for total_part, fresh in zip(running, grads_all[1:])))
        return (running, (seq_out.astype(jnp.bfloat16), grads_all[0].astype(jnp.bfloat16)))
    initial = tuple((jnp.zeros(param.shape, jnp.float32) for param in params))
    running, (outs_all, grads_in) = lax.scan(per_sequence, initial, (layer_in, upstream, seq_weight))
    return (outs_all.reshape(TOKENS, D), grads_in.reshape(TOKENS, D), running[0], running[1], running[2], running[3], running[4], running[5], running[6], running[7], running[8], running[9])
```

```python
import math

import jax
import jax.numpy as jnp
from jax import lax
from jax.sharding import PartitionSpec as P

HEAD = 64


epsilon = 1e-05
root_half = 0.7071067811865476
gauss_norm = 0.3989422804014327
masked_score = -1e30


def norm_stats(vec_in):
    center = vec_in - jnp.mean(vec_in, axis=-1, keepdims=True)
    inverse = lax.rsqrt(jnp.mean(center * center, axis=-1, keepdims=True) + epsilon)
    return (center * inverse, inverse)


def norm_back(normed, inverse, gain_row, upstream):
    scaled = upstream * gain_row
    return inverse * (
        scaled
        - jnp.mean(scaled, axis=-1, keepdims=True)
        - normed * jnp.mean(scaled * normed, axis=-1, keepdims=True)
    )


def rotary_tables(length, head_size):
    half_size = head_size // 2
    inv_freq = jnp.exp(jnp.arange(half_size, dtype=jnp.float32) * (-math.log(10000.0) / half_size))
    angles = jnp.arange(length, dtype=jnp.float32)[:, None] * inv_freq[None, :]
    return (jnp.cos(angles), jnp.sin(angles))


def rotate(vectors, cos_table, sine_table):
    half_size = vectors.shape[-1] // 2
    front_half = vectors[..., :half_size]
    back_half = vectors[..., half_size:]
    cos_grid = cos_table[:, None, :]
    sin_grid = sine_table[:, None, :]
    return jnp.concatenate(
        [
            front_half * cos_grid - back_half * sin_grid,
            front_half * sin_grid + back_half * cos_grid,
        ],
        axis=-1,
    )


def rotate_back(vectors, cos_table, sine_table):
    half_size = vectors.shape[-1] // 2
    front_half = vectors[..., :half_size]
    back_half = vectors[..., half_size:]
    cos_grid = cos_table[:, None, :]
    sin_grid = sine_table[:, None, :]
    return jnp.concatenate(
        [
            front_half * cos_grid + back_half * sin_grid,
            back_half * cos_grid - front_half * sin_grid,
        ],
        axis=-1,
    )


def gelu_value(hidden):
    return 0.5 * hidden * (1.0 + lax.erf(hidden * root_half))


def gelu_slope(hidden):
    return (
        0.5 * (1.0 + lax.erf(hidden * root_half))
        + hidden * jnp.exp(-0.5 * hidden * hidden) * gauss_norm
    )


def project_qkv(gathered, qkv_weight, qkv_bias, cos_table, sine_table, seq_count, length):
    heads_here = qkv_weight.shape[2] // HEAD
    qkv_pre = (
        jnp.einsum("sd,tde->tse", gathered, qkv_weight, preferred_element_type=jnp.float32)
        + qkv_bias[:, None, :]
    )
    shaped = qkv_pre.reshape(3, seq_count, length, heads_here, HEAD)
    query = rotate(shaped[0], cos_table, sine_table).astype(jnp.bfloat16)
    key_rows = rotate(shaped[1], cos_table, sine_table).astype(jnp.bfloat16)
    values = shaped[2].astype(jnp.bfloat16)
    return (query, key_rows, values)


def block_scores(query, key_rows, block_start, block_rows):
    key_stop = block_start + block_rows
    query_block = query[:, block_start:key_stop]
    key_block = key_rows[:, :key_stop]
    scores = jnp.einsum(
        "bqhd,bkhd->bhqk", query_block, key_block, preferred_element_type=jnp.float32
    ) * (1.0 / math.sqrt(HEAD))
    query_pos = block_start + jnp.arange(block_rows)
    key_pos = jnp.arange(key_stop)
    allowed = key_pos[None, :] <= query_pos[:, None]
    return (jnp.where(allowed[None, None], scores, masked_score), query_block, key_block)


def attend_forward(query, key_rows, values, block_rows):
    length = query.shape[1]
    outputs = []
    totals = []
    for block_start in range(0, length, block_rows):
        key_stop = block_start + block_rows
        scores, query_block, key_block = block_scores(query, key_rows, block_start, block_rows)
        row_max = jnp.max(scores, axis=-1, keepdims=True)
        log_total = row_max + jnp.log(jnp.sum(jnp.exp(scores - row_max), axis=-1, keepdims=True))
        probs_low = jnp.exp(scores - log_total).astype(jnp.bfloat16)
        outputs.append(
            jnp.einsum(
                "bhqk,bkhd->bqhd",
                probs_low,
                values[:, :key_stop],
                preferred_element_type=jnp.float32,
            )
        )
        totals.append(log_total)
    return (jnp.concatenate(outputs, axis=1), totals)


def attend_backward(query, key_rows, values, attn_grad, totals, block_rows):
    length = query.shape[1]
    score_scale = 1.0 / math.sqrt(HEAD)
    keys_grad = jnp.zeros(key_rows.shape, jnp.float32)
    values_grad = jnp.zeros(values.shape, jnp.float32)
    query_grads = []
    for block_number, block_start in enumerate(range(0, length, block_rows)):
        key_stop = block_start + block_rows
        scores, query_block, key_block = block_scores(query, key_rows, block_start, block_rows)
        value_block = values[:, :key_stop]
        grad_block = attn_grad[:, block_start:key_stop]
        probs_full = jnp.exp(scores - totals[block_number])
        probs_low = probs_full.astype(jnp.bfloat16)
        probs_grad = jnp.einsum(
            "bqhd,bkhd->bhqk", grad_block, value_block, preferred_element_type=jnp.float32
        )
        row_dot = jnp.sum(probs_full * probs_grad, axis=-1, keepdims=True)
        scores_grad = (probs_full * (probs_grad - row_dot)).astype(jnp.bfloat16)
        query_grads.append(
            jnp.einsum(
                "bhqk,bkhd->bqhd", scores_grad, key_block, preferred_element_type=jnp.float32
            )
            * score_scale
        )
        pad_rows = ((0, 0), (0, length - key_stop), (0, 0), (0, 0))
        keys_grad = keys_grad + jnp.pad(
            jnp.einsum(
                "bhqk,bqhd->bkhd", scores_grad, query_block, preferred_element_type=jnp.float32
            )
            * score_scale,
            pad_rows,
        )
        values_grad = values_grad + jnp.pad(
            jnp.einsum(
                "bhqk,bqhd->bkhd", probs_low, grad_block, preferred_element_type=jnp.float32
            ),
            pad_rows,
        )
    return (
        jnp.concatenate(query_grads, axis=1),
        keys_grad,
        values_grad,
    )


def shards(
    tokens,
    cotangent,
    corpus_ids,
    corpus_weights,
    qkv_weight,
    qkv_bias,
    out_weight,
    out_bias,
    up_weight,
    up_bias,
    down_weight,
    down_bias,
    norm_gains,
    norm_biases,
):
    shard_rows = tokens.shape[0]
    group_rows = shard_rows * lax.axis_size("narrow")
    seq_count = corpus_ids.shape[0]
    length = group_rows // seq_count
    block_rows = min(512, length)
    inner = qkv_weight.shape[2]
    first_row = lax.axis_index("narrow") * shard_rows
    cos_table, sine_table = rotary_tables(length, HEAD)
    layer_in = tokens.astype(jnp.float32)
    normed_first, inverse_first = norm_stats(layer_in)
    low_first = (normed_first * norm_gains[0] + norm_biases[0]).astype(jnp.bfloat16)
    gathered_first = lax.all_gather(low_first, "narrow", axis=0, tiled=True)
    query, key_rows, values = project_qkv(
        gathered_first, qkv_weight, qkv_bias, cos_table, sine_table, seq_count, length
    )
    attn_heads, totals = attend_forward(query, key_rows, values, block_rows)
    attn_low = attn_heads.reshape(group_rows, inner).astype(jnp.bfloat16)
    attn_rows = lax.all_to_all(attn_low, "narrow", 0, 1, tiled=True)
    out_full = lax.all_gather(out_weight, "narrow", axis=0, tiled=True)
    pre_attn = jnp.dot(attn_rows, out_full, preferred_element_type=jnp.float32) + out_bias
    normed_second, inverse_second = norm_stats(pre_attn)
    residual = layer_in + normed_second * norm_gains[1] + norm_biases[1]
    normed_third, inverse_third = norm_stats(residual)
    low_third = (normed_third * norm_gains[2] + norm_biases[2]).astype(jnp.bfloat16)
    gathered_third = lax.all_gather(low_third, "narrow", axis=0, tiled=True)
    hidden = jnp.dot(gathered_third, up_weight, preferred_element_type=jnp.float32) + up_bias
    act_low = gelu_value(hidden).astype(jnp.bfloat16)
    pre_mlp = (
        lax.psum_scatter(
            jnp.dot(act_low, down_weight, preferred_element_type=jnp.float32).astype(jnp.bfloat16),
            "narrow",
            scatter_dimension=0,
            tiled=True,
        ).astype(jnp.float32)
        + down_bias
    )
    normed_fourth, inverse_fourth = norm_stats(pre_mlp)
    final_sum = residual + normed_fourth * norm_gains[3] + norm_biases[3]
    layer_out = final_sum.astype(jnp.bfloat16)
    row_sequence = (first_row + jnp.arange(shard_rows, dtype=jnp.int32)) // length
    row_corpus = jnp.sum(
        jnp.where(
            row_sequence[:, None] == jnp.arange(seq_count, dtype=jnp.int32)[None, :],
            corpus_ids[None, :],
            0,
        ),
        axis=1,
    )
    row_weight = jnp.sum(
        jnp.where(
            row_corpus[:, None] == jnp.arange(corpus_weights.shape[0], dtype=jnp.int32)[None, :],
            corpus_weights[None, :],
            0.0,
        ),
        axis=1,
    )
    upstream = cotangent.astype(jnp.float32) * row_weight[:, None]
    mlp_grad = norm_back(normed_fourth, inverse_fourth, norm_gains[3], upstream).astype(
        jnp.bfloat16
    )
    mlp_full = lax.all_gather(mlp_grad, "narrow", axis=0, tiled=True)
    gathered_third = lax.all_gather(low_third, "narrow", axis=0, tiled=True)
    hidden = jnp.dot(gathered_third, up_weight, preferred_element_type=jnp.float32) + up_bias
    act_low = gelu_value(hidden).astype(jnp.bfloat16)
    down_wgrad = lax.dot_general(
        act_low, mlp_full, (((0,), (0,)), ((), ())), preferred_element_type=jnp.float32
    )
    act_grad = lax.dot_general(
        mlp_full, down_weight, (((1,), (1,)), ((), ())), preferred_element_type=jnp.float32
    )
    hidden_grad = (act_grad * gelu_slope(hidden)).astype(jnp.bfloat16)
    up_bgrad = jnp.sum(hidden_grad.astype(jnp.float32), axis=0)
    up_wgrad = lax.dot_general(
        gathered_third, hidden_grad, (((0,), (0,)), ((), ())), preferred_element_type=jnp.float32
    )
    rows_here = hidden_grad
    third_grad = lax.psum_scatter(
        lax.dot_general(
            rows_here, up_weight, (((1,), (1,)), ((), ())), preferred_element_type=jnp.float32
        ).astype(jnp.bfloat16),
        "narrow",
        scatter_dimension=0,
        tiled=True,
    ).astype(jnp.float32)
    residual_grad = upstream + norm_back(normed_third, inverse_third, norm_gains[2], third_grad)
    branch_grad = norm_back(normed_second, inverse_second, norm_gains[1], residual_grad).astype(
        jnp.bfloat16
    )
    gathered_first = lax.all_gather(low_first, "narrow", axis=0, tiled=True)
    query, key_rows, values = project_qkv(
        gathered_first, qkv_weight, qkv_bias, cos_table, sine_table, seq_count, length
    )
    attn_grad_rows = lax.dot_general(
        branch_grad, out_full, (((1,), (1,)), ((), ())), preferred_element_type=jnp.float32
    ).astype(jnp.bfloat16)
    attn_grad = lax.all_to_all(attn_grad_rows, "narrow", 1, 0, tiled=True)
    attn_grad = attn_grad.reshape(query.shape)
    query_grad, keys_grad, values_grad = attend_backward(
        query, key_rows, values, attn_grad, totals, block_rows
    )
    out_wgrad_rows = lax.dot_general(
        attn_rows, branch_grad, (((0,), (0,)), ((), ())), preferred_element_type=jnp.float32
    )
    out_wgrad = lax.psum_scatter(
        out_wgrad_rows.astype(jnp.bfloat16), "narrow", scatter_dimension=0, tiled=True
    )
    qkv_grad = jnp.stack(
        [
            rotate_back(query_grad, cos_table, sine_table),
            rotate_back(keys_grad, cos_table, sine_table),
            values_grad,
        ]
    )
    qkv_grad = qkv_grad.reshape(3, group_rows, inner).astype(jnp.bfloat16)
    qkv_bgrad = jnp.sum(qkv_grad.astype(jnp.float32), axis=1)
    qkv_wgrad = jnp.einsum(
        "sd,tse->tde", gathered_first, qkv_grad, preferred_element_type=jnp.float32
    )
    rows_here = qkv_grad
    first_grad = lax.psum_scatter(
        jnp.einsum("tse,tde->sd", rows_here, qkv_weight, preferred_element_type=jnp.float32).astype(
            jnp.bfloat16
        ),
        "narrow",
        scatter_dimension=0,
        tiled=True,
    ).astype(jnp.float32)
    input_grad = (
        residual_grad + norm_back(normed_first, inverse_first, norm_gains[0], first_grad)
    ).astype(jnp.bfloat16)
    gain_local = jnp.stack(
        [
            jnp.sum(first_grad * normed_first, axis=0),
            jnp.sum(residual_grad * normed_second, axis=0),
            jnp.sum(third_grad * normed_third, axis=0),
            jnp.sum(upstream * normed_fourth, axis=0),
        ]
    )
    bias_local = jnp.stack(
        [
            jnp.sum(first_grad, axis=0),
            jnp.sum(residual_grad, axis=0),
            jnp.sum(third_grad, axis=0),
            jnp.sum(upstream, axis=0),
        ]
    )
    out_blocal = jnp.sum(branch_grad.astype(jnp.float32), axis=0)
    down_blocal = jnp.sum(mlp_grad.astype(jnp.float32), axis=0)
    weight_sums = (
        lax.psum(qkv_wgrad.astype(jnp.bfloat16), "wide").astype(jnp.float32),
        lax.psum(qkv_bgrad.astype(jnp.bfloat16), "wide").astype(jnp.float32),
        lax.psum(out_wgrad, "wide").astype(jnp.float32),
        lax.psum(up_wgrad.astype(jnp.bfloat16), "wide").astype(jnp.float32),
        lax.psum(up_bgrad.astype(jnp.bfloat16), "wide").astype(jnp.float32),
        lax.psum(down_wgrad.astype(jnp.bfloat16), "wide").astype(jnp.float32),
    )
    small_sums = lax.psum((gain_local, bias_local, out_blocal, down_blocal), ("wide", "narrow"))
    return (
        layer_out,
        input_grad,
        weight_sums[0],
        weight_sums[1],
        weight_sums[2],
        small_sums[2],
        weight_sums[3],
        weight_sums[4],
        weight_sums[5],
        small_sums[3],
        small_sums[0],
        small_sums[1],
    )


def solution(mesh):
    return jax.shard_map(
        shards,
        mesh=mesh,
        in_specs=(
            P(("wide", "narrow"), None),
            P(("wide", "narrow"), None),
            P("wide"),
            P(),
            P(None, None, "narrow"),
            P(None, "narrow"),
            P("narrow", None),
            P(),
            P(None, "narrow"),
            P("narrow"),
            P("narrow", None),
            P(),
            P(),
            P(),
        ),
        out_specs=(
            P(("wide", "narrow"), None),
            P(("wide", "narrow"), None),
            P(None, None, "narrow"),
            P(None, "narrow"),
            P("narrow", None),
            P(),
            P(None, "narrow"),
            P("narrow"),
            P("narrow", None),
            P(),
            P(),
            P(),
        ),
        check_vma=False,
    )
```

```python
import math

import jax
import jax.numpy as jnp
from jax import lax
from jax.sharding import PartitionSpec as P

HEAD = 64


epsilon = 1e-05
root_half = 0.7071067811865476
gauss_norm = 0.3989422804014327
masked_score = -1e30


def norm_stats(vec_in):
    center = vec_in - jnp.mean(vec_in, axis=-1, keepdims=True)
    inverse = lax.rsqrt(jnp.mean(center * center, axis=-1, keepdims=True) + epsilon)
    return (center * inverse, inverse)


def norm_back(normed, inverse, gain_row, upstream):
    scaled = upstream * gain_row
    return inverse * (
        scaled
        - jnp.mean(scaled, axis=-1, keepdims=True)
        - normed * jnp.mean(scaled * normed, axis=-1, keepdims=True)
    )


def rotary_tables(length, head_size):
    half_size = head_size // 2
    inv_freq = jnp.exp(jnp.arange(half_size, dtype=jnp.float32) * (-math.log(10000.0) / half_size))
    angles = jnp.arange(length, dtype=jnp.float32)[:, None] * inv_freq[None, :]
    return (jnp.cos(angles), jnp.sin(angles))


def rotate(vectors, cos_table, sine_table):
    half_size = vectors.shape[-1] // 2
    front_half = vectors[..., :half_size]
    back_half = vectors[..., half_size:]
    cos_grid = cos_table[:, None, :]
    sin_grid = sine_table[:, None, :]
    return jnp.concatenate(
        [
            front_half * cos_grid - back_half * sin_grid,
            front_half * sin_grid + back_half * cos_grid,
        ],
        axis=-1,
    )


def rotate_back(vectors, cos_table, sine_table):
    half_size = vectors.shape[-1] // 2
    front_half = vectors[..., :half_size]
    back_half = vectors[..., half_size:]
    cos_grid = cos_table[:, None, :]
    sin_grid = sine_table[:, None, :]
    return jnp.concatenate(
        [
            front_half * cos_grid + back_half * sin_grid,
            back_half * cos_grid - front_half * sin_grid,
        ],
        axis=-1,
    )


def gelu_value(hidden):
    return 0.5 * hidden * (1.0 + lax.erf(hidden * root_half))


def gelu_slope(hidden):
    return (
        0.5 * (1.0 + lax.erf(hidden * root_half))
        + hidden * jnp.exp(-0.5 * hidden * hidden) * gauss_norm
    )


def project_qkv(gathered, qkv_weight, qkv_bias, cos_table, sine_table, seq_count, length):
    heads_here = qkv_weight.shape[2] // HEAD
    qkv_pre = (
        jnp.einsum("sd,tde->tse", gathered, qkv_weight, preferred_element_type=jnp.float32)
        + qkv_bias[:, None, :]
    )
    shaped = qkv_pre.reshape(3, seq_count, length, heads_here, HEAD)
    query = rotate(shaped[0], cos_table, sine_table).astype(jnp.bfloat16)
    key_rows = rotate(shaped[1], cos_table, sine_table).astype(jnp.bfloat16)
    values = shaped[2].astype(jnp.bfloat16)
    return (query, key_rows, values)


def block_scores(query, key_rows, block_start, block_rows):
    key_stop = block_start + block_rows
    query_block = query[:, block_start:key_stop]
    key_block = key_rows[:, :key_stop]
    scores = jnp.einsum(
        "bqhd,bkhd->bhqk", query_block, key_block, preferred_element_type=jnp.float32
    ) * (1.0 / math.sqrt(HEAD))
    query_pos = block_start + jnp.arange(block_rows)
    key_pos = jnp.arange(key_stop)
    allowed = key_pos[None, :] <= query_pos[:, None]
    return (jnp.where(allowed[None, None], scores, masked_score), query_block, key_block)


def attend_forward(query, key_rows, values, block_rows):
    length = query.shape[1]
    outputs = []
    totals = []
    for block_start in range(0, length, block_rows):
        key_stop = block_start + block_rows
        scores, query_block, key_block = block_scores(query, key_rows, block_start, block_rows)
        row_max = jnp.max(scores, axis=-1, keepdims=True)
        log_total = row_max + jnp.log(jnp.sum(jnp.exp(scores - row_max), axis=-1, keepdims=True))
        probs_low = jnp.exp(scores - log_total).astype(jnp.bfloat16)
        outputs.append(
            jnp.einsum(
                "bhqk,bkhd->bqhd",
                probs_low,
                values[:, :key_stop],
                preferred_element_type=jnp.float32,
            )
        )
        totals.append(log_total)
    return (jnp.concatenate(outputs, axis=1), totals)


def attend_backward(query, key_rows, values, attn_grad, totals, block_rows):
    length = query.shape[1]
    score_scale = 1.0 / math.sqrt(HEAD)
    keys_grad = jnp.zeros(key_rows.shape, jnp.float32)
    values_grad = jnp.zeros(values.shape, jnp.float32)
    query_grads = []
    for block_number, block_start in enumerate(range(0, length, block_rows)):
        key_stop = block_start + block_rows
        scores, query_block, key_block = block_scores(query, key_rows, block_start, block_rows)
        value_block = values[:, :key_stop]
        grad_block = attn_grad[:, block_start:key_stop]
        probs_full = jnp.exp(scores - totals[block_number])
        probs_low = probs_full.astype(jnp.bfloat16)
        probs_grad = jnp.einsum(
            "bqhd,bkhd->bhqk", grad_block, value_block, preferred_element_type=jnp.float32
        )
        row_dot = jnp.sum(probs_full * probs_grad, axis=-1, keepdims=True)
        scores_grad = (probs_full * (probs_grad - row_dot)).astype(jnp.bfloat16)
        query_grads.append(
            jnp.einsum(
                "bhqk,bkhd->bqhd", scores_grad, key_block, preferred_element_type=jnp.float32
            )
            * score_scale
        )
        pad_rows = ((0, 0), (0, length - key_stop), (0, 0), (0, 0))
        keys_grad = keys_grad + jnp.pad(
            jnp.einsum(
                "bhqk,bqhd->bkhd", scores_grad, query_block, preferred_element_type=jnp.float32
            )
            * score_scale,
            pad_rows,
        )
        values_grad = values_grad + jnp.pad(
            jnp.einsum(
                "bhqk,bqhd->bkhd", probs_low, grad_block, preferred_element_type=jnp.float32
            ),
            pad_rows,
        )
    return (
        jnp.concatenate(query_grads, axis=1),
        keys_grad,
        values_grad,
    )


def swap_cores(block):
    count = lax.axis_size("wide")
    return lax.ppermute(block, "wide", [(index, index ^ 1) for index in range(count)])


def gather_halves(shard, core, split_axis, gather_axis):
    half = shard.shape[split_axis] // 2
    mine = lax.dynamic_slice_in_dim(shard, core * half, half, axis=split_axis)
    gathered = lax.all_gather(mine, "narrow", axis=gather_axis, tiled=True)
    partner = swap_cores(gathered)
    first = jnp.where(core == 0, gathered, partner)
    second = jnp.where(core == 0, partner, gathered)
    return jnp.concatenate([first, second], axis=split_axis)


def reduce_halves(rows, core, split_axis, scatter_axis):
    half = rows.shape[split_axis] // 2
    mine = lax.dynamic_slice_in_dim(rows, core * half, half, axis=split_axis)
    other = lax.dynamic_slice_in_dim(rows, (1 - core) * half, half, axis=split_axis)
    chip_sum = mine + swap_cores(other.astype(jnp.bfloat16)).astype(jnp.float32)
    part = lax.psum_scatter(
        chip_sum.astype(jnp.bfloat16), "narrow", scatter_dimension=scatter_axis, tiled=True
    )
    empty = jnp.zeros_like(part)
    return jnp.stack(
        [jnp.where(core == 0, part, empty), jnp.where(core == 0, empty, part)], axis=split_axis
    )


def merge_slots(slots, split_axis):
    shape = list(slots.shape)
    shape[split_axis : split_axis + 2] = [shape[split_axis] * shape[split_axis + 1]]
    return slots.reshape(shape)


def shards(
    tokens,
    cotangent,
    corpus_ids,
    corpus_weights,
    qkv_weight,
    qkv_bias,
    out_weight,
    out_bias,
    up_weight,
    up_bias,
    down_weight,
    down_bias,
    norm_gains,
    norm_biases,
):
    shard_rows = tokens.shape[0]
    group_rows = shard_rows * lax.axis_size("narrow")
    seq_count = corpus_ids.shape[0]
    length = group_rows // seq_count
    block_rows = min(512, length)
    inner = qkv_weight.shape[2]
    first_row = lax.axis_index("narrow") * shard_rows
    cos_table, sine_table = rotary_tables(length, HEAD)
    layer_in = tokens.astype(jnp.float32)
    normed_first, inverse_first = norm_stats(layer_in)
    low_first = (normed_first * norm_gains[0] + norm_biases[0]).astype(jnp.bfloat16)
    gathered_first = lax.all_gather(low_first, "narrow", axis=0, tiled=True)
    query, key_rows, values = project_qkv(
        gathered_first, qkv_weight, qkv_bias, cos_table, sine_table, seq_count, length
    )
    attn_heads, totals = attend_forward(query, key_rows, values, block_rows)
    attn_low = attn_heads.reshape(group_rows, inner).astype(jnp.bfloat16)
    attn_rows = lax.all_to_all(attn_low, "narrow", 0, 1, tiled=True)
    out_full = lax.all_gather(out_weight, "narrow", axis=0, tiled=True)
    pre_attn = jnp.dot(attn_rows, out_full, preferred_element_type=jnp.float32) + out_bias
    normed_second, inverse_second = norm_stats(pre_attn)
    residual = layer_in + normed_second * norm_gains[1] + norm_biases[1]
    normed_third, inverse_third = norm_stats(residual)
    low_third = (normed_third * norm_gains[2] + norm_biases[2]).astype(jnp.bfloat16)
    core = lax.axis_index("wide") % 2
    up_full = gather_halves(up_weight, core, 0, 1)
    down_full = gather_halves(down_weight, core, 1, 0)
    up_bias_full = lax.all_gather(up_bias, "narrow", axis=0, tiled=True)
    hidden = jnp.dot(low_third, up_full, preferred_element_type=jnp.float32) + up_bias_full
    act_low = gelu_value(hidden).astype(jnp.bfloat16)
    pre_mlp = jnp.dot(act_low, down_full, preferred_element_type=jnp.float32) + down_bias
    normed_fourth, inverse_fourth = norm_stats(pre_mlp)
    final_sum = residual + normed_fourth * norm_gains[3] + norm_biases[3]
    layer_out = final_sum.astype(jnp.bfloat16)
    row_sequence = (first_row + jnp.arange(shard_rows, dtype=jnp.int32)) // length
    row_corpus = jnp.sum(
        jnp.where(
            row_sequence[:, None] == jnp.arange(seq_count, dtype=jnp.int32)[None, :],
            corpus_ids[None, :],
            0,
        ),
        axis=1,
    )
    row_weight = jnp.sum(
        jnp.where(
            row_corpus[:, None] == jnp.arange(corpus_weights.shape[0], dtype=jnp.int32)[None, :],
            corpus_weights[None, :],
            0.0,
        ),
        axis=1,
    )
    upstream = cotangent.astype(jnp.float32) * row_weight[:, None]
    mlp_grad = norm_back(normed_fourth, inverse_fourth, norm_gains[3], upstream).astype(
        jnp.bfloat16
    )
    down_wgrad_rows = lax.dot_general(
        act_low, mlp_grad, (((0,), (0,)), ((), ())), preferred_element_type=jnp.float32
    )
    act_grad = lax.dot_general(
        mlp_grad, down_full, (((1,), (1,)), ((), ())), preferred_element_type=jnp.float32
    )
    hidden_grad = (act_grad * gelu_slope(hidden)).astype(jnp.bfloat16)
    up_bgrad_rows = jnp.sum(hidden_grad.astype(jnp.float32), axis=0)
    up_wgrad_rows = lax.dot_general(
        low_third, hidden_grad, (((0,), (0,)), ((), ())), preferred_element_type=jnp.float32
    )
    third_grad = lax.dot_general(
        hidden_grad, up_full, (((1,), (1,)), ((), ())), preferred_element_type=jnp.float32
    )
    up_slots = reduce_halves(up_wgrad_rows, core, 0, 1)
    down_slots = reduce_halves(down_wgrad_rows, core, 1, 0)
    residual_grad = upstream + norm_back(normed_third, inverse_third, norm_gains[2], third_grad)
    branch_grad = norm_back(normed_second, inverse_second, norm_gains[1], residual_grad).astype(
        jnp.bfloat16
    )
    gathered_first = lax.all_gather(low_first, "narrow", axis=0, tiled=True)
    query, key_rows, values = project_qkv(
        gathered_first, qkv_weight, qkv_bias, cos_table, sine_table, seq_count, length
    )
    attn_grad_rows = lax.dot_general(
        branch_grad, out_full, (((1,), (1,)), ((), ())), preferred_element_type=jnp.float32
    ).astype(jnp.bfloat16)
    attn_grad = lax.all_to_all(attn_grad_rows, "narrow", 1, 0, tiled=True)
    attn_grad = attn_grad.reshape(query.shape)
    query_grad, keys_grad, values_grad = attend_backward(
        query, key_rows, values, attn_grad, totals, block_rows
    )
    out_wgrad_rows = lax.dot_general(
        attn_rows, branch_grad, (((0,), (0,)), ((), ())), preferred_element_type=jnp.float32
    )
    out_wgrad = lax.psum_scatter(
        out_wgrad_rows.astype(jnp.bfloat16), "narrow", scatter_dimension=0, tiled=True
    )
    qkv_grad = jnp.stack(
        [
            rotate_back(query_grad, cos_table, sine_table),
            rotate_back(keys_grad, cos_table, sine_table),
            values_grad,
        ]
    )
    qkv_grad = qkv_grad.reshape(3, group_rows, inner).astype(jnp.bfloat16)
    qkv_bgrad = jnp.sum(qkv_grad.astype(jnp.float32), axis=1)
    qkv_wgrad = jnp.einsum(
        "sd,tse->tde", gathered_first, qkv_grad, preferred_element_type=jnp.float32
    )
    rows_here = qkv_grad
    first_grad = lax.psum_scatter(
        jnp.einsum("tse,tde->sd", rows_here, qkv_weight, preferred_element_type=jnp.float32).astype(
            jnp.bfloat16
        ),
        "narrow",
        scatter_dimension=0,
        tiled=True,
    ).astype(jnp.float32)
    input_grad = (
        residual_grad + norm_back(normed_first, inverse_first, norm_gains[0], first_grad)
    ).astype(jnp.bfloat16)
    gain_local = jnp.stack(
        [
            jnp.sum(first_grad * normed_first, axis=0),
            jnp.sum(residual_grad * normed_second, axis=0),
            jnp.sum(third_grad * normed_third, axis=0),
            jnp.sum(upstream * normed_fourth, axis=0),
        ]
    )
    bias_local = jnp.stack(
        [
            jnp.sum(first_grad, axis=0),
            jnp.sum(residual_grad, axis=0),
            jnp.sum(third_grad, axis=0),
            jnp.sum(upstream, axis=0),
        ]
    )
    out_blocal = jnp.sum(branch_grad.astype(jnp.float32), axis=0)
    down_blocal = jnp.sum(mlp_grad.astype(jnp.float32), axis=0)
    weight_sums = (
        lax.psum(qkv_wgrad.astype(jnp.bfloat16), "wide").astype(jnp.float32),
        lax.psum(qkv_bgrad.astype(jnp.bfloat16), "wide").astype(jnp.float32),
        lax.psum(out_wgrad, "wide").astype(jnp.float32),
        lax.psum(up_slots, "wide").astype(jnp.float32),
        None,
        lax.psum(down_slots, "wide").astype(jnp.float32),
    )
    small_sums = lax.psum(
        (gain_local, bias_local, out_blocal, down_blocal, up_bgrad_rows), ("wide", "narrow")
    )
    units = up_bias.shape[0]
    up_bgrad = lax.dynamic_slice_in_dim(small_sums[4], lax.axis_index("narrow") * units, units)
    up_wgrad = merge_slots(weight_sums[3], 0)
    down_wgrad = merge_slots(weight_sums[5], 1)
    return (
        layer_out,
        input_grad,
        weight_sums[0],
        weight_sums[1],
        weight_sums[2],
        small_sums[2],
        up_wgrad,
        up_bgrad,
        down_wgrad,
        small_sums[3],
        small_sums[0],
        small_sums[1],
    )


def solution(mesh):
    return jax.shard_map(
        shards,
        mesh=mesh,
        in_specs=(
            P(("wide", "narrow"), None),
            P(("wide", "narrow"), None),
            P("wide"),
            P(),
            P(None, None, "narrow"),
            P(None, "narrow"),
            P("narrow", None),
            P(),
            P(None, "narrow"),
            P("narrow"),
            P("narrow", None),
            P(),
            P(),
            P(),
        ),
        out_specs=(
            P(("wide", "narrow"), None),
            P(("wide", "narrow"), None),
            P(None, None, "narrow"),
            P(None, "narrow"),
            P("narrow", None),
            P(),
            P(None, "narrow"),
            P("narrow"),
            P("narrow", None),
            P(),
            P(),
            P(),
        ),
        check_vma=False,
    )
```

```python
import math

import jax
import jax.numpy as jnp
from jax import lax
from jax.sharding import PartitionSpec as P

HEAD = 64


epsilon = 1e-05
root_half = 0.7071067811865476
gauss_norm = 0.3989422804014327
masked_score = -1e30


def norm_stats(vec_in):
    center = vec_in - jnp.mean(vec_in, axis=-1, keepdims=True)
    inverse = lax.rsqrt(jnp.mean(center * center, axis=-1, keepdims=True) + epsilon)
    return (center * inverse, inverse)


def norm_back(normed, inverse, gain_row, upstream):
    scaled = upstream * gain_row
    return inverse * (
        scaled
        - jnp.mean(scaled, axis=-1, keepdims=True)
        - normed * jnp.mean(scaled * normed, axis=-1, keepdims=True)
    )


def rotary_tables(length, head_size):
    half_size = head_size // 2
    inv_freq = jnp.exp(jnp.arange(half_size, dtype=jnp.float32) * (-math.log(10000.0) / half_size))
    angles = jnp.arange(length, dtype=jnp.float32)[:, None] * inv_freq[None, :]
    return (jnp.cos(angles), jnp.sin(angles))


def rotate(vectors, cos_table, sine_table):
    half_size = vectors.shape[-1] // 2
    front_half = vectors[..., :half_size]
    back_half = vectors[..., half_size:]
    cos_grid = cos_table[:, None, :]
    sin_grid = sine_table[:, None, :]
    return jnp.concatenate(
        [
            front_half * cos_grid - back_half * sin_grid,
            front_half * sin_grid + back_half * cos_grid,
        ],
        axis=-1,
    )


def rotate_back(vectors, cos_table, sine_table):
    half_size = vectors.shape[-1] // 2
    front_half = vectors[..., :half_size]
    back_half = vectors[..., half_size:]
    cos_grid = cos_table[:, None, :]
    sin_grid = sine_table[:, None, :]
    return jnp.concatenate(
        [
            front_half * cos_grid + back_half * sin_grid,
            back_half * cos_grid - front_half * sin_grid,
        ],
        axis=-1,
    )


def gelu_value(hidden):
    return 0.5 * hidden * (1.0 + lax.erf(hidden * root_half))


def gelu_slope(hidden):
    return (
        0.5 * (1.0 + lax.erf(hidden * root_half))
        + hidden * jnp.exp(-0.5 * hidden * hidden) * gauss_norm
    )


def project_qkv(gathered, qkv_weight, qkv_bias, cos_table, sine_table, seq_count, length):
    heads_here = qkv_weight.shape[2] // HEAD
    qkv_pre = (
        jnp.einsum("sd,tde->tse", gathered, qkv_weight, preferred_element_type=jnp.float32)
        + qkv_bias[:, None, :]
    )
    shaped = qkv_pre.reshape(3, seq_count, length, heads_here, HEAD)
    query = rotate(shaped[0], cos_table, sine_table).astype(jnp.bfloat16)
    key_rows = rotate(shaped[1], cos_table, sine_table).astype(jnp.bfloat16)
    values = shaped[2].astype(jnp.bfloat16)
    return (query, key_rows, values)


def block_scores(query, key_rows, block_start, block_rows):
    key_stop = block_start + block_rows
    query_block = query[:, block_start:key_stop]
    key_block = key_rows[:, :key_stop]
    scores = jnp.einsum(
        "bqhd,bkhd->bhqk", query_block, key_block, preferred_element_type=jnp.float32
    ) * (1.0 / math.sqrt(HEAD))
    query_pos = block_start + jnp.arange(block_rows)
    key_pos = jnp.arange(key_stop)
    allowed = key_pos[None, :] <= query_pos[:, None]
    return (jnp.where(allowed[None, None], scores, masked_score), query_block, key_block)


def attend_forward(query, key_rows, values, block_rows):
    length = query.shape[1]
    outputs = []
    totals = []
    for block_start in range(0, length, block_rows):
        key_stop = block_start + block_rows
        scores, query_block, key_block = block_scores(query, key_rows, block_start, block_rows)
        row_max = jnp.max(scores, axis=-1, keepdims=True)
        log_total = row_max + jnp.log(jnp.sum(jnp.exp(scores - row_max), axis=-1, keepdims=True))
        probs_low = jnp.exp(scores - log_total).astype(jnp.bfloat16)
        outputs.append(
            jnp.einsum(
                "bhqk,bkhd->bqhd",
                probs_low,
                values[:, :key_stop],
                preferred_element_type=jnp.float32,
            )
        )
        totals.append(log_total)
    return (jnp.concatenate(outputs, axis=1), totals)


def attend_backward(query, key_rows, values, attn_grad, totals, block_rows):
    length = query.shape[1]
    score_scale = 1.0 / math.sqrt(HEAD)
    keys_grad = jnp.zeros(key_rows.shape, jnp.float32)
    values_grad = jnp.zeros(values.shape, jnp.float32)
    query_grads = []
    for block_number, block_start in enumerate(range(0, length, block_rows)):
        key_stop = block_start + block_rows
        scores, query_block, key_block = block_scores(query, key_rows, block_start, block_rows)
        value_block = values[:, :key_stop]
        grad_block = attn_grad[:, block_start:key_stop]
        probs_full = jnp.exp(scores - totals[block_number])
        probs_low = probs_full.astype(jnp.bfloat16)
        probs_grad = jnp.einsum(
            "bqhd,bkhd->bhqk", grad_block, value_block, preferred_element_type=jnp.float32
        )
        row_dot = jnp.sum(probs_full * probs_grad, axis=-1, keepdims=True)
        scores_grad = (probs_full * (probs_grad - row_dot)).astype(jnp.bfloat16)
        query_grads.append(
            jnp.einsum(
                "bhqk,bkhd->bqhd", scores_grad, key_block, preferred_element_type=jnp.float32
            )
            * score_scale
        )
        pad_rows = ((0, 0), (0, length - key_stop), (0, 0), (0, 0))
        keys_grad = keys_grad + jnp.pad(
            jnp.einsum(
                "bhqk,bqhd->bkhd", scores_grad, query_block, preferred_element_type=jnp.float32
            )
            * score_scale,
            pad_rows,
        )
        values_grad = values_grad + jnp.pad(
            jnp.einsum(
                "bhqk,bqhd->bkhd", probs_low, grad_block, preferred_element_type=jnp.float32
            ),
            pad_rows,
        )
    return (
        jnp.concatenate(query_grads, axis=1),
        keys_grad,
        values_grad,
    )


def swap_cores(block):
    count = lax.axis_size("wide")
    return lax.ppermute(block, "wide", [(index, index ^ 1) for index in range(count)])


def gather_halves(shard, core, split_axis, gather_axis):
    half = shard.shape[split_axis] // 2
    mine = lax.dynamic_slice_in_dim(shard, core * half, half, axis=split_axis)
    gathered = lax.all_gather(mine, "narrow", axis=gather_axis, tiled=True)
    partner = swap_cores(gathered)
    first = jnp.where(core == 0, gathered, partner)
    second = jnp.where(core == 0, partner, gathered)
    return jnp.concatenate([first, second], axis=split_axis)


def reduce_halves(rows, core, split_axis, scatter_axis):
    half = rows.shape[split_axis] // 2
    mine = lax.dynamic_slice_in_dim(rows, core * half, half, axis=split_axis)
    other = lax.dynamic_slice_in_dim(rows, (1 - core) * half, half, axis=split_axis)
    chip_sum = mine + swap_cores(other.astype(jnp.bfloat16)).astype(jnp.float32)
    part = lax.psum_scatter(
        chip_sum.astype(jnp.bfloat16), "narrow", scatter_dimension=scatter_axis, tiled=True
    )
    empty = jnp.zeros_like(part)
    return jnp.stack(
        [jnp.where(core == 0, part, empty), jnp.where(core == 0, empty, part)], axis=split_axis
    )


def merge_slots(slots, split_axis):
    shape = list(slots.shape)
    shape[split_axis : split_axis + 2] = [shape[split_axis] * shape[split_axis + 1]]
    return slots.reshape(shape)


def shards(
    tokens,
    cotangent,
    corpus_ids,
    corpus_weights,
    qkv_weight,
    qkv_bias,
    out_weight,
    out_bias,
    up_weight,
    up_bias,
    down_weight,
    down_bias,
    norm_gains,
    norm_biases,
):
    shard_rows = tokens.shape[0]
    group_rows = shard_rows * lax.axis_size("narrow")
    seq_count = corpus_ids.shape[0]
    length = group_rows // seq_count
    block_rows = min(512, length)
    inner = qkv_weight.shape[2]
    first_row = lax.axis_index("narrow") * shard_rows
    cos_table, sine_table = rotary_tables(length, HEAD)
    layer_in = tokens.astype(jnp.float32)
    normed_first, inverse_first = norm_stats(layer_in)
    low_first = (normed_first * norm_gains[0] + norm_biases[0]).astype(jnp.bfloat16)
    gathered_first = lax.all_gather(low_first, "narrow", axis=0, tiled=True)
    gathered_first, up_weight, down_weight = lax.optimization_barrier(
        (gathered_first, up_weight, down_weight)
    )
    query, key_rows, values = project_qkv(
        gathered_first, qkv_weight, qkv_bias, cos_table, sine_table, seq_count, length
    )
    attn_heads, totals = attend_forward(query, key_rows, values, block_rows)
    attn_low = attn_heads.reshape(group_rows, inner).astype(jnp.bfloat16)
    attn_rows = lax.all_to_all(attn_low, "narrow", 0, 1, tiled=True)
    out_full = lax.all_gather(out_weight, "narrow", axis=0, tiled=True)
    pre_attn = jnp.dot(attn_rows, out_full, preferred_element_type=jnp.float32) + out_bias
    normed_second, inverse_second = norm_stats(pre_attn)
    residual = layer_in + normed_second * norm_gains[1] + norm_biases[1]
    normed_third, inverse_third = norm_stats(residual)
    low_third = (normed_third * norm_gains[2] + norm_biases[2]).astype(jnp.bfloat16)
    core = lax.axis_index("wide") % 2
    up_full = gather_halves(up_weight, core, 0, 1)
    down_full = gather_halves(down_weight, core, 1, 0)
    up_bias_full = lax.all_gather(up_bias, "narrow", axis=0, tiled=True)
    hidden = jnp.dot(low_third, up_full, preferred_element_type=jnp.float32) + up_bias_full
    act_low = gelu_value(hidden).astype(jnp.bfloat16)
    pre_mlp = jnp.dot(act_low, down_full, preferred_element_type=jnp.float32) + down_bias
    normed_fourth, inverse_fourth = norm_stats(pre_mlp)
    final_sum = residual + normed_fourth * norm_gains[3] + norm_biases[3]
    layer_out = final_sum.astype(jnp.bfloat16)
    row_sequence = (first_row + jnp.arange(shard_rows, dtype=jnp.int32)) // length
    row_corpus = jnp.sum(
        jnp.where(
            row_sequence[:, None] == jnp.arange(seq_count, dtype=jnp.int32)[None, :],
            corpus_ids[None, :],
            0,
        ),
        axis=1,
    )
    row_weight = jnp.sum(
        jnp.where(
            row_corpus[:, None] == jnp.arange(corpus_weights.shape[0], dtype=jnp.int32)[None, :],
            corpus_weights[None, :],
            0.0,
        ),
        axis=1,
    )
    upstream = cotangent.astype(jnp.float32) * row_weight[:, None]
    mlp_grad = norm_back(normed_fourth, inverse_fourth, norm_gains[3], upstream).astype(
        jnp.bfloat16
    )
    down_wgrad_rows = lax.dot_general(
        act_low, mlp_grad, (((0,), (0,)), ((), ())), preferred_element_type=jnp.float32
    )
    act_grad = lax.dot_general(
        mlp_grad, down_full, (((1,), (1,)), ((), ())), preferred_element_type=jnp.float32
    )
    hidden_grad = (act_grad * gelu_slope(hidden)).astype(jnp.bfloat16)
    up_bgrad_rows = jnp.sum(hidden_grad.astype(jnp.float32), axis=0)
    up_wgrad_rows = lax.dot_general(
        low_third, hidden_grad, (((0,), (0,)), ((), ())), preferred_element_type=jnp.float32
    )
    third_grad = lax.dot_general(
        hidden_grad, up_full, (((1,), (1,)), ((), ())), preferred_element_type=jnp.float32
    )
    up_slots = reduce_halves(up_wgrad_rows, core, 0, 1)
    down_slots = reduce_halves(down_wgrad_rows, core, 1, 0)
    residual_grad = upstream + norm_back(normed_third, inverse_third, norm_gains[2], third_grad)
    branch_grad = norm_back(normed_second, inverse_second, norm_gains[1], residual_grad).astype(
        jnp.bfloat16
    )
    gathered_first = lax.all_gather(low_first, "narrow", axis=0, tiled=True)
    query, key_rows, values = project_qkv(
        gathered_first, qkv_weight, qkv_bias, cos_table, sine_table, seq_count, length
    )
    attn_grad_rows = lax.dot_general(
        branch_grad, out_full, (((1,), (1,)), ((), ())), preferred_element_type=jnp.float32
    ).astype(jnp.bfloat16)
    attn_grad = lax.all_to_all(attn_grad_rows, "narrow", 1, 0, tiled=True)
    attn_grad = attn_grad.reshape(query.shape)
    query_grad, keys_grad, values_grad = attend_backward(
        query, key_rows, values, attn_grad, totals, block_rows
    )
    out_wgrad_rows = lax.dot_general(
        attn_rows, branch_grad, (((0,), (0,)), ((), ())), preferred_element_type=jnp.float32
    )
    out_wgrad = lax.psum_scatter(
        out_wgrad_rows.astype(jnp.bfloat16), "narrow", scatter_dimension=0, tiled=True
    )
    qkv_grad = jnp.stack(
        [
            rotate_back(query_grad, cos_table, sine_table),
            rotate_back(keys_grad, cos_table, sine_table),
            values_grad,
        ]
    )
    qkv_grad = qkv_grad.reshape(3, group_rows, inner).astype(jnp.bfloat16)
    qkv_bgrad = jnp.sum(qkv_grad.astype(jnp.float32), axis=1)
    qkv_wgrad = jnp.einsum(
        "sd,tse->tde", gathered_first, qkv_grad, preferred_element_type=jnp.float32
    )
    rows_here = qkv_grad
    first_grad = lax.psum_scatter(
        jnp.einsum("tse,tde->sd", rows_here, qkv_weight, preferred_element_type=jnp.float32).astype(
            jnp.bfloat16
        ),
        "narrow",
        scatter_dimension=0,
        tiled=True,
    ).astype(jnp.float32)
    first_grad, qkv_wgrad, qkv_bgrad, out_wgrad, up_slots, down_slots = lax.optimization_barrier(
        (first_grad, qkv_wgrad, qkv_bgrad, out_wgrad, up_slots, down_slots)
    )
    input_grad = (
        residual_grad + norm_back(normed_first, inverse_first, norm_gains[0], first_grad)
    ).astype(jnp.bfloat16)
    gain_local = jnp.stack(
        [
            jnp.sum(first_grad * normed_first, axis=0),
            jnp.sum(residual_grad * normed_second, axis=0),
            jnp.sum(third_grad * normed_third, axis=0),
            jnp.sum(upstream * normed_fourth, axis=0),
        ]
    )
    bias_local = jnp.stack(
        [
            jnp.sum(first_grad, axis=0),
            jnp.sum(residual_grad, axis=0),
            jnp.sum(third_grad, axis=0),
            jnp.sum(upstream, axis=0),
        ]
    )
    out_blocal = jnp.sum(branch_grad.astype(jnp.float32), axis=0)
    down_blocal = jnp.sum(mlp_grad.astype(jnp.float32), axis=0)
    weight_sums = (
        lax.psum(qkv_wgrad.astype(jnp.bfloat16), "wide").astype(jnp.float32),
        lax.psum(qkv_bgrad.astype(jnp.bfloat16), "wide").astype(jnp.float32),
        lax.psum(out_wgrad, "wide").astype(jnp.float32),
        lax.psum(up_slots, "wide").astype(jnp.float32),
        None,
        lax.psum(down_slots, "wide").astype(jnp.float32),
    )
    small_sums = lax.psum(
        (gain_local, bias_local, out_blocal, down_blocal, up_bgrad_rows), ("wide", "narrow")
    )
    units = up_bias.shape[0]
    up_bgrad = lax.dynamic_slice_in_dim(small_sums[4], lax.axis_index("narrow") * units, units)
    up_wgrad = merge_slots(weight_sums[3], 0)
    down_wgrad = merge_slots(weight_sums[5], 1)
    return (
        layer_out,
        input_grad,
        weight_sums[0],
        weight_sums[1],
        weight_sums[2],
        small_sums[2],
        up_wgrad,
        up_bgrad,
        down_wgrad,
        small_sums[3],
        small_sums[0],
        small_sums[1],
    )


def solution(mesh):
    return jax.shard_map(
        shards,
        mesh=mesh,
        in_specs=(
            P(("wide", "narrow"), None),
            P(("wide", "narrow"), None),
            P("wide"),
            P(),
            P(None, None, "narrow"),
            P(None, "narrow"),
            P("narrow", None),
            P(),
            P(None, "narrow"),
            P("narrow"),
            P("narrow", None),
            P(),
            P(),
            P(),
        ),
        out_specs=(
            P(("wide", "narrow"), None),
            P(("wide", "narrow"), None),
            P(None, None, "narrow"),
            P(None, "narrow"),
            P("narrow", None),
            P(),
            P(None, "narrow"),
            P("narrow"),
            P("narrow", None),
            P(),
            P(),
            P(),
        ),
        check_vma=False,
    )
```

```python
import math

import jax
import jax.numpy as jnp
from jax import lax
from jax.sharding import PartitionSpec as P

HEAD = 64


epsilon = 1e-05
root_half = 0.7071067811865476
gauss_norm = 0.3989422804014327
masked_score = -1e30


def norm_stats(vec_in):
    center = vec_in - jnp.mean(vec_in, axis=-1, keepdims=True)
    inverse = lax.rsqrt(jnp.mean(center * center, axis=-1, keepdims=True) + epsilon)
    return (center * inverse, inverse)


def norm_back(normed, inverse, gain_row, upstream):
    scaled = upstream * gain_row
    return inverse * (
        scaled
        - jnp.mean(scaled, axis=-1, keepdims=True)
        - normed * jnp.mean(scaled * normed, axis=-1, keepdims=True)
    )


def rotary_tables(length, head_size):
    half_size = head_size // 2
    inv_freq = jnp.exp(jnp.arange(half_size, dtype=jnp.float32) * (-math.log(10000.0) / half_size))
    angles = jnp.arange(length, dtype=jnp.float32)[:, None] * inv_freq[None, :]
    return (jnp.cos(angles), jnp.sin(angles))


def rotate(vectors, cos_table, sine_table):
    half_size = vectors.shape[-1] // 2
    front_half = vectors[..., :half_size]
    back_half = vectors[..., half_size:]
    cos_grid = cos_table[:, None, :]
    sin_grid = sine_table[:, None, :]
    return jnp.concatenate(
        [
            front_half * cos_grid - back_half * sin_grid,
            front_half * sin_grid + back_half * cos_grid,
        ],
        axis=-1,
    )


def rotate_back(vectors, cos_table, sine_table):
    half_size = vectors.shape[-1] // 2
    front_half = vectors[..., :half_size]
    back_half = vectors[..., half_size:]
    cos_grid = cos_table[:, None, :]
    sin_grid = sine_table[:, None, :]
    return jnp.concatenate(
        [
            front_half * cos_grid + back_half * sin_grid,
            back_half * cos_grid - front_half * sin_grid,
        ],
        axis=-1,
    )


def gelu_value(hidden):
    return 0.5 * hidden * (1.0 + lax.erf(hidden * root_half))


def gelu_slope(hidden):
    return (
        0.5 * (1.0 + lax.erf(hidden * root_half))
        + hidden * jnp.exp(-0.5 * hidden * hidden) * gauss_norm
    )


def project_qkv(gathered, qkv_weight, qkv_bias, cos_table, sine_table, seq_count, length):
    heads_here = qkv_weight.shape[2] // HEAD
    qkv_pre = (
        jnp.einsum("sd,tde->tse", gathered, qkv_weight, preferred_element_type=jnp.float32)
        + qkv_bias[:, None, :]
    )
    shaped = qkv_pre.reshape(3, seq_count, length, heads_here, HEAD)
    query = rotate(shaped[0], cos_table, sine_table).astype(jnp.bfloat16)
    key_rows = rotate(shaped[1], cos_table, sine_table).astype(jnp.bfloat16)
    values = shaped[2].astype(jnp.bfloat16)
    return (query, key_rows, values)


def block_scores(query, key_rows, block_start, block_rows):
    key_stop = block_start + block_rows
    query_block = query[:, block_start:key_stop]
    key_block = key_rows[:, :key_stop]
    scores = jnp.einsum(
        "bqhd,bkhd->bhqk", query_block, key_block, preferred_element_type=jnp.float32
    ) * (1.0 / math.sqrt(HEAD))
    query_pos = block_start + jnp.arange(block_rows)
    key_pos = jnp.arange(key_stop)
    allowed = key_pos[None, :] <= query_pos[:, None]
    return (jnp.where(allowed[None, None], scores, masked_score), query_block, key_block)


def attend_forward(query, key_rows, values, block_rows):
    length = query.shape[1]
    outputs = []
    totals = []
    for block_start in range(0, length, block_rows):
        key_stop = block_start + block_rows
        scores, query_block, key_block = block_scores(query, key_rows, block_start, block_rows)
        row_max = jnp.max(scores, axis=-1, keepdims=True)
        log_total = row_max + jnp.log(jnp.sum(jnp.exp(scores - row_max), axis=-1, keepdims=True))
        probs_low = jnp.exp(scores - log_total).astype(jnp.bfloat16)
        outputs.append(
            jnp.einsum(
                "bhqk,bkhd->bqhd",
                probs_low,
                values[:, :key_stop],
                preferred_element_type=jnp.float32,
            )
        )
        totals.append(log_total)
    return (jnp.concatenate(outputs, axis=1), totals)


def attend_backward(query, key_rows, values, attn_grad, totals, block_rows):
    length = query.shape[1]
    score_scale = 1.0 / math.sqrt(HEAD)
    keys_grad = jnp.zeros(key_rows.shape, jnp.float32)
    values_grad = jnp.zeros(values.shape, jnp.float32)
    query_grads = []
    for block_number, block_start in enumerate(range(0, length, block_rows)):
        key_stop = block_start + block_rows
        scores, query_block, key_block = block_scores(query, key_rows, block_start, block_rows)
        value_block = values[:, :key_stop]
        grad_block = attn_grad[:, block_start:key_stop]
        probs_full = jnp.exp(scores - totals[block_number])
        probs_low = probs_full.astype(jnp.bfloat16)
        probs_grad = jnp.einsum(
            "bqhd,bkhd->bhqk", grad_block, value_block, preferred_element_type=jnp.float32
        )
        row_dot = jnp.sum(probs_full * probs_grad, axis=-1, keepdims=True)
        scores_grad = (probs_full * (probs_grad - row_dot)).astype(jnp.bfloat16)
        query_grads.append(
            jnp.einsum(
                "bhqk,bkhd->bqhd", scores_grad, key_block, preferred_element_type=jnp.float32
            )
            * score_scale
        )
        pad_rows = ((0, 0), (0, length - key_stop), (0, 0), (0, 0))
        keys_grad = keys_grad + jnp.pad(
            jnp.einsum(
                "bhqk,bqhd->bkhd", scores_grad, query_block, preferred_element_type=jnp.float32
            )
            * score_scale,
            pad_rows,
        )
        values_grad = values_grad + jnp.pad(
            jnp.einsum(
                "bhqk,bqhd->bkhd", probs_low, grad_block, preferred_element_type=jnp.float32
            ),
            pad_rows,
        )
    return (
        jnp.concatenate(query_grads, axis=1),
        keys_grad,
        values_grad,
    )


def swap_cores(block):
    count = lax.axis_size("wide")
    return lax.ppermute(block, "wide", [(index, index ^ 1) for index in range(count)])


def gather_halves(shard, core, split_axis, gather_axis):
    half = shard.shape[split_axis] // 2
    mine = lax.dynamic_slice_in_dim(shard, core * half, half, axis=split_axis)
    gathered = lax.all_gather(mine, "narrow", axis=gather_axis, tiled=True)
    partner = swap_cores(gathered)
    first = jnp.where(core == 0, gathered, partner)
    second = jnp.where(core == 0, partner, gathered)
    return jnp.concatenate([first, second], axis=split_axis)


def reduce_halves(rows, core, split_axis, scatter_axis):
    half = rows.shape[split_axis] // 2
    mine = lax.dynamic_slice_in_dim(rows, core * half, half, axis=split_axis)
    other = lax.dynamic_slice_in_dim(rows, (1 - core) * half, half, axis=split_axis)
    chip_sum = mine + swap_cores(other.astype(jnp.bfloat16)).astype(jnp.float32)
    part = lax.psum_scatter(
        chip_sum.astype(jnp.bfloat16), "narrow", scatter_dimension=scatter_axis, tiled=True
    )
    empty = jnp.zeros_like(part)
    return jnp.stack(
        [jnp.where(core == 0, part, empty), jnp.where(core == 0, empty, part)], axis=split_axis
    )


def reduce_column_halves(mats, core):
    count = lax.axis_size("narrow")
    pieces = []
    for rows in mats:
        half = rows.shape[1] // 2
        mine = lax.dynamic_slice_in_dim(rows, core * half, half, axis=1)
        other = lax.dynamic_slice_in_dim(rows, (1 - core) * half, half, axis=1)
        chip_sum = mine + swap_cores(other.astype(jnp.bfloat16)).astype(jnp.float32)
        pieces.append(chip_sum.astype(jnp.bfloat16).reshape(count, -1, half))
    joined = lax.psum_scatter(
        jnp.concatenate(pieces, axis=1), "narrow", scatter_dimension=0, tiled=True
    )[0]
    results = []
    start = 0
    for piece in pieces:
        part = joined[start : start + piece.shape[1]]
        start += piece.shape[1]
        empty = jnp.zeros_like(part)
        results.append(
            jnp.stack([jnp.where(core == 0, part, empty), jnp.where(core == 0, empty, part)], axis=1)
        )
    return results


def merge_slots(slots, split_axis):
    shape = list(slots.shape)
    shape[split_axis : split_axis + 2] = [shape[split_axis] * shape[split_axis + 1]]
    return slots.reshape(shape)


def shards(
    tokens,
    cotangent,
    corpus_ids,
    corpus_weights,
    qkv_weight,
    qkv_bias,
    out_weight,
    out_bias,
    up_weight,
    up_bias,
    down_weight,
    down_bias,
    norm_gains,
    norm_biases,
):
    shard_rows = tokens.shape[0]
    group_rows = shard_rows * lax.axis_size("narrow")
    seq_count = corpus_ids.shape[0]
    length = group_rows // seq_count
    block_rows = min(512, length)
    inner = qkv_weight.shape[2]
    first_row = lax.axis_index("narrow") * shard_rows
    cos_table, sine_table = rotary_tables(length, HEAD)
    layer_in = tokens.astype(jnp.float32)
    normed_first, inverse_first = norm_stats(layer_in)
    low_first = (normed_first * norm_gains[0] + norm_biases[0]).astype(jnp.bfloat16)
    up_bias_full = lax.all_gather(up_bias, "narrow", axis=0, tiled=True)
    gathered_first = lax.all_gather(low_first, "narrow", axis=0, tiled=True)
    gathered_first, up_weight, down_weight, up_bias_full = lax.optimization_barrier(
        (gathered_first, up_weight, down_weight, up_bias_full)
    )
    query, key_rows, values = project_qkv(
        gathered_first, qkv_weight, qkv_bias, cos_table, sine_table, seq_count, length
    )
    attn_heads, totals = attend_forward(query, key_rows, values, block_rows)
    attn_low = attn_heads.reshape(group_rows, inner).astype(jnp.bfloat16)
    attn_rows = lax.all_to_all(attn_low, "narrow", 0, 1, tiled=True)
    out_full = lax.all_gather(out_weight, "narrow", axis=0, tiled=True)
    pre_attn = jnp.dot(attn_rows, out_full, preferred_element_type=jnp.float32) + out_bias
    normed_second, inverse_second = norm_stats(pre_attn)
    residual = layer_in + normed_second * norm_gains[1] + norm_biases[1]
    normed_third, inverse_third = norm_stats(residual)
    low_third = (normed_third * norm_gains[2] + norm_biases[2]).astype(jnp.bfloat16)
    core = lax.axis_index("wide") % 2
    up_full = gather_halves(up_weight, core, 0, 1)
    down_full = gather_halves(down_weight, core, 1, 0)
    hidden = jnp.dot(low_third, up_full, preferred_element_type=jnp.float32) + up_bias_full
    act_low = gelu_value(hidden).astype(jnp.bfloat16)
    pre_mlp = jnp.dot(act_low, down_full, preferred_element_type=jnp.float32) + down_bias
    normed_fourth, inverse_fourth = norm_stats(pre_mlp)
    final_sum = residual + normed_fourth * norm_gains[3] + norm_biases[3]
    layer_out = final_sum.astype(jnp.bfloat16)
    row_sequence = (first_row + jnp.arange(shard_rows, dtype=jnp.int32)) // length
    row_corpus = jnp.sum(
        jnp.where(
            row_sequence[:, None] == jnp.arange(seq_count, dtype=jnp.int32)[None, :],
            corpus_ids[None, :],
            0,
        ),
        axis=1,
    )
    row_weight = jnp.sum(
        jnp.where(
            row_corpus[:, None] == jnp.arange(corpus_weights.shape[0], dtype=jnp.int32)[None, :],
            corpus_weights[None, :],
            0.0,
        ),
        axis=1,
    )
    upstream = cotangent.astype(jnp.float32) * row_weight[:, None]
    mlp_grad = norm_back(normed_fourth, inverse_fourth, norm_gains[3], upstream).astype(
        jnp.bfloat16
    )
    down_wgrad_rows = lax.dot_general(
        act_low, mlp_grad, (((0,), (0,)), ((), ())), preferred_element_type=jnp.float32
    )
    act_grad = lax.dot_general(
        mlp_grad, down_full, (((1,), (1,)), ((), ())), preferred_element_type=jnp.float32
    )
    hidden_grad = (act_grad * gelu_slope(hidden)).astype(jnp.bfloat16)
    up_bgrad_rows = jnp.sum(hidden_grad.astype(jnp.float32), axis=0)
    up_wgrad_rows = lax.dot_general(
        low_third, hidden_grad, (((0,), (0,)), ((), ())), preferred_element_type=jnp.float32
    )
    third_grad = lax.dot_general(
        hidden_grad, up_full, (((1,), (1,)), ((), ())), preferred_element_type=jnp.float32
    )
    up_slots = reduce_halves(up_wgrad_rows, core, 0, 1)
    residual_grad = upstream + norm_back(normed_third, inverse_third, norm_gains[2], third_grad)
    branch_grad = norm_back(normed_second, inverse_second, norm_gains[1], residual_grad).astype(
        jnp.bfloat16
    )
    gathered_first = lax.all_gather(low_first, "narrow", axis=0, tiled=True)
    query, key_rows, values = project_qkv(
        gathered_first, qkv_weight, qkv_bias, cos_table, sine_table, seq_count, length
    )
    attn_grad_rows = lax.dot_general(
        branch_grad, out_full, (((1,), (1,)), ((), ())), preferred_element_type=jnp.float32
    ).astype(jnp.bfloat16)
    attn_grad = lax.all_to_all(attn_grad_rows, "narrow", 1, 0, tiled=True)
    attn_grad = attn_grad.reshape(query.shape)
    query_grad, keys_grad, values_grad = attend_backward(
        query, key_rows, values, attn_grad, totals, block_rows
    )
    out_wgrad_rows = lax.dot_general(
        attn_rows, branch_grad, (((0,), (0,)), ((), ())), preferred_element_type=jnp.float32
    )
    down_slots, out_slots = reduce_column_halves((down_wgrad_rows, out_wgrad_rows), core)
    qkv_grad = jnp.stack(
        [
            rotate_back(query_grad, cos_table, sine_table),
            rotate_back(keys_grad, cos_table, sine_table),
            values_grad,
        ]
    )
    qkv_grad = qkv_grad.reshape(3, group_rows, inner).astype(jnp.bfloat16)
    qkv_bgrad = jnp.sum(qkv_grad.astype(jnp.float32), axis=1)
    qkv_wgrad = jnp.einsum(
        "sd,tse->tde", gathered_first, qkv_grad, preferred_element_type=jnp.float32
    )
    rows_here = qkv_grad
    first_grad = lax.psum_scatter(
        jnp.einsum("tse,tde->sd", rows_here, qkv_weight, preferred_element_type=jnp.float32).astype(
            jnp.bfloat16
        ),
        "narrow",
        scatter_dimension=0,
        tiled=True,
    ).astype(jnp.float32)
    first_grad, qkv_wgrad, qkv_bgrad = lax.optimization_barrier((first_grad, qkv_wgrad, qkv_bgrad))
    input_grad = (
        residual_grad + norm_back(normed_first, inverse_first, norm_gains[0], first_grad)
    ).astype(jnp.bfloat16)
    gain_local = jnp.stack(
        [
            jnp.sum(first_grad * normed_first, axis=0),
            jnp.sum(residual_grad * normed_second, axis=0),
            jnp.sum(third_grad * normed_third, axis=0),
            jnp.sum(upstream * normed_fourth, axis=0),
        ]
    )
    bias_local = jnp.stack(
        [
            jnp.sum(first_grad, axis=0),
            jnp.sum(residual_grad, axis=0),
            jnp.sum(third_grad, axis=0),
            jnp.sum(upstream, axis=0),
        ]
    )
    out_blocal = jnp.sum(branch_grad.astype(jnp.float32), axis=0)
    down_blocal = jnp.sum(mlp_grad.astype(jnp.float32), axis=0)
    weight_sums = (
        lax.psum(qkv_wgrad.astype(jnp.bfloat16), "wide").astype(jnp.float32),
        lax.psum(qkv_bgrad.astype(jnp.bfloat16), "wide").astype(jnp.float32),
        lax.psum(out_slots, "wide").astype(jnp.float32),
        lax.psum(up_slots, "wide").astype(jnp.float32),
        None,
        lax.psum(down_slots, "wide").astype(jnp.float32),
    )
    small_sums = lax.psum(
        (gain_local, bias_local, out_blocal, down_blocal, up_bgrad_rows), ("wide", "narrow")
    )
    units = up_bias.shape[0]
    up_bgrad = lax.dynamic_slice_in_dim(small_sums[4], lax.axis_index("narrow") * units, units)
    up_wgrad = merge_slots(weight_sums[3], 0)
    down_wgrad = merge_slots(weight_sums[5], 1)
    out_wgrad = merge_slots(weight_sums[2], 1)
    return (
        layer_out,
        input_grad,
        weight_sums[0],
        weight_sums[1],
        out_wgrad,
        small_sums[2],
        up_wgrad,
        up_bgrad,
        down_wgrad,
        small_sums[3],
        small_sums[0],
        small_sums[1],
    )


def solution(mesh):
    return jax.shard_map(
        shards,
        mesh=mesh,
        in_specs=(
            P(("wide", "narrow"), None),
            P(("wide", "narrow"), None),
            P("wide"),
            P(),
            P(None, None, "narrow"),
            P(None, "narrow"),
            P("narrow", None),
            P(),
            P(None, "narrow"),
            P("narrow"),
            P("narrow", None),
            P(),
            P(),
            P(),
        ),
        out_specs=(
            P(("wide", "narrow"), None),
            P(("wide", "narrow"), None),
            P(None, None, "narrow"),
            P(None, "narrow"),
            P("narrow", None),
            P(),
            P(None, "narrow"),
            P("narrow"),
            P("narrow", None),
            P(),
            P(),
            P(),
        ),
        check_vma=False,
    )
```

```python
import math

import jax
import jax.numpy as jnp
from jax import lax
from jax.sharding import PartitionSpec as P

HEAD = 64


epsilon = 1e-05
root_half = 0.7071067811865476
gauss_norm = 0.3989422804014327
masked_score = -1e30


def norm_stats(vec_in):
    center = vec_in - jnp.mean(vec_in, axis=-1, keepdims=True)
    inverse = lax.rsqrt(jnp.mean(center * center, axis=-1, keepdims=True) + epsilon)
    return (center * inverse, inverse)


def norm_back(normed, inverse, gain_row, upstream):
    scaled = upstream * gain_row
    return inverse * (
        scaled
        - jnp.mean(scaled, axis=-1, keepdims=True)
        - normed * jnp.mean(scaled * normed, axis=-1, keepdims=True)
    )


def rotary_tables(length, head_size):
    half_size = head_size // 2
    inv_freq = jnp.exp(jnp.arange(half_size, dtype=jnp.float32) * (-math.log(10000.0) / half_size))
    angles = jnp.arange(length, dtype=jnp.float32)[:, None] * inv_freq[None, :]
    return (jnp.cos(angles), jnp.sin(angles))


def rotate(vectors, cos_table, sine_table):
    half_size = vectors.shape[-1] // 2
    front_half = vectors[..., :half_size]
    back_half = vectors[..., half_size:]
    cos_grid = cos_table[:, None, :]
    sin_grid = sine_table[:, None, :]
    return jnp.concatenate(
        [
            front_half * cos_grid - back_half * sin_grid,
            front_half * sin_grid + back_half * cos_grid,
        ],
        axis=-1,
    )


def rotate_back(vectors, cos_table, sine_table):
    half_size = vectors.shape[-1] // 2
    front_half = vectors[..., :half_size]
    back_half = vectors[..., half_size:]
    cos_grid = cos_table[:, None, :]
    sin_grid = sine_table[:, None, :]
    return jnp.concatenate(
        [
            front_half * cos_grid + back_half * sin_grid,
            back_half * cos_grid - front_half * sin_grid,
        ],
        axis=-1,
    )


def gelu_value(hidden):
    return 0.5 * hidden * (1.0 + lax.erf(hidden * root_half))


def gelu_slope(hidden):
    return (
        0.5 * (1.0 + lax.erf(hidden * root_half))
        + hidden * jnp.exp(-0.5 * hidden * hidden) * gauss_norm
    )


def project_qkv(gathered, qkv_weight, qkv_bias, cos_table, sine_table, seq_count, length):
    heads_here = qkv_weight.shape[2] // HEAD
    qkv_pre = (
        jnp.einsum("sd,tde->tse", gathered, qkv_weight, preferred_element_type=jnp.float32)
        + qkv_bias[:, None, :]
    )
    shaped = qkv_pre.reshape(3, seq_count, length, heads_here, HEAD)
    query = rotate(shaped[0], cos_table, sine_table).astype(jnp.bfloat16)
    key_rows = rotate(shaped[1], cos_table, sine_table).astype(jnp.bfloat16)
    values = shaped[2].astype(jnp.bfloat16)
    return (query, key_rows, values)


def block_scores(query, key_rows, block_start, block_rows):
    key_stop = block_start + block_rows
    query_block = query[:, block_start:key_stop]
    key_block = key_rows[:, :key_stop]
    scores = jnp.einsum(
        "bqhd,bkhd->bhqk", query_block, key_block, preferred_element_type=jnp.float32
    ) * (1.0 / math.sqrt(HEAD))
    query_pos = block_start + jnp.arange(block_rows)
    key_pos = jnp.arange(key_stop)
    allowed = key_pos[None, :] <= query_pos[:, None]
    return (jnp.where(allowed[None, None], scores, masked_score), query_block, key_block)


def attend_forward(query, key_rows, values, block_rows):
    length = query.shape[1]
    outputs = []
    totals = []
    for block_start in range(0, length, block_rows):
        key_stop = block_start + block_rows
        scores, query_block, key_block = block_scores(query, key_rows, block_start, block_rows)
        row_max = jnp.max(scores, axis=-1, keepdims=True)
        log_total = row_max + jnp.log(jnp.sum(jnp.exp(scores - row_max), axis=-1, keepdims=True))
        probs_low = jnp.exp(scores - log_total).astype(jnp.bfloat16)
        outputs.append(
            jnp.einsum(
                "bhqk,bkhd->bqhd",
                probs_low,
                values[:, :key_stop],
                preferred_element_type=jnp.float32,
            )
        )
        totals.append(log_total)
    return (jnp.concatenate(outputs, axis=1), totals)


def attend_backward(query, key_rows, values, attn_grad, totals, block_rows):
    length = query.shape[1]
    score_scale = 1.0 / math.sqrt(HEAD)
    keys_grad = jnp.zeros(key_rows.shape, jnp.float32)
    values_grad = jnp.zeros(values.shape, jnp.float32)
    query_grads = []
    for block_number, block_start in enumerate(range(0, length, block_rows)):
        key_stop = block_start + block_rows
        scores, query_block, key_block = block_scores(query, key_rows, block_start, block_rows)
        value_block = values[:, :key_stop]
        grad_block = attn_grad[:, block_start:key_stop]
        probs_full = jnp.exp(scores - totals[block_number])
        probs_low = probs_full.astype(jnp.bfloat16)
        probs_grad = jnp.einsum(
            "bqhd,bkhd->bhqk", grad_block, value_block, preferred_element_type=jnp.float32
        )
        row_dot = jnp.sum(probs_full * probs_grad, axis=-1, keepdims=True)
        scores_grad = (probs_full * (probs_grad - row_dot)).astype(jnp.bfloat16)
        query_grads.append(
            jnp.einsum(
                "bhqk,bkhd->bqhd", scores_grad, key_block, preferred_element_type=jnp.float32
            )
            * score_scale
        )
        pad_rows = ((0, 0), (0, length - key_stop), (0, 0), (0, 0))
        keys_grad = keys_grad + jnp.pad(
            jnp.einsum(
                "bhqk,bqhd->bkhd", scores_grad, query_block, preferred_element_type=jnp.float32
            )
            * score_scale,
            pad_rows,
        )
        values_grad = values_grad + jnp.pad(
            jnp.einsum(
                "bhqk,bqhd->bkhd", probs_low, grad_block, preferred_element_type=jnp.float32
            ),
            pad_rows,
        )
    return (
        jnp.concatenate(query_grads, axis=1),
        keys_grad,
        values_grad,
    )


def swap_cores(block):
    count = lax.axis_size("wide")
    return lax.ppermute(block, "wide", [(index, index ^ 1) for index in range(count)])


def gather_mine(shard, core, split_axis, gather_axis):
    half = shard.shape[split_axis] // 2
    mine = lax.dynamic_slice_in_dim(shard, core * half, half, axis=split_axis)
    return lax.all_gather(mine, "narrow", axis=gather_axis, tiled=True)


def gather_halves(shard, core, split_axis, gather_axis):
    return join_halves(gather_mine(shard, core, split_axis, gather_axis), core, split_axis)


def join_halves(gathered, core, split_axis):
    partner = swap_cores(gathered)
    first = jnp.where(core == 0, gathered, partner)
    second = jnp.where(core == 0, partner, gathered)
    return jnp.concatenate([first, second], axis=split_axis)


def reduce_halves(rows, core, split_axis, scatter_axis):
    half = rows.shape[split_axis] // 2
    mine = lax.dynamic_slice_in_dim(rows, core * half, half, axis=split_axis)
    other = lax.dynamic_slice_in_dim(rows, (1 - core) * half, half, axis=split_axis)
    chip_sum = mine + swap_cores(other.astype(jnp.bfloat16)).astype(jnp.float32)
    part = lax.psum_scatter(
        chip_sum.astype(jnp.bfloat16), "narrow", scatter_dimension=scatter_axis, tiled=True
    )
    empty = jnp.zeros_like(part)
    return jnp.stack(
        [jnp.where(core == 0, part, empty), jnp.where(core == 0, empty, part)], axis=split_axis
    )


def reduce_column_halves(mats, core):
    count = lax.axis_size("narrow")
    pieces = []
    for rows in mats:
        half = rows.shape[1] // 2
        mine = lax.dynamic_slice_in_dim(rows, core * half, half, axis=1)
        other = lax.dynamic_slice_in_dim(rows, (1 - core) * half, half, axis=1)
        chip_sum = mine + swap_cores(other.astype(jnp.bfloat16)).astype(jnp.float32)
        pieces.append(chip_sum.astype(jnp.bfloat16).reshape(count, -1, half))
    joined = lax.psum_scatter(
        jnp.concatenate(pieces, axis=1), "narrow", scatter_dimension=0, tiled=True
    )[0]
    results = []
    start = 0
    for piece in pieces:
        part = joined[start : start + piece.shape[1]]
        start += piece.shape[1]
        empty = jnp.zeros_like(part)
        results.append(
            jnp.stack([jnp.where(core == 0, part, empty), jnp.where(core == 0, empty, part)], axis=1)
        )
    return results


def merge_slots(slots, split_axis):
    shape = list(slots.shape)
    shape[split_axis : split_axis + 2] = [shape[split_axis] * shape[split_axis + 1]]
    return slots.reshape(shape)


def shards(
    tokens,
    cotangent,
    corpus_ids,
    corpus_weights,
    qkv_weight,
    qkv_bias,
    out_weight,
    out_bias,
    up_weight,
    up_bias,
    down_weight,
    down_bias,
    norm_gains,
    norm_biases,
):
    shard_rows = tokens.shape[0]
    group_rows = shard_rows * lax.axis_size("narrow")
    seq_count = corpus_ids.shape[0]
    length = group_rows // seq_count
    block_rows = min(512, length)
    inner = qkv_weight.shape[2]
    first_row = lax.axis_index("narrow") * shard_rows
    cos_table, sine_table = rotary_tables(length, HEAD)
    layer_in = tokens.astype(jnp.float32)
    normed_first, inverse_first = norm_stats(layer_in)
    low_first = (normed_first * norm_gains[0] + norm_biases[0]).astype(jnp.bfloat16)
    core = lax.axis_index("wide") % 2
    model = layer_in.shape[1]
    heads_here = inner // HEAD
    bias_flat = jnp.concatenate([qkv_bias.reshape(-1), up_bias])
    bias_full = lax.all_gather(bias_flat, "narrow", axis=0)
    qkv_gathered = gather_mine(qkv_weight, core, 1, 2)
    qkv_gathered, up_weight, down_weight, bias_full = lax.optimization_barrier(
        (qkv_gathered, up_weight, down_weight, bias_full)
    )
    qkv_full = join_halves(qkv_gathered, core, 1)
    qkv_bias_full = jnp.swapaxes(bias_full[:, : 3 * inner].reshape(-1, 3, inner), 0, 1).reshape(
        3, model
    )
    up_bias_full = bias_full[:, 3 * inner :].reshape(-1)
    position_start = first_row % length
    cos_rows = lax.dynamic_slice_in_dim(cos_table, position_start, shard_rows, 0)
    sine_rows = lax.dynamic_slice_in_dim(sine_table, position_start, shard_rows, 0)
    qkv_rows = (
        jnp.einsum("sd,tde->tse", low_first, qkv_full, preferred_element_type=jnp.float32)
        + qkv_bias_full[:, None, :]
    )
    shaped = qkv_rows.reshape(3, shard_rows, model // HEAD, HEAD)
    qkv_tok = jnp.stack(
        [
            rotate(shaped[0], cos_rows, sine_rows),
            rotate(shaped[1], cos_rows, sine_rows),
            shaped[2],
        ]
    ).astype(jnp.bfloat16)
    qkv_heads = lax.all_to_all(qkv_tok, "narrow", 2, 1, tiled=True)
    qkv_heads = qkv_heads.reshape(3, seq_count, length, heads_here, HEAD)
    query, key_rows, values = qkv_heads[0], qkv_heads[1], qkv_heads[2]
    attn_heads, totals = attend_forward(query, key_rows, values, block_rows)
    attn_low = attn_heads.reshape(group_rows, inner).astype(jnp.bfloat16)
    attn_rows = lax.all_to_all(attn_low, "narrow", 0, 1, tiled=True)
    out_full = lax.all_gather(out_weight, "narrow", axis=0, tiled=True)
    pre_attn = jnp.dot(attn_rows, out_full, preferred_element_type=jnp.float32) + out_bias
    normed_second, inverse_second = norm_stats(pre_attn)
    residual = layer_in + normed_second * norm_gains[1] + norm_biases[1]
    normed_third, inverse_third = norm_stats(residual)
    low_third = (normed_third * norm_gains[2] + norm_biases[2]).astype(jnp.bfloat16)
    up_full = gather_halves(up_weight, core, 0, 1)
    down_full = gather_halves(down_weight, core, 1, 0)
    hidden = jnp.dot(low_third, up_full, preferred_element_type=jnp.float32) + up_bias_full
    act_low = gelu_value(hidden).astype(jnp.bfloat16)
    pre_mlp = jnp.dot(act_low, down_full, preferred_element_type=jnp.float32) + down_bias
    normed_fourth, inverse_fourth = norm_stats(pre_mlp)
    final_sum = residual + normed_fourth * norm_gains[3] + norm_biases[3]
    layer_out = final_sum.astype(jnp.bfloat16)
    row_sequence = (first_row + jnp.arange(shard_rows, dtype=jnp.int32)) // length
    row_corpus = jnp.sum(
        jnp.where(
            row_sequence[:, None] == jnp.arange(seq_count, dtype=jnp.int32)[None, :],
            corpus_ids[None, :],
            0,
        ),
        axis=1,
    )
    row_weight = jnp.sum(
        jnp.where(
            row_corpus[:, None] == jnp.arange(corpus_weights.shape[0], dtype=jnp.int32)[None, :],
            corpus_weights[None, :],
            0.0,
        ),
        axis=1,
    )
    upstream = cotangent.astype(jnp.float32) * row_weight[:, None]
    mlp_grad = norm_back(normed_fourth, inverse_fourth, norm_gains[3], upstream).astype(
        jnp.bfloat16
    )
    down_wgrad_rows = lax.dot_general(
        act_low, mlp_grad, (((0,), (0,)), ((), ())), preferred_element_type=jnp.float32
    )
    act_grad = lax.dot_general(
        mlp_grad, down_full, (((1,), (1,)), ((), ())), preferred_element_type=jnp.float32
    )
    hidden_grad = (act_grad * gelu_slope(hidden)).astype(jnp.bfloat16)
    up_bgrad_rows = jnp.sum(hidden_grad.astype(jnp.float32), axis=0)
    up_wgrad_rows = lax.dot_general(
        low_third, hidden_grad, (((0,), (0,)), ((), ())), preferred_element_type=jnp.float32
    )
    third_grad = lax.dot_general(
        hidden_grad, up_full, (((1,), (1,)), ((), ())), preferred_element_type=jnp.float32
    )
    up_slots = reduce_halves(up_wgrad_rows, core, 0, 1)
    residual_grad = upstream + norm_back(normed_third, inverse_third, norm_gains[2], third_grad)
    branch_grad = norm_back(normed_second, inverse_second, norm_gains[1], residual_grad).astype(
        jnp.bfloat16
    )
    attn_grad_rows = lax.dot_general(
        branch_grad, out_full, (((1,), (1,)), ((), ())), preferred_element_type=jnp.float32
    ).astype(jnp.bfloat16)
    attn_grad = lax.all_to_all(attn_grad_rows, "narrow", 1, 0, tiled=True)
    attn_grad = attn_grad.reshape(query.shape)
    query_grad, keys_grad, values_grad = attend_backward(
        query, key_rows, values, attn_grad, totals, block_rows
    )
    out_wgrad_rows = lax.dot_general(
        attn_rows, branch_grad, (((0,), (0,)), ((), ())), preferred_element_type=jnp.float32
    )
    down_slots, out_slots = reduce_column_halves((down_wgrad_rows, out_wgrad_rows), core)
    qkv_grad = jnp.stack(
        [
            rotate_back(query_grad, cos_table, sine_table),
            rotate_back(keys_grad, cos_table, sine_table),
            values_grad,
        ]
    )
    qkv_grad = qkv_grad.reshape(3, group_rows, inner).astype(jnp.bfloat16)
    qkv_bgrad = jnp.sum(qkv_grad.astype(jnp.float32), axis=1)
    qkv_grad_rows = lax.all_to_all(
        qkv_grad.reshape(3, group_rows, heads_here, HEAD), "narrow", 1, 2, tiled=True
    ).reshape(3, shard_rows, model)
    qkv_wgrad_rows = jnp.einsum(
        "sd,tse->tde", low_first, qkv_grad_rows, preferred_element_type=jnp.float32
    )
    first_grad = jnp.einsum(
        "tse,tde->sd", qkv_grad_rows, qkv_full, preferred_element_type=jnp.float32
    )
    qkv_slots = reduce_halves(qkv_wgrad_rows, core, 1, 2)
    input_grad = (
        residual_grad + norm_back(normed_first, inverse_first, norm_gains[0], first_grad)
    ).astype(jnp.bfloat16)
    gain_local = jnp.stack(
        [
            jnp.sum(first_grad * normed_first, axis=0),
            jnp.sum(residual_grad * normed_second, axis=0),
            jnp.sum(third_grad * normed_third, axis=0),
            jnp.sum(upstream * normed_fourth, axis=0),
        ]
    )
    bias_local = jnp.stack(
        [
            jnp.sum(first_grad, axis=0),
            jnp.sum(residual_grad, axis=0),
            jnp.sum(third_grad, axis=0),
            jnp.sum(upstream, axis=0),
        ]
    )
    out_blocal = jnp.sum(branch_grad.astype(jnp.float32), axis=0)
    down_blocal = jnp.sum(mlp_grad.astype(jnp.float32), axis=0)
    weight_sums = (
        lax.psum(qkv_slots, "wide").astype(jnp.float32),
        lax.psum(qkv_bgrad.astype(jnp.bfloat16), "wide").astype(jnp.float32),
        lax.psum(out_slots, "wide").astype(jnp.float32),
        lax.psum(up_slots, "wide").astype(jnp.float32),
        None,
        lax.psum(down_slots, "wide").astype(jnp.float32),
    )
    small_sums = lax.psum(
        (gain_local, bias_local, out_blocal, down_blocal, up_bgrad_rows), ("wide", "narrow")
    )
    units = up_bias.shape[0]
    up_bgrad = lax.dynamic_slice_in_dim(small_sums[4], lax.axis_index("narrow") * units, units)
    up_wgrad = merge_slots(weight_sums[3], 0)
    down_wgrad = merge_slots(weight_sums[5], 1)
    out_wgrad = merge_slots(weight_sums[2], 1)
    qkv_wgrad = merge_slots(weight_sums[0], 1)
    return (
        layer_out,
        input_grad,
        qkv_wgrad,
        weight_sums[1],
        out_wgrad,
        small_sums[2],
        up_wgrad,
        up_bgrad,
        down_wgrad,
        small_sums[3],
        small_sums[0],
        small_sums[1],
    )


def solution(mesh):
    return jax.shard_map(
        shards,
        mesh=mesh,
        in_specs=(
            P(("wide", "narrow"), None),
            P(("wide", "narrow"), None),
            P("wide"),
            P(),
            P(None, None, "narrow"),
            P(None, "narrow"),
            P("narrow", None),
            P(),
            P(None, "narrow"),
            P("narrow"),
            P("narrow", None),
            P(),
            P(),
            P(),
        ),
        out_specs=(
            P(("wide", "narrow"), None),
            P(("wide", "narrow"), None),
            P(None, None, "narrow"),
            P(None, "narrow"),
            P("narrow", None),
            P(),
            P(None, "narrow"),
            P("narrow"),
            P("narrow", None),
            P(),
            P(),
            P(),
        ),
        check_vma=False,
    )
```

```python
import math

import jax
import jax.numpy as jnp
from jax import lax
from jax.sharding import PartitionSpec as P

HEAD = 64


epsilon = 1e-05
root_half = 0.7071067811865476
gauss_norm = 0.3989422804014327
masked_score = -1e30


def norm_stats(vec_in):
    center = vec_in - jnp.mean(vec_in, axis=-1, keepdims=True)
    inverse = lax.rsqrt(jnp.mean(center * center, axis=-1, keepdims=True) + epsilon)
    return (center * inverse, inverse)


def norm_back(normed, inverse, gain_row, upstream):
    scaled = upstream * gain_row
    return inverse * (
        scaled
        - jnp.mean(scaled, axis=-1, keepdims=True)
        - normed * jnp.mean(scaled * normed, axis=-1, keepdims=True)
    )


def rotary_tables(length, head_size):
    half_size = head_size // 2
    inv_freq = jnp.exp(jnp.arange(half_size, dtype=jnp.float32) * (-math.log(10000.0) / half_size))
    angles = jnp.arange(length, dtype=jnp.float32)[:, None] * inv_freq[None, :]
    return (jnp.cos(angles), jnp.sin(angles))


def rotate(vectors, cos_table, sine_table):
    half_size = vectors.shape[-1] // 2
    front_half = vectors[..., :half_size]
    back_half = vectors[..., half_size:]
    cos_grid = cos_table[:, None, :]
    sin_grid = sine_table[:, None, :]
    return jnp.concatenate(
        [
            front_half * cos_grid - back_half * sin_grid,
            front_half * sin_grid + back_half * cos_grid,
        ],
        axis=-1,
    )


def rotate_back(vectors, cos_table, sine_table):
    half_size = vectors.shape[-1] // 2
    front_half = vectors[..., :half_size]
    back_half = vectors[..., half_size:]
    cos_grid = cos_table[:, None, :]
    sin_grid = sine_table[:, None, :]
    return jnp.concatenate(
        [
            front_half * cos_grid + back_half * sin_grid,
            back_half * cos_grid - front_half * sin_grid,
        ],
        axis=-1,
    )


def gelu_value(hidden):
    return 0.5 * hidden * (1.0 + lax.erf(hidden * root_half))


def gelu_slope(hidden):
    return (
        0.5 * (1.0 + lax.erf(hidden * root_half))
        + hidden * jnp.exp(-0.5 * hidden * hidden) * gauss_norm
    )


def project_qkv(gathered, qkv_weight, qkv_bias, cos_table, sine_table, seq_count, length):
    heads_here = qkv_weight.shape[2] // HEAD
    qkv_pre = (
        jnp.einsum("sd,tde->tse", gathered, qkv_weight, preferred_element_type=jnp.float32)
        + qkv_bias[:, None, :]
    )
    shaped = qkv_pre.reshape(3, seq_count, length, heads_here, HEAD)
    query = rotate(shaped[0], cos_table, sine_table).astype(jnp.bfloat16)
    key_rows = rotate(shaped[1], cos_table, sine_table).astype(jnp.bfloat16)
    values = shaped[2].astype(jnp.bfloat16)
    return (query, key_rows, values)


def block_scores(query, key_rows, block_start, block_rows):
    key_stop = block_start + block_rows
    query_block = query[:, block_start:key_stop]
    key_block = key_rows[:, :key_stop]
    scores = jnp.einsum(
        "bqhd,bkhd->bhqk", query_block, key_block, preferred_element_type=jnp.float32
    ) * (1.0 / math.sqrt(HEAD))
    query_pos = block_start + jnp.arange(block_rows)
    key_pos = jnp.arange(key_stop)
    allowed = key_pos[None, :] <= query_pos[:, None]
    return (jnp.where(allowed[None, None], scores, masked_score), query_block, key_block)


def attend_forward(query, key_rows, values, block_rows):
    length = query.shape[1]
    outputs = []
    totals = []
    for block_start in range(0, length, block_rows):
        key_stop = block_start + block_rows
        scores, query_block, key_block = block_scores(query, key_rows, block_start, block_rows)
        row_max = jnp.max(scores, axis=-1, keepdims=True)
        log_total = row_max + jnp.log(jnp.sum(jnp.exp(scores - row_max), axis=-1, keepdims=True))
        probs_low = jnp.exp(scores - log_total).astype(jnp.bfloat16)
        outputs.append(
            jnp.einsum(
                "bhqk,bkhd->bqhd",
                probs_low,
                values[:, :key_stop],
                preferred_element_type=jnp.float32,
            )
        )
        totals.append(log_total)
    return (jnp.concatenate(outputs, axis=1), totals)


def attend_backward(query, key_rows, values, attn_grad, totals, block_rows):
    length = query.shape[1]
    score_scale = 1.0 / math.sqrt(HEAD)
    keys_grad = jnp.zeros(key_rows.shape, jnp.float32)
    values_grad = jnp.zeros(values.shape, jnp.float32)
    query_grads = []
    for block_number, block_start in enumerate(range(0, length, block_rows)):
        key_stop = block_start + block_rows
        scores, query_block, key_block = block_scores(query, key_rows, block_start, block_rows)
        value_block = values[:, :key_stop]
        grad_block = attn_grad[:, block_start:key_stop]
        probs_full = jnp.exp(scores - totals[block_number])
        probs_low = probs_full.astype(jnp.bfloat16)
        probs_grad = jnp.einsum(
            "bqhd,bkhd->bhqk", grad_block, value_block, preferred_element_type=jnp.float32
        )
        row_dot = jnp.sum(probs_full * probs_grad, axis=-1, keepdims=True)
        scores_grad = (probs_full * (probs_grad - row_dot)).astype(jnp.bfloat16)
        query_grads.append(
            jnp.einsum(
                "bhqk,bkhd->bqhd", scores_grad, key_block, preferred_element_type=jnp.float32
            )
            * score_scale
        )
        pad_rows = ((0, 0), (0, length - key_stop), (0, 0), (0, 0))
        keys_grad = keys_grad + jnp.pad(
            jnp.einsum(
                "bhqk,bqhd->bkhd", scores_grad, query_block, preferred_element_type=jnp.float32
            )
            * score_scale,
            pad_rows,
        )
        values_grad = values_grad + jnp.pad(
            jnp.einsum(
                "bhqk,bqhd->bkhd", probs_low, grad_block, preferred_element_type=jnp.float32
            ),
            pad_rows,
        )
    return (
        jnp.concatenate(query_grads, axis=1),
        keys_grad,
        values_grad,
    )


def swap(block, bit):
    count = lax.axis_size("wide")
    return lax.ppermute(block, "wide", [(index, index ^ bit) for index in range(count)])


def order_pair(low_bit, mine, theirs, axis):
    first = jnp.where(low_bit == 0, mine, theirs)
    second = jnp.where(low_bit == 0, theirs, mine)
    return jnp.concatenate([first, second], axis=axis)


def gather_quarter(shard, core, pair, split_axis, gather_axis):
    quarter = shard.shape[split_axis] // 4
    mine = lax.dynamic_slice_in_dim(shard, (2 * core + pair) * quarter, quarter, axis=split_axis)
    return lax.all_gather(mine, "narrow", axis=gather_axis, tiled=True)


def join_quarters(gathered, core, pair, split_axis):
    half = order_pair(pair, gathered, swap(gathered, 2), split_axis)
    return order_pair(core, half, swap(half, 1), split_axis)


def reduce_quarters(rows, core, pair, split_axis):
    half = rows.shape[split_axis] // 2
    mine = lax.dynamic_slice_in_dim(rows, core * half, half, axis=split_axis)
    other = lax.dynamic_slice_in_dim(rows, (1 - core) * half, half, axis=split_axis)
    chip_sum = mine + swap(other.astype(jnp.bfloat16), 1).astype(jnp.float32)
    quarter = half // 2
    keep = lax.dynamic_slice_in_dim(chip_sum, pair * quarter, quarter, axis=split_axis)
    give = lax.dynamic_slice_in_dim(chip_sum, (1 - pair) * quarter, quarter, axis=split_axis)
    return (keep + swap(give.astype(jnp.bfloat16), 2).astype(jnp.float32)).astype(jnp.bfloat16)


def spread_quarters(part, core, pair, split_axis):
    if lax.axis_size("wide") == 4:
        return join_quarters(part, core, pair, split_axis).astype(jnp.float32)
    slot = 2 * core + pair
    empty = jnp.zeros_like(part)
    slots = jnp.stack([jnp.where(slot == index, part, empty) for index in range(4)], axis=split_axis)
    total = lax.psum(slots, "wide")
    shape = list(part.shape)
    shape[split_axis] *= 4
    return total.reshape(shape).astype(jnp.float32)


def reduce_weight(rows, core, pair, split_axis, scatter_axis):
    part = lax.psum_scatter(
        reduce_quarters(rows, core, pair, split_axis),
        "narrow",
        scatter_dimension=scatter_axis,
        tiled=True,
    )
    return spread_quarters(part, core, pair, split_axis)


def reduce_column_weights(mats, core, pair):
    count = lax.axis_size("narrow")
    pieces = [reduce_quarters(rows, core, pair, 1) for rows in mats]
    joined = lax.psum_scatter(
        jnp.concatenate([piece.reshape(count, -1, piece.shape[1]) for piece in pieces], axis=1),
        "narrow",
        scatter_dimension=0,
        tiled=True,
    )[0]
    results = []
    start = 0
    for piece in pieces:
        rows_here = piece.shape[0] // count
        results.append(spread_quarters(joined[start : start + rows_here], core, pair, 1))
        start += rows_here
    return results


def shards(
    tokens,
    cotangent,
    corpus_ids,
    corpus_weights,
    qkv_weight,
    qkv_bias,
    out_weight,
    out_bias,
    up_weight,
    up_bias,
    down_weight,
    down_bias,
    norm_gains,
    norm_biases,
):
    shard_rows = tokens.shape[0]
    group_rows = shard_rows * lax.axis_size("narrow")
    seq_count = corpus_ids.shape[0]
    length = group_rows // seq_count
    block_rows = min(512, length)
    inner = qkv_weight.shape[2]
    first_row = lax.axis_index("narrow") * shard_rows
    cos_table, sine_table = rotary_tables(length, HEAD)
    layer_in = tokens.astype(jnp.float32)
    normed_first, inverse_first = norm_stats(layer_in)
    low_first = (normed_first * norm_gains[0] + norm_biases[0]).astype(jnp.bfloat16)
    core = lax.axis_index("wide") % 2
    model = layer_in.shape[1]
    heads_here = inner // HEAD
    bias_flat = jnp.concatenate([qkv_bias.reshape(-1), up_bias])
    bias_full = lax.all_gather(bias_flat, "narrow", axis=0)
    pair = (lax.axis_index("wide") // 2) % 2
    qkv_gathered = gather_quarter(qkv_weight, core, pair, 1, 2)
    qkv_gathered, up_weight, down_weight, out_weight, bias_full = lax.optimization_barrier(
        (qkv_gathered, up_weight, down_weight, out_weight, bias_full)
    )
    qkv_full = join_quarters(qkv_gathered, core, pair, 1)
    qkv_bias_full = jnp.swapaxes(bias_full[:, : 3 * inner].reshape(-1, 3, inner), 0, 1).reshape(
        3, model
    )
    up_bias_full = bias_full[:, 3 * inner :].reshape(-1)
    position_start = first_row % length
    cos_rows = lax.dynamic_slice_in_dim(cos_table, position_start, shard_rows, 0)
    sine_rows = lax.dynamic_slice_in_dim(sine_table, position_start, shard_rows, 0)
    qkv_rows = (
        jnp.einsum("sd,tde->tse", low_first, qkv_full, preferred_element_type=jnp.float32)
        + qkv_bias_full[:, None, :]
    )
    shaped = qkv_rows.reshape(3, shard_rows, model // HEAD, HEAD)
    qkv_tok = jnp.stack(
        [
            rotate(shaped[0], cos_rows, sine_rows),
            rotate(shaped[1], cos_rows, sine_rows),
            shaped[2],
        ]
    ).astype(jnp.bfloat16)
    qkv_heads = lax.all_to_all(qkv_tok, "narrow", 2, 1, tiled=True)
    qkv_heads = qkv_heads.reshape(3, seq_count, length, heads_here, HEAD)
    query, key_rows, values = qkv_heads[0], qkv_heads[1], qkv_heads[2]
    attn_heads, totals = attend_forward(query, key_rows, values, block_rows)
    attn_low = attn_heads.reshape(group_rows, inner).astype(jnp.bfloat16)
    attn_rows = lax.all_to_all(attn_low, "narrow", 0, 1, tiled=True)
    out_full = join_quarters(gather_quarter(out_weight, core, pair, 1, 0), core, pair, 1)
    pre_attn = jnp.dot(attn_rows, out_full, preferred_element_type=jnp.float32) + out_bias
    normed_second, inverse_second = norm_stats(pre_attn)
    residual = layer_in + normed_second * norm_gains[1] + norm_biases[1]
    normed_third, inverse_third = norm_stats(residual)
    low_third = (normed_third * norm_gains[2] + norm_biases[2]).astype(jnp.bfloat16)
    up_full = join_quarters(gather_quarter(up_weight, core, pair, 0, 1), core, pair, 0)
    down_full = join_quarters(gather_quarter(down_weight, core, pair, 1, 0), core, pair, 1)
    hidden = jnp.dot(low_third, up_full, preferred_element_type=jnp.float32) + up_bias_full
    act_low = gelu_value(hidden).astype(jnp.bfloat16)
    pre_mlp = jnp.dot(act_low, down_full, preferred_element_type=jnp.float32) + down_bias
    normed_fourth, inverse_fourth = norm_stats(pre_mlp)
    final_sum = residual + normed_fourth * norm_gains[3] + norm_biases[3]
    layer_out = final_sum.astype(jnp.bfloat16)
    row_sequence = (first_row + jnp.arange(shard_rows, dtype=jnp.int32)) // length
    row_corpus = jnp.sum(
        jnp.where(
            row_sequence[:, None] == jnp.arange(seq_count, dtype=jnp.int32)[None, :],
            corpus_ids[None, :],
            0,
        ),
        axis=1,
    )
    row_weight = jnp.sum(
        jnp.where(
            row_corpus[:, None] == jnp.arange(corpus_weights.shape[0], dtype=jnp.int32)[None, :],
            corpus_weights[None, :],
            0.0,
        ),
        axis=1,
    )
    upstream = cotangent.astype(jnp.float32) * row_weight[:, None]
    mlp_grad = norm_back(normed_fourth, inverse_fourth, norm_gains[3], upstream).astype(
        jnp.bfloat16
    )
    down_wgrad_rows = lax.dot_general(
        act_low, mlp_grad, (((0,), (0,)), ((), ())), preferred_element_type=jnp.float32
    )
    act_grad = lax.dot_general(
        mlp_grad, down_full, (((1,), (1,)), ((), ())), preferred_element_type=jnp.float32
    )
    hidden_grad = (act_grad * gelu_slope(hidden)).astype(jnp.bfloat16)
    up_bgrad_rows = jnp.sum(hidden_grad.astype(jnp.float32), axis=0)
    up_wgrad_rows = lax.dot_general(
        low_third, hidden_grad, (((0,), (0,)), ((), ())), preferred_element_type=jnp.float32
    )
    third_grad = lax.dot_general(
        hidden_grad, up_full, (((1,), (1,)), ((), ())), preferred_element_type=jnp.float32
    )
    up_wgrad = reduce_weight(up_wgrad_rows, core, pair, 0, 1)
    residual_grad = upstream + norm_back(normed_third, inverse_third, norm_gains[2], third_grad)
    branch_grad = norm_back(normed_second, inverse_second, norm_gains[1], residual_grad).astype(
        jnp.bfloat16
    )
    attn_grad_rows = lax.dot_general(
        branch_grad, out_full, (((1,), (1,)), ((), ())), preferred_element_type=jnp.float32
    ).astype(jnp.bfloat16)
    attn_grad = lax.all_to_all(attn_grad_rows, "narrow", 1, 0, tiled=True)
    attn_grad = attn_grad.reshape(query.shape)
    query_grad, keys_grad, values_grad = attend_backward(
        query, key_rows, values, attn_grad, totals, block_rows
    )
    out_wgrad_rows = lax.dot_general(
        attn_rows, branch_grad, (((0,), (0,)), ((), ())), preferred_element_type=jnp.float32
    )
    down_wgrad, out_wgrad = reduce_column_weights((down_wgrad_rows, out_wgrad_rows), core, pair)
    qkv_grad = jnp.stack(
        [
            rotate_back(query_grad, cos_table, sine_table),
            rotate_back(keys_grad, cos_table, sine_table),
            values_grad,
        ]
    )
    qkv_grad = qkv_grad.reshape(3, group_rows, inner).astype(jnp.bfloat16)
    qkv_bgrad = jnp.sum(qkv_grad.astype(jnp.float32), axis=1)
    qkv_grad_rows = lax.all_to_all(
        qkv_grad.reshape(3, group_rows, heads_here, HEAD), "narrow", 1, 2, tiled=True
    ).reshape(3, shard_rows, model)
    qkv_wgrad_rows = jnp.einsum(
        "sd,tse->tde", low_first, qkv_grad_rows, preferred_element_type=jnp.float32
    )
    first_grad = jnp.einsum(
        "tse,tde->sd", qkv_grad_rows, qkv_full, preferred_element_type=jnp.float32
    )
    qkv_wgrad = reduce_weight(qkv_wgrad_rows, core, pair, 1, 2)
    input_grad = (
        residual_grad + norm_back(normed_first, inverse_first, norm_gains[0], first_grad)
    ).astype(jnp.bfloat16)
    gain_local = jnp.stack(
        [
            jnp.sum(first_grad * normed_first, axis=0),
            jnp.sum(residual_grad * normed_second, axis=0),
            jnp.sum(third_grad * normed_third, axis=0),
            jnp.sum(upstream * normed_fourth, axis=0),
        ]
    )
    bias_local = jnp.stack(
        [
            jnp.sum(first_grad, axis=0),
            jnp.sum(residual_grad, axis=0),
            jnp.sum(third_grad, axis=0),
            jnp.sum(upstream, axis=0),
        ]
    )
    out_blocal = jnp.sum(branch_grad.astype(jnp.float32), axis=0)
    down_blocal = jnp.sum(mlp_grad.astype(jnp.float32), axis=0)
    qkv_bgrad = lax.psum(qkv_bgrad.astype(jnp.bfloat16), "wide").astype(jnp.float32)
    small_sums = lax.psum(
        (gain_local, bias_local, out_blocal, down_blocal, up_bgrad_rows), ("wide", "narrow")
    )
    units = up_bias.shape[0]
    up_bgrad = lax.dynamic_slice_in_dim(small_sums[4], lax.axis_index("narrow") * units, units)
    return (
        layer_out,
        input_grad,
        qkv_wgrad,
        qkv_bgrad,
        out_wgrad,
        small_sums[2],
        up_wgrad,
        up_bgrad,
        down_wgrad,
        small_sums[3],
        small_sums[0],
        small_sums[1],
    )


def solution(mesh):
    return jax.shard_map(
        shards,
        mesh=mesh,
        in_specs=(
            P(("wide", "narrow"), None),
            P(("wide", "narrow"), None),
            P("wide"),
            P(),
            P(None, None, "narrow"),
            P(None, "narrow"),
            P("narrow", None),
            P(),
            P(None, "narrow"),
            P("narrow"),
            P("narrow", None),
            P(),
            P(),
            P(),
        ),
        out_specs=(
            P(("wide", "narrow"), None),
            P(("wide", "narrow"), None),
            P(None, None, "narrow"),
            P(None, "narrow"),
            P("narrow", None),
            P(),
            P(None, "narrow"),
            P("narrow"),
            P("narrow", None),
            P(),
            P(),
            P(),
        ),
        check_vma=False,
    )
```

```python
import math

import jax
import jax.numpy as jnp
from jax import lax
from jax.sharding import PartitionSpec as P

HEAD = 64


epsilon = 1e-05
root_half = 0.7071067811865476
gauss_norm = 0.3989422804014327
masked_score = -1e30


def norm_stats(vec_in):
    center = vec_in - jnp.mean(vec_in, axis=-1, keepdims=True)
    inverse = lax.rsqrt(jnp.mean(center * center, axis=-1, keepdims=True) + epsilon)
    return (center * inverse, inverse)


def norm_back(normed, inverse, gain_row, upstream):
    scaled = upstream * gain_row
    return inverse * (
        scaled
        - jnp.mean(scaled, axis=-1, keepdims=True)
        - normed * jnp.mean(scaled * normed, axis=-1, keepdims=True)
    )


def rotary_tables(length, head_size):
    half_size = head_size // 2
    inv_freq = jnp.exp(jnp.arange(half_size, dtype=jnp.float32) * (-math.log(10000.0) / half_size))
    angles = jnp.arange(length, dtype=jnp.float32)[:, None] * inv_freq[None, :]
    return (jnp.cos(angles), jnp.sin(angles))


def rotate(vectors, cos_table, sine_table):
    half_size = vectors.shape[-1] // 2
    front_half = vectors[..., :half_size]
    back_half = vectors[..., half_size:]
    cos_grid = cos_table[:, None, :]
    sin_grid = sine_table[:, None, :]
    return jnp.concatenate(
        [
            front_half * cos_grid - back_half * sin_grid,
            front_half * sin_grid + back_half * cos_grid,
        ],
        axis=-1,
    )


def rotate_back(vectors, cos_table, sine_table):
    half_size = vectors.shape[-1] // 2
    front_half = vectors[..., :half_size]
    back_half = vectors[..., half_size:]
    cos_grid = cos_table[:, None, :]
    sin_grid = sine_table[:, None, :]
    return jnp.concatenate(
        [
            front_half * cos_grid + back_half * sin_grid,
            back_half * cos_grid - front_half * sin_grid,
        ],
        axis=-1,
    )


def gelu_value(hidden):
    return 0.5 * hidden * (1.0 + lax.erf(hidden * root_half))


def gelu_slope(hidden):
    return (
        0.5 * (1.0 + lax.erf(hidden * root_half))
        + hidden * jnp.exp(-0.5 * hidden * hidden) * gauss_norm
    )


def project_qkv(gathered, qkv_weight, qkv_bias, cos_table, sine_table, seq_count, length):
    heads_here = qkv_weight.shape[2] // HEAD
    qkv_pre = (
        jnp.einsum("sd,tde->tse", gathered, qkv_weight, preferred_element_type=jnp.float32)
        + qkv_bias[:, None, :]
    )
    shaped = qkv_pre.reshape(3, seq_count, length, heads_here, HEAD)
    query = rotate(shaped[0], cos_table, sine_table).astype(jnp.bfloat16)
    key_rows = rotate(shaped[1], cos_table, sine_table).astype(jnp.bfloat16)
    values = shaped[2].astype(jnp.bfloat16)
    return (query, key_rows, values)


def block_scores(query, key_rows, block_start, block_rows):
    key_stop = block_start + block_rows
    query_block = query[:, block_start:key_stop]
    key_block = key_rows[:, :key_stop]
    scores = jnp.einsum(
        "bqhd,bkhd->bhqk", query_block, key_block, preferred_element_type=jnp.float32
    ) * (1.0 / math.sqrt(HEAD))
    query_pos = block_start + jnp.arange(block_rows)
    key_pos = jnp.arange(key_stop)
    allowed = key_pos[None, :] <= query_pos[:, None]
    return (jnp.where(allowed[None, None], scores, masked_score), query_block, key_block)


def attend_forward(query, key_rows, values, block_rows):
    length = query.shape[1]
    outputs = []
    totals = []
    for block_start in range(0, length, block_rows):
        key_stop = block_start + block_rows
        scores, query_block, key_block = block_scores(query, key_rows, block_start, block_rows)
        row_max = jnp.max(scores, axis=-1, keepdims=True)
        log_total = row_max + jnp.log(jnp.sum(jnp.exp(scores - row_max), axis=-1, keepdims=True))
        probs_low = jnp.exp(scores - log_total).astype(jnp.bfloat16)
        outputs.append(
            jnp.einsum(
                "bhqk,bkhd->bqhd",
                probs_low,
                values[:, :key_stop],
                preferred_element_type=jnp.float32,
            )
        )
        totals.append(log_total)
    return (jnp.concatenate(outputs, axis=1), totals)


def attend_backward(query, key_rows, values, attn_grad, totals, block_rows):
    length = query.shape[1]
    score_scale = 1.0 / math.sqrt(HEAD)
    keys_grad = jnp.zeros(key_rows.shape, jnp.float32)
    values_grad = jnp.zeros(values.shape, jnp.float32)
    query_grads = []
    for block_number, block_start in enumerate(range(0, length, block_rows)):
        key_stop = block_start + block_rows
        scores, query_block, key_block = block_scores(query, key_rows, block_start, block_rows)
        value_block = values[:, :key_stop]
        grad_block = attn_grad[:, block_start:key_stop]
        probs_full = jnp.exp(scores - totals[block_number])
        probs_low = probs_full.astype(jnp.bfloat16)
        probs_grad = jnp.einsum(
            "bqhd,bkhd->bhqk", grad_block, value_block, preferred_element_type=jnp.float32
        )
        row_dot = jnp.sum(probs_full * probs_grad, axis=-1, keepdims=True)
        scores_grad = (probs_full * (probs_grad - row_dot)).astype(jnp.bfloat16)
        query_grads.append(
            jnp.einsum(
                "bhqk,bkhd->bqhd", scores_grad, key_block, preferred_element_type=jnp.float32
            )
            * score_scale
        )
        pad_rows = ((0, 0), (0, length - key_stop), (0, 0), (0, 0))
        keys_grad = keys_grad + jnp.pad(
            jnp.einsum(
                "bhqk,bqhd->bkhd", scores_grad, query_block, preferred_element_type=jnp.float32
            )
            * score_scale,
            pad_rows,
        )
        values_grad = values_grad + jnp.pad(
            jnp.einsum(
                "bhqk,bqhd->bkhd", probs_low, grad_block, preferred_element_type=jnp.float32
            ),
            pad_rows,
        )
    return (
        jnp.concatenate(query_grads, axis=1),
        keys_grad,
        values_grad,
    )


def swap_cores(block):
    count = lax.axis_size("wide")
    return lax.ppermute(block, "wide", [(index, index ^ 1) for index in range(count)])


def gather_mine(shard, core, split_axis, gather_axis):
    half = shard.shape[split_axis] // 2
    mine = lax.dynamic_slice_in_dim(shard, core * half, half, axis=split_axis)
    return lax.all_gather(mine, "narrow", axis=gather_axis, tiled=True)


def gather_halves(shard, core, split_axis, gather_axis):
    return join_halves(gather_mine(shard, core, split_axis, gather_axis), core, split_axis)


def join_halves(gathered, core, split_axis):
    partner = swap_cores(gathered)
    first = jnp.where(core == 0, gathered, partner)
    second = jnp.where(core == 0, partner, gathered)
    return jnp.concatenate([first, second], axis=split_axis)


def chip_half(rows, core, split_axis):
    half = rows.shape[split_axis] // 2
    mine = lax.dynamic_slice_in_dim(rows, core * half, half, axis=split_axis)
    other = lax.dynamic_slice_in_dim(rows, (1 - core) * half, half, axis=split_axis)
    chip_sum = mine + swap_cores(other.astype(jnp.bfloat16)).astype(jnp.float32)
    return chip_sum.astype(jnp.bfloat16)


def reduce_halves(rows, core, split_axis, scatter_axis):
    return scatter_slots(chip_half(rows, core, split_axis), core, split_axis, scatter_axis)


def scatter_slots(chip_sum, core, split_axis, scatter_axis):
    part = lax.psum_scatter(chip_sum, "narrow", scatter_dimension=scatter_axis, tiled=True)
    empty = jnp.zeros_like(part)
    return jnp.stack(
        [jnp.where(core == 0, part, empty), jnp.where(core == 0, empty, part)], axis=split_axis
    )


def reduce_column_halves(mats, core):
    count = lax.axis_size("narrow")
    pieces = []
    for rows in mats:
        half = rows.shape[1] // 2
        mine = lax.dynamic_slice_in_dim(rows, core * half, half, axis=1)
        other = lax.dynamic_slice_in_dim(rows, (1 - core) * half, half, axis=1)
        chip_sum = mine + swap_cores(other.astype(jnp.bfloat16)).astype(jnp.float32)
        pieces.append(chip_sum.astype(jnp.bfloat16).reshape(count, -1, half))
    joined = lax.psum_scatter(
        jnp.concatenate(pieces, axis=1), "narrow", scatter_dimension=0, tiled=True
    )[0]
    results = []
    start = 0
    for piece in pieces:
        part = joined[start : start + piece.shape[1]]
        start += piece.shape[1]
        empty = jnp.zeros_like(part)
        results.append(
            jnp.stack([jnp.where(core == 0, part, empty), jnp.where(core == 0, empty, part)], axis=1)
        )
    return results


def merge_slots(slots, split_axis):
    shape = list(slots.shape)
    shape[split_axis : split_axis + 2] = [shape[split_axis] * shape[split_axis + 1]]
    return slots.reshape(shape)


def shards(
    tokens,
    cotangent,
    corpus_ids,
    corpus_weights,
    qkv_weight,
    qkv_bias,
    out_weight,
    out_bias,
    up_weight,
    up_bias,
    down_weight,
    down_bias,
    norm_gains,
    norm_biases,
):
    shard_rows = tokens.shape[0]
    group_rows = shard_rows * lax.axis_size("narrow")
    seq_count = corpus_ids.shape[0]
    length = group_rows // seq_count
    block_rows = min(512, length)
    inner = qkv_weight.shape[2]
    first_row = lax.axis_index("narrow") * shard_rows
    cos_table, sine_table = rotary_tables(length, HEAD)
    layer_in = tokens.astype(jnp.float32)
    normed_first, inverse_first = norm_stats(layer_in)
    low_first = (normed_first * norm_gains[0] + norm_biases[0]).astype(jnp.bfloat16)
    core = lax.axis_index("wide") % 2
    model = layer_in.shape[1]
    heads_here = inner // HEAD
    bias_flat = jnp.concatenate([qkv_bias.reshape(-1), up_bias])
    bias_full = lax.all_gather(bias_flat, "narrow", axis=0)
    qkv_gathered = gather_mine(qkv_weight, core, 1, 2)
    qkv_gathered, up_weight, down_weight, bias_full = lax.optimization_barrier(
        (qkv_gathered, up_weight, down_weight, bias_full)
    )
    qkv_full = join_halves(qkv_gathered, core, 1)
    qkv_bias_full = jnp.swapaxes(bias_full[:, : 3 * inner].reshape(-1, 3, inner), 0, 1).reshape(
        3, model
    )
    up_bias_full = bias_full[:, 3 * inner :].reshape(-1)
    position_start = first_row % length
    cos_rows = lax.dynamic_slice_in_dim(cos_table, position_start, shard_rows, 0)
    sine_rows = lax.dynamic_slice_in_dim(sine_table, position_start, shard_rows, 0)
    qkv_rows = (
        jnp.einsum("sd,tde->tse", low_first, qkv_full, preferred_element_type=jnp.float32)
        + qkv_bias_full[:, None, :]
    )
    shaped = qkv_rows.reshape(3, shard_rows, model // HEAD, HEAD)
    qkv_tok = (
        jnp.stack(
            [
                rotate(shaped[0], cos_rows, sine_rows),
                rotate(shaped[1], cos_rows, sine_rows),
                shaped[2],
            ]
        )
        .astype(jnp.bfloat16)
        .reshape(3, shard_rows, model)
    )
    qkv_heads = lax.all_to_all(qkv_tok, "narrow", 2, 1, tiled=True)
    qkv_heads = qkv_heads.reshape(3, seq_count, length, heads_here, HEAD)
    query, key_rows, values = qkv_heads[0], qkv_heads[1], qkv_heads[2]
    attn_heads, totals = attend_forward(query, key_rows, values, block_rows)
    attn_low = attn_heads.reshape(group_rows, inner).astype(jnp.bfloat16)
    attn_rows = lax.all_to_all(attn_low, "narrow", 0, 1, tiled=True)
    out_full = lax.all_gather(out_weight, "narrow", axis=0, tiled=True)
    pre_attn = jnp.dot(attn_rows, out_full, preferred_element_type=jnp.float32) + out_bias
    normed_second, inverse_second = norm_stats(pre_attn)
    residual = layer_in + normed_second * norm_gains[1] + norm_biases[1]
    normed_third, inverse_third = norm_stats(residual)
    low_third = (normed_third * norm_gains[2] + norm_biases[2]).astype(jnp.bfloat16)
    up_full = gather_halves(up_weight, core, 0, 1)
    down_full = gather_halves(down_weight, core, 1, 0)
    hidden = jnp.dot(low_third, up_full, preferred_element_type=jnp.float32) + up_bias_full
    act_low = gelu_value(hidden).astype(jnp.bfloat16)
    pre_mlp = jnp.dot(act_low, down_full, preferred_element_type=jnp.float32) + down_bias
    normed_fourth, inverse_fourth = norm_stats(pre_mlp)
    final_sum = residual + normed_fourth * norm_gains[3] + norm_biases[3]
    layer_out = final_sum.astype(jnp.bfloat16)
    row_sequence = (first_row + jnp.arange(shard_rows, dtype=jnp.int32)) // length
    row_corpus = jnp.sum(
        jnp.where(
            row_sequence[:, None] == jnp.arange(seq_count, dtype=jnp.int32)[None, :],
            corpus_ids[None, :],
            0,
        ),
        axis=1,
    )
    row_weight = jnp.sum(
        jnp.where(
            row_corpus[:, None] == jnp.arange(corpus_weights.shape[0], dtype=jnp.int32)[None, :],
            corpus_weights[None, :],
            0.0,
        ),
        axis=1,
    )
    upstream = cotangent.astype(jnp.float32) * row_weight[:, None]
    mlp_grad = norm_back(normed_fourth, inverse_fourth, norm_gains[3], upstream).astype(
        jnp.bfloat16
    )
    down_wgrad_rows = lax.dot_general(
        act_low, mlp_grad, (((0,), (0,)), ((), ())), preferred_element_type=jnp.float32
    )
    act_grad = lax.dot_general(
        mlp_grad, down_full, (((1,), (1,)), ((), ())), preferred_element_type=jnp.float32
    )
    hidden_grad = (act_grad * gelu_slope(hidden)).astype(jnp.bfloat16)
    up_bgrad_rows = jnp.sum(hidden_grad.astype(jnp.float32), axis=0)
    up_wgrad_rows = lax.dot_general(
        low_third, hidden_grad, (((0,), (0,)), ((), ())), preferred_element_type=jnp.float32
    )
    third_grad = lax.dot_general(
        hidden_grad, up_full, (((1,), (1,)), ((), ())), preferred_element_type=jnp.float32
    )
    up_chip = chip_half(up_wgrad_rows, core, 0)
    down_chip = chip_half(down_wgrad_rows, core, 1)
    residual_grad = upstream + norm_back(normed_third, inverse_third, norm_gains[2], third_grad)
    branch_grad = norm_back(normed_second, inverse_second, norm_gains[1], residual_grad).astype(
        jnp.bfloat16
    )
    attn_grad_rows = lax.dot_general(
        branch_grad, out_full, (((1,), (1,)), ((), ())), preferred_element_type=jnp.float32
    ).astype(jnp.bfloat16)
    attn_grad_rows, up_chip, down_chip = lax.optimization_barrier(
        (attn_grad_rows, up_chip, down_chip)
    )
    up_slots = scatter_slots(up_chip, core, 0, 1)
    down_slots = scatter_slots(down_chip, core, 1, 0)
    attn_grad = lax.all_to_all(attn_grad_rows, "narrow", 1, 0, tiled=True)
    attn_grad = attn_grad.reshape(query.shape)
    query_grad, keys_grad, values_grad = attend_backward(
        query, key_rows, values, attn_grad, totals, block_rows
    )
    out_wgrad_rows = lax.dot_general(
        attn_rows, branch_grad, (((0,), (0,)), ((), ())), preferred_element_type=jnp.float32
    )
    out_slots = reduce_halves(out_wgrad_rows, core, 1, 0)
    qkv_grad = jnp.stack(
        [
            rotate_back(query_grad, cos_table, sine_table),
            rotate_back(keys_grad, cos_table, sine_table),
            values_grad,
        ]
    )
    qkv_grad = qkv_grad.reshape(3, group_rows, inner).astype(jnp.bfloat16)
    qkv_bgrad = jnp.sum(qkv_grad.astype(jnp.float32), axis=1)
    qkv_grad_rows = lax.all_to_all(qkv_grad, "narrow", 1, 2, tiled=True)
    qkv_wgrad_rows = jnp.einsum(
        "sd,tse->tde", low_first, qkv_grad_rows, preferred_element_type=jnp.float32
    )
    first_grad = jnp.einsum(
        "tse,tde->sd", qkv_grad_rows, qkv_full, preferred_element_type=jnp.float32
    )
    qkv_slots = reduce_halves(qkv_wgrad_rows, core, 1, 2)
    input_grad = (
        residual_grad + norm_back(normed_first, inverse_first, norm_gains[0], first_grad)
    ).astype(jnp.bfloat16)
    gain_local = jnp.stack(
        [
            jnp.sum(first_grad * normed_first, axis=0),
            jnp.sum(residual_grad * normed_second, axis=0),
            jnp.sum(third_grad * normed_third, axis=0),
            jnp.sum(upstream * normed_fourth, axis=0),
        ]
    )
    bias_local = jnp.stack(
        [
            jnp.sum(first_grad, axis=0),
            jnp.sum(residual_grad, axis=0),
            jnp.sum(third_grad, axis=0),
            jnp.sum(upstream, axis=0),
        ]
    )
    out_blocal = jnp.sum(branch_grad.astype(jnp.float32), axis=0)
    down_blocal = jnp.sum(mlp_grad.astype(jnp.float32), axis=0)
    weight_sums = (
        lax.psum(qkv_slots, "wide").astype(jnp.float32),
        None,
        lax.psum(out_slots, "wide").astype(jnp.float32),
        lax.psum(up_slots, "wide").astype(jnp.float32),
        None,
        lax.psum(down_slots, "wide").astype(jnp.float32),
    )
    narrow_index = lax.axis_index("narrow")
    bias_slots = jnp.where(
        jnp.arange(lax.axis_size("narrow"))[:, None, None] == narrow_index, qkv_bgrad[None], 0.0
    )
    small_sums = lax.psum(
        (gain_local, bias_local, out_blocal, down_blocal, up_bgrad_rows, bias_slots),
        ("wide", "narrow"),
    )
    qkv_bgrad = small_sums[5][narrow_index]
    units = up_bias.shape[0]
    up_bgrad = lax.dynamic_slice_in_dim(small_sums[4], lax.axis_index("narrow") * units, units)
    up_wgrad = merge_slots(weight_sums[3], 0)
    down_wgrad = merge_slots(weight_sums[5], 1)
    out_wgrad = merge_slots(weight_sums[2], 1)
    qkv_wgrad = merge_slots(weight_sums[0], 1)
    return (
        layer_out,
        input_grad,
        qkv_wgrad,
        qkv_bgrad,
        out_wgrad,
        small_sums[2],
        up_wgrad,
        up_bgrad,
        down_wgrad,
        small_sums[3],
        small_sums[0],
        small_sums[1],
    )


def solution(mesh):
    return jax.shard_map(
        shards,
        mesh=mesh,
        in_specs=(
            P(("wide", "narrow"), None),
            P(("wide", "narrow"), None),
            P("wide"),
            P(),
            P(None, None, "narrow"),
            P(None, "narrow"),
            P("narrow", None),
            P(),
            P(None, "narrow"),
            P("narrow"),
            P("narrow", None),
            P(),
            P(),
            P(),
        ),
        out_specs=(
            P(("wide", "narrow"), None),
            P(("wide", "narrow"), None),
            P(None, None, "narrow"),
            P(None, "narrow"),
            P("narrow", None),
            P(),
            P(None, "narrow"),
            P("narrow"),
            P("narrow", None),
            P(),
            P(),
            P(),
        ),
        check_vma=False,
    )
```

```python
import math

import jax
import jax.numpy as jnp
from jax import lax
from jax.sharding import PartitionSpec as P

HEAD = 64


epsilon = 1e-05
root_half = 0.7071067811865476
gauss_norm = 0.3989422804014327
masked_score = -1e30


def norm_stats(vec_in):
    center = vec_in - jnp.mean(vec_in, axis=-1, keepdims=True)
    inverse = lax.rsqrt(jnp.mean(center * center, axis=-1, keepdims=True) + epsilon)
    return (center * inverse, inverse)


def norm_back(normed, inverse, gain_row, upstream):
    scaled = upstream * gain_row
    return inverse * (
        scaled
        - jnp.mean(scaled, axis=-1, keepdims=True)
        - normed * jnp.mean(scaled * normed, axis=-1, keepdims=True)
    )


def rotary_tables(length, head_size):
    half_size = head_size // 2
    inv_freq = jnp.exp(jnp.arange(half_size, dtype=jnp.float32) * (-math.log(10000.0) / half_size))
    angles = jnp.arange(length, dtype=jnp.float32)[:, None] * inv_freq[None, :]
    return (jnp.cos(angles), jnp.sin(angles))


def rotate(vectors, cos_table, sine_table):
    half_size = vectors.shape[-1] // 2
    front_half = vectors[..., :half_size]
    back_half = vectors[..., half_size:]
    cos_grid = cos_table[:, None, :]
    sin_grid = sine_table[:, None, :]
    return jnp.concatenate(
        [
            front_half * cos_grid - back_half * sin_grid,
            front_half * sin_grid + back_half * cos_grid,
        ],
        axis=-1,
    )


def rotate_back(vectors, cos_table, sine_table):
    half_size = vectors.shape[-1] // 2
    front_half = vectors[..., :half_size]
    back_half = vectors[..., half_size:]
    cos_grid = cos_table[:, None, :]
    sin_grid = sine_table[:, None, :]
    return jnp.concatenate(
        [
            front_half * cos_grid + back_half * sin_grid,
            back_half * cos_grid - front_half * sin_grid,
        ],
        axis=-1,
    )


def gelu_value(hidden):
    return 0.5 * hidden * (1.0 + lax.erf(hidden * root_half))


def gelu_slope(hidden):
    return (
        0.5 * (1.0 + lax.erf(hidden * root_half))
        + hidden * jnp.exp(-0.5 * hidden * hidden) * gauss_norm
    )


def project_qkv(gathered, qkv_weight, qkv_bias, cos_table, sine_table, seq_count, length):
    heads_here = qkv_weight.shape[2] // HEAD
    qkv_pre = (
        jnp.einsum("sd,tde->tse", gathered, qkv_weight, preferred_element_type=jnp.float32)
        + qkv_bias[:, None, :]
    )
    shaped = qkv_pre.reshape(3, seq_count, length, heads_here, HEAD)
    query = rotate(shaped[0], cos_table, sine_table).astype(jnp.bfloat16)
    key_rows = rotate(shaped[1], cos_table, sine_table).astype(jnp.bfloat16)
    values = shaped[2].astype(jnp.bfloat16)
    return (query, key_rows, values)


def block_scores(query, key_rows, block_start, block_rows):
    key_stop = block_start + block_rows
    query_block = query[:, block_start:key_stop]
    key_block = key_rows[:, :key_stop]
    scores = jnp.einsum(
        "bqhd,bkhd->bhqk", query_block, key_block, preferred_element_type=jnp.float32
    ) * (1.0 / math.sqrt(HEAD))
    query_pos = block_start + jnp.arange(block_rows)
    key_pos = jnp.arange(key_stop)
    allowed = key_pos[None, :] <= query_pos[:, None]
    return (jnp.where(allowed[None, None], scores, masked_score), query_block, key_block)


def attend_forward(query, key_rows, values, block_rows):
    length = query.shape[1]
    outputs = []
    totals = []
    for block_start in range(0, length, block_rows):
        key_stop = block_start + block_rows
        scores, query_block, key_block = block_scores(query, key_rows, block_start, block_rows)
        row_max = jnp.max(scores, axis=-1, keepdims=True)
        log_total = row_max + jnp.log(jnp.sum(jnp.exp(scores - row_max), axis=-1, keepdims=True))
        probs_low = jnp.exp(scores - log_total).astype(jnp.bfloat16)
        outputs.append(
            jnp.einsum(
                "bhqk,bkhd->bqhd",
                probs_low,
                values[:, :key_stop],
                preferred_element_type=jnp.float32,
            )
        )
        totals.append(log_total)
    return (jnp.concatenate(outputs, axis=1), totals)


def attend_backward(query, key_rows, values, attn_grad, totals, block_rows):
    length = query.shape[1]
    score_scale = 1.0 / math.sqrt(HEAD)
    keys_grad = jnp.zeros(key_rows.shape, jnp.float32)
    values_grad = jnp.zeros(values.shape, jnp.float32)
    query_grads = []
    for block_number, block_start in enumerate(range(0, length, block_rows)):
        key_stop = block_start + block_rows
        scores, query_block, key_block = block_scores(query, key_rows, block_start, block_rows)
        value_block = values[:, :key_stop]
        grad_block = attn_grad[:, block_start:key_stop]
        probs_full = jnp.exp(scores - totals[block_number])
        probs_low = probs_full.astype(jnp.bfloat16)
        probs_grad = jnp.einsum(
            "bqhd,bkhd->bhqk", grad_block, value_block, preferred_element_type=jnp.float32
        )
        row_dot = jnp.sum(probs_full * probs_grad, axis=-1, keepdims=True)
        scores_grad = (probs_full * (probs_grad - row_dot)).astype(jnp.bfloat16)
        query_grads.append(
            jnp.einsum(
                "bhqk,bkhd->bqhd", scores_grad, key_block, preferred_element_type=jnp.float32
            )
            * score_scale
        )
        pad_rows = ((0, 0), (0, length - key_stop), (0, 0), (0, 0))
        keys_grad = keys_grad + jnp.pad(
            jnp.einsum(
                "bhqk,bqhd->bkhd", scores_grad, query_block, preferred_element_type=jnp.float32
            )
            * score_scale,
            pad_rows,
        )
        values_grad = values_grad + jnp.pad(
            jnp.einsum(
                "bhqk,bqhd->bkhd", probs_low, grad_block, preferred_element_type=jnp.float32
            ),
            pad_rows,
        )
    return (
        jnp.concatenate(query_grads, axis=1),
        keys_grad,
        values_grad,
    )


def swap_cores(block):
    count = lax.axis_size("wide")
    return lax.ppermute(block, "wide", [(index, index ^ 1) for index in range(count)])


def gather_mine(shard, core, split_axis, gather_axis):
    half = shard.shape[split_axis] // 2
    mine = lax.dynamic_slice_in_dim(shard, core * half, half, axis=split_axis)
    return lax.all_gather(mine, "narrow", axis=gather_axis, tiled=True)


def gather_halves(shard, core, split_axis, gather_axis):
    return join_halves(gather_mine(shard, core, split_axis, gather_axis), core, split_axis)


def join_halves(gathered, core, split_axis):
    partner = swap_cores(gathered)
    first = jnp.where(core == 0, gathered, partner)
    second = jnp.where(core == 0, partner, gathered)
    return jnp.concatenate([first, second], axis=split_axis)


def chip_half(rows, core, split_axis):
    half = rows.shape[split_axis] // 2
    mine = lax.dynamic_slice_in_dim(rows, core * half, half, axis=split_axis)
    other = lax.dynamic_slice_in_dim(rows, (1 - core) * half, half, axis=split_axis)
    chip_sum = mine + swap_cores(other.astype(jnp.bfloat16)).astype(jnp.float32)
    return chip_sum.astype(jnp.bfloat16)


def reduce_halves(rows, core, split_axis, scatter_axis):
    return scatter_slots(chip_half(rows, core, split_axis), core, split_axis, scatter_axis)


def scatter_slots(chip_sum, core, split_axis, scatter_axis):
    part = lax.psum_scatter(chip_sum, "narrow", scatter_dimension=scatter_axis, tiled=True)
    empty = jnp.zeros_like(part)
    return jnp.stack(
        [jnp.where(core == 0, part, empty), jnp.where(core == 0, empty, part)], axis=split_axis
    )


def reduce_column_halves(mats, core):
    count = lax.axis_size("narrow")
    pieces = []
    for rows in mats:
        half = rows.shape[1] // 2
        mine = lax.dynamic_slice_in_dim(rows, core * half, half, axis=1)
        other = lax.dynamic_slice_in_dim(rows, (1 - core) * half, half, axis=1)
        chip_sum = mine + swap_cores(other.astype(jnp.bfloat16)).astype(jnp.float32)
        pieces.append(chip_sum.astype(jnp.bfloat16).reshape(count, -1, half))
    joined = lax.psum_scatter(
        jnp.concatenate(pieces, axis=1), "narrow", scatter_dimension=0, tiled=True
    )[0]
    results = []
    start = 0
    for piece in pieces:
        part = joined[start : start + piece.shape[1]]
        start += piece.shape[1]
        empty = jnp.zeros_like(part)
        results.append(
            jnp.stack([jnp.where(core == 0, part, empty), jnp.where(core == 0, empty, part)], axis=1)
        )
    return results


def merge_slots(slots, split_axis):
    shape = list(slots.shape)
    shape[split_axis : split_axis + 2] = [shape[split_axis] * shape[split_axis + 1]]
    return slots.reshape(shape)


def shards(
    tokens,
    cotangent,
    corpus_ids,
    corpus_weights,
    qkv_weight,
    qkv_bias,
    out_weight,
    out_bias,
    up_weight,
    up_bias,
    down_weight,
    down_bias,
    norm_gains,
    norm_biases,
):
    shard_rows = tokens.shape[0]
    group_rows = shard_rows * lax.axis_size("narrow")
    seq_count = corpus_ids.shape[0]
    length = group_rows // seq_count
    block_rows = min(512, length)
    inner = qkv_weight.shape[2]
    first_row = lax.axis_index("narrow") * shard_rows
    cos_table, sine_table = rotary_tables(length, HEAD)
    layer_in = tokens.astype(jnp.float32)
    normed_first, inverse_first = norm_stats(layer_in)
    low_first = (normed_first * norm_gains[0] + norm_biases[0]).astype(jnp.bfloat16)
    core = lax.axis_index("wide") % 2
    model = layer_in.shape[1]
    heads_here = inner // HEAD
    bias_flat = jnp.concatenate([qkv_bias.reshape(-1), up_bias])
    bias_full = lax.all_gather(bias_flat, "narrow", axis=0)
    qkv_gathered = gather_mine(qkv_weight, core, 1, 2)
    qkv_gathered, up_weight, down_weight, bias_full = lax.optimization_barrier(
        (qkv_gathered, up_weight, down_weight, bias_full)
    )
    qkv_full = join_halves(qkv_gathered, core, 1)
    qkv_bias_full = jnp.swapaxes(bias_full[:, : 3 * inner].reshape(-1, 3, inner), 0, 1).reshape(
        3, model
    )
    up_bias_full = bias_full[:, 3 * inner :].reshape(-1)
    position_start = first_row % length
    cos_rows = lax.dynamic_slice_in_dim(cos_table, position_start, shard_rows, 0)
    sine_rows = lax.dynamic_slice_in_dim(sine_table, position_start, shard_rows, 0)
    qkv_rows = (
        jnp.einsum("sd,tde->tse", low_first, qkv_full, preferred_element_type=jnp.float32)
        + qkv_bias_full[:, None, :]
    )
    shaped = qkv_rows.reshape(3, shard_rows, model // HEAD, HEAD)
    qkv_tok = (
        jnp.stack(
            [
                rotate(shaped[0], cos_rows, sine_rows),
                rotate(shaped[1], cos_rows, sine_rows),
                shaped[2],
            ]
        )
        .astype(jnp.bfloat16)
        .reshape(3, shard_rows, model)
    )
    qkv_heads = lax.all_to_all(qkv_tok, "narrow", 2, 1, tiled=True)
    qkv_heads = qkv_heads.reshape(3, seq_count, length, heads_here, HEAD)
    query, key_rows, values = qkv_heads[0], qkv_heads[1], qkv_heads[2]
    attn_heads, totals = attend_forward(query, key_rows, values, block_rows)
    attn_low = attn_heads.reshape(group_rows, inner).astype(jnp.bfloat16)
    attn_rows = lax.all_to_all(attn_low, "narrow", 0, 1, tiled=True)
    out_full = lax.all_gather(out_weight, "narrow", axis=0, tiled=True)
    pre_attn = jnp.dot(attn_rows, out_full, preferred_element_type=jnp.float32) + out_bias
    normed_second, inverse_second = norm_stats(pre_attn)
    residual = layer_in + normed_second * norm_gains[1] + norm_biases[1]
    normed_third, inverse_third = norm_stats(residual)
    low_third = (normed_third * norm_gains[2] + norm_biases[2]).astype(jnp.bfloat16)
    up_full = gather_halves(up_weight, core, 0, 1)
    down_full = gather_halves(down_weight, core, 1, 0)
    hidden = jnp.dot(low_third, up_full, preferred_element_type=jnp.float32) + up_bias_full
    act_low = gelu_value(hidden).astype(jnp.bfloat16)
    pre_mlp = jnp.dot(act_low, down_full, preferred_element_type=jnp.float32) + down_bias
    normed_fourth, inverse_fourth = norm_stats(pre_mlp)
    final_sum = residual + normed_fourth * norm_gains[3] + norm_biases[3]
    layer_out = final_sum.astype(jnp.bfloat16)
    row_sequence = (first_row + jnp.arange(shard_rows, dtype=jnp.int32)) // length
    row_corpus = jnp.sum(
        jnp.where(
            row_sequence[:, None] == jnp.arange(seq_count, dtype=jnp.int32)[None, :],
            corpus_ids[None, :],
            0,
        ),
        axis=1,
    )
    row_weight = jnp.sum(
        jnp.where(
            row_corpus[:, None] == jnp.arange(corpus_weights.shape[0], dtype=jnp.int32)[None, :],
            corpus_weights[None, :],
            0.0,
        ),
        axis=1,
    )
    upstream = cotangent.astype(jnp.float32) * row_weight[:, None]
    mlp_grad = norm_back(normed_fourth, inverse_fourth, norm_gains[3], upstream).astype(
        jnp.bfloat16
    )
    down_wgrad_rows = lax.dot_general(
        act_low, mlp_grad, (((0,), (0,)), ((), ())), preferred_element_type=jnp.float32
    )
    act_grad = lax.dot_general(
        mlp_grad, down_full, (((1,), (1,)), ((), ())), preferred_element_type=jnp.float32
    )
    hidden_grad = (act_grad * gelu_slope(hidden)).astype(jnp.bfloat16)
    up_bgrad_rows = jnp.sum(hidden_grad.astype(jnp.float32), axis=0)
    up_wgrad_rows = lax.dot_general(
        low_third, hidden_grad, (((0,), (0,)), ((), ())), preferred_element_type=jnp.float32
    )
    third_grad = lax.dot_general(
        hidden_grad, up_full, (((1,), (1,)), ((), ())), preferred_element_type=jnp.float32
    )
    up_chip = chip_half(up_wgrad_rows, core, 0)
    down_chip = chip_half(down_wgrad_rows, core, 1)
    residual_grad = upstream + norm_back(normed_third, inverse_third, norm_gains[2], third_grad)
    branch_grad = norm_back(normed_second, inverse_second, norm_gains[1], residual_grad).astype(
        jnp.bfloat16
    )
    attn_grad_rows = lax.dot_general(
        branch_grad, out_full, (((1,), (1,)), ((), ())), preferred_element_type=jnp.float32
    ).astype(jnp.bfloat16)
    attn_grad_rows, up_chip, down_chip = lax.optimization_barrier(
        (attn_grad_rows, up_chip, down_chip)
    )
    up_slots = scatter_slots(up_chip, core, 0, 1)
    down_slots = scatter_slots(down_chip, core, 1, 0)
    attn_grad = lax.all_to_all(attn_grad_rows, "narrow", 1, 0, tiled=True)
    attn_grad = attn_grad.reshape(query.shape)
    query_grad, keys_grad, values_grad = attend_backward(
        query, key_rows, values, attn_grad, totals, block_rows
    )
    out_wgrad_rows = lax.dot_general(
        attn_rows, branch_grad, (((0,), (0,)), ((), ())), preferred_element_type=jnp.float32
    )
    out_slots = reduce_halves(out_wgrad_rows, core, 1, 0)
    qkv_grad = jnp.stack(
        [
            rotate_back(query_grad, cos_table, sine_table),
            rotate_back(keys_grad, cos_table, sine_table),
            values_grad,
        ]
    )
    qkv_grad = qkv_grad.reshape(3, group_rows, inner).astype(jnp.bfloat16)
    qkv_bgrad = jnp.sum(qkv_grad.astype(jnp.float32), axis=1)
    qkv_grad_rows = lax.all_to_all(qkv_grad, "narrow", 1, 2, tiled=True)
    qkv_wgrad_rows = jnp.einsum(
        "sd,tse->tde", low_first, qkv_grad_rows, preferred_element_type=jnp.float32
    )
    first_grad = jnp.einsum(
        "tse,tde->sd", qkv_grad_rows, qkv_full, preferred_element_type=jnp.float32
    )
    qkv_slots = reduce_halves(qkv_wgrad_rows, core, 1, 2)
    input_grad = (
        residual_grad + norm_back(normed_first, inverse_first, norm_gains[0], first_grad)
    ).astype(jnp.bfloat16)
    gain_local = jnp.stack(
        [
            jnp.sum(first_grad * normed_first, axis=0),
            jnp.sum(residual_grad * normed_second, axis=0),
            jnp.sum(third_grad * normed_third, axis=0),
            jnp.sum(upstream * normed_fourth, axis=0),
        ]
    )
    bias_local = jnp.stack(
        [
            jnp.sum(first_grad, axis=0),
            jnp.sum(residual_grad, axis=0),
            jnp.sum(third_grad, axis=0),
            jnp.sum(upstream, axis=0),
        ]
    )
    out_blocal = jnp.sum(branch_grad.astype(jnp.float32), axis=0)
    down_blocal = jnp.sum(mlp_grad.astype(jnp.float32), axis=0)
    weight_sums = (
        lax.psum(qkv_slots, "wide").astype(jnp.float32),
        lax.psum(qkv_bgrad.astype(jnp.bfloat16), "wide").astype(jnp.float32),
        lax.psum(out_slots, "wide").astype(jnp.float32),
        lax.psum(up_slots, "wide").astype(jnp.float32),
        None,
        lax.psum(down_slots, "wide").astype(jnp.float32),
    )
    small_sums = lax.psum(
        (gain_local, bias_local, out_blocal, down_blocal, up_bgrad_rows), ("wide", "narrow")
    )
    units = up_bias.shape[0]
    up_bgrad = lax.dynamic_slice_in_dim(small_sums[4], lax.axis_index("narrow") * units, units)
    up_wgrad = merge_slots(weight_sums[3], 0)
    down_wgrad = merge_slots(weight_sums[5], 1)
    out_wgrad = merge_slots(weight_sums[2], 1)
    qkv_wgrad = merge_slots(weight_sums[0], 1)
    return (
        layer_out,
        input_grad,
        qkv_wgrad,
        weight_sums[1],
        out_wgrad,
        small_sums[2],
        up_wgrad,
        up_bgrad,
        down_wgrad,
        small_sums[3],
        small_sums[0],
        small_sums[1],
    )


def solution(mesh):
    return jax.shard_map(
        shards,
        mesh=mesh,
        in_specs=(
            P(("wide", "narrow"), None),
            P(("wide", "narrow"), None),
            P("wide"),
            P(),
            P(None, None, "narrow"),
            P(None, "narrow"),
            P("narrow", None),
            P(),
            P(None, "narrow"),
            P("narrow"),
            P("narrow", None),
            P(),
            P(),
            P(),
        ),
        out_specs=(
            P(("wide", "narrow"), None),
            P(("wide", "narrow"), None),
            P(None, None, "narrow"),
            P(None, "narrow"),
            P("narrow", None),
            P(),
            P(None, "narrow"),
            P("narrow"),
            P("narrow", None),
            P(),
            P(),
            P(),
        ),
        check_vma=False,
    )
```

```python
import math

import jax
import jax.numpy as jnp
from jax import lax
from jax.sharding import PartitionSpec as P

HEAD = 64


epsilon = 1e-05
root_half = 0.7071067811865476
gauss_norm = 0.3989422804014327
masked_score = -1e30


def norm_stats(vec_in):
    center = vec_in - jnp.mean(vec_in, axis=-1, keepdims=True)
    inverse = lax.rsqrt(jnp.mean(center * center, axis=-1, keepdims=True) + epsilon)
    return (center * inverse, inverse)


def norm_back(normed, inverse, gain_row, upstream):
    scaled = upstream * gain_row
    return inverse * (
        scaled
        - jnp.mean(scaled, axis=-1, keepdims=True)
        - normed * jnp.mean(scaled * normed, axis=-1, keepdims=True)
    )


def rotary_tables(length, head_size):
    half_size = head_size // 2
    inv_freq = jnp.exp(jnp.arange(half_size, dtype=jnp.float32) * (-math.log(10000.0) / half_size))
    angles = jnp.arange(length, dtype=jnp.float32)[:, None] * inv_freq[None, :]
    return (jnp.cos(angles), jnp.sin(angles))


def rotate(vectors, cos_table, sine_table):
    half_size = vectors.shape[-1] // 2
    front_half = vectors[..., :half_size]
    back_half = vectors[..., half_size:]
    cos_grid = cos_table[:, None, :]
    sin_grid = sine_table[:, None, :]
    return jnp.concatenate(
        [
            front_half * cos_grid - back_half * sin_grid,
            front_half * sin_grid + back_half * cos_grid,
        ],
        axis=-1,
    )


def rotate_back(vectors, cos_table, sine_table):
    half_size = vectors.shape[-1] // 2
    front_half = vectors[..., :half_size]
    back_half = vectors[..., half_size:]
    cos_grid = cos_table[:, None, :]
    sin_grid = sine_table[:, None, :]
    return jnp.concatenate(
        [
            front_half * cos_grid + back_half * sin_grid,
            back_half * cos_grid - front_half * sin_grid,
        ],
        axis=-1,
    )


def gelu_value(hidden):
    return 0.5 * hidden * (1.0 + lax.erf(hidden * root_half))


def gelu_slope(hidden):
    return (
        0.5 * (1.0 + lax.erf(hidden * root_half))
        + hidden * jnp.exp(-0.5 * hidden * hidden) * gauss_norm
    )


def project_qkv(gathered, qkv_weight, qkv_bias, cos_table, sine_table, seq_count, length):
    heads_here = qkv_weight.shape[2] // HEAD
    qkv_pre = (
        jnp.einsum("sd,tde->tse", gathered, qkv_weight, preferred_element_type=jnp.float32)
        + qkv_bias[:, None, :]
    )
    shaped = qkv_pre.reshape(3, seq_count, length, heads_here, HEAD)
    query = rotate(shaped[0], cos_table, sine_table).astype(jnp.bfloat16)
    key_rows = rotate(shaped[1], cos_table, sine_table).astype(jnp.bfloat16)
    values = shaped[2].astype(jnp.bfloat16)
    return (query, key_rows, values)


def block_scores(query, key_rows, block_start, block_rows):
    key_stop = block_start + block_rows
    query_block = query[:, block_start:key_stop]
    key_block = key_rows[:, :key_stop]
    scores = jnp.einsum(
        "bqhd,bkhd->bhqk", query_block, key_block, preferred_element_type=jnp.float32
    ) * (1.0 / math.sqrt(HEAD))
    query_pos = block_start + jnp.arange(block_rows)
    key_pos = jnp.arange(key_stop)
    allowed = key_pos[None, :] <= query_pos[:, None]
    return (jnp.where(allowed[None, None], scores, masked_score), query_block, key_block)


def attend_forward(query, key_rows, values, block_rows):
    length = query.shape[1]
    outputs = []
    totals = []
    for block_start in range(0, length, block_rows):
        key_stop = block_start + block_rows
        scores, query_block, key_block = block_scores(query, key_rows, block_start, block_rows)
        row_max = jnp.max(scores, axis=-1, keepdims=True)
        log_total = row_max + jnp.log(jnp.sum(jnp.exp(scores - row_max), axis=-1, keepdims=True))
        probs_low = jnp.exp(scores - log_total).astype(jnp.bfloat16)
        outputs.append(
            jnp.einsum(
                "bhqk,bkhd->bqhd",
                probs_low,
                values[:, :key_stop],
                preferred_element_type=jnp.float32,
            )
        )
        totals.append(log_total)
    return (jnp.concatenate(outputs, axis=1), totals)


def attend_backward(query, key_rows, values, attn_grad, totals, block_rows):
    length = query.shape[1]
    score_scale = 1.0 / math.sqrt(HEAD)
    keys_grad = jnp.zeros(key_rows.shape, jnp.float32)
    values_grad = jnp.zeros(values.shape, jnp.float32)
    query_grads = []
    for block_number, block_start in enumerate(range(0, length, block_rows)):
        key_stop = block_start + block_rows
        scores, query_block, key_block = block_scores(query, key_rows, block_start, block_rows)
        value_block = values[:, :key_stop]
        grad_block = attn_grad[:, block_start:key_stop]
        probs_full = jnp.exp(scores - totals[block_number])
        probs_low = probs_full.astype(jnp.bfloat16)
        probs_grad = jnp.einsum(
            "bqhd,bkhd->bhqk", grad_block, value_block, preferred_element_type=jnp.float32
        )
        row_dot = jnp.sum(probs_full * probs_grad, axis=-1, keepdims=True)
        scores_grad = (probs_full * (probs_grad - row_dot)).astype(jnp.bfloat16)
        query_grads.append(
            jnp.einsum(
                "bhqk,bkhd->bqhd", scores_grad, key_block, preferred_element_type=jnp.float32
            )
            * score_scale
        )
        pad_rows = ((0, 0), (0, length - key_stop), (0, 0), (0, 0))
        keys_grad = keys_grad + jnp.pad(
            jnp.einsum(
                "bhqk,bqhd->bkhd", scores_grad, query_block, preferred_element_type=jnp.float32
            )
            * score_scale,
            pad_rows,
        )
        values_grad = values_grad + jnp.pad(
            jnp.einsum(
                "bhqk,bqhd->bkhd", probs_low, grad_block, preferred_element_type=jnp.float32
            ),
            pad_rows,
        )
    return (
        jnp.concatenate(query_grads, axis=1),
        keys_grad,
        values_grad,
    )


def swap_cores(block):
    count = lax.axis_size("wide")
    return lax.ppermute(block, "wide", [(index, index ^ 1) for index in range(count)])


def gather_mine(shard, core, split_axis, gather_axis):
    half = shard.shape[split_axis] // 2
    mine = lax.dynamic_slice_in_dim(shard, core * half, half, axis=split_axis)
    return lax.all_gather(mine, "narrow", axis=gather_axis, tiled=True)


def gather_halves(shard, core, split_axis, gather_axis):
    return join_halves(gather_mine(shard, core, split_axis, gather_axis), core, split_axis)


def join_halves(gathered, core, split_axis):
    partner = swap_cores(gathered)
    first = jnp.where(core == 0, gathered, partner)
    second = jnp.where(core == 0, partner, gathered)
    return jnp.concatenate([first, second], axis=split_axis)


def chip_half(rows, core, split_axis):
    half = rows.shape[split_axis] // 2
    mine = lax.dynamic_slice_in_dim(rows, core * half, half, axis=split_axis)
    other = lax.dynamic_slice_in_dim(rows, (1 - core) * half, half, axis=split_axis)
    chip_sum = mine + swap_cores(other.astype(jnp.bfloat16)).astype(jnp.float32)
    return chip_sum.astype(jnp.bfloat16)


def reduce_halves(rows, core, split_axis, scatter_axis):
    return scatter_slots(chip_half(rows, core, split_axis), core, split_axis, scatter_axis)


def scatter_slots(chip_sum, core, split_axis, scatter_axis):
    part = lax.psum_scatter(chip_sum, "narrow", scatter_dimension=scatter_axis, tiled=True)
    empty = jnp.zeros_like(part)
    return jnp.stack(
        [jnp.where(core == 0, part, empty), jnp.where(core == 0, empty, part)], axis=split_axis
    )


def reduce_column_halves(mats, core):
    count = lax.axis_size("narrow")
    pieces = []
    for rows in mats:
        half = rows.shape[1] // 2
        mine = lax.dynamic_slice_in_dim(rows, core * half, half, axis=1)
        other = lax.dynamic_slice_in_dim(rows, (1 - core) * half, half, axis=1)
        chip_sum = mine + swap_cores(other.astype(jnp.bfloat16)).astype(jnp.float32)
        pieces.append(chip_sum.astype(jnp.bfloat16).reshape(count, -1, half))
    joined = lax.psum_scatter(
        jnp.concatenate(pieces, axis=1), "narrow", scatter_dimension=0, tiled=True
    )[0]
    results = []
    start = 0
    for piece in pieces:
        part = joined[start : start + piece.shape[1]]
        start += piece.shape[1]
        empty = jnp.zeros_like(part)
        results.append(
            jnp.stack([jnp.where(core == 0, part, empty), jnp.where(core == 0, empty, part)], axis=1)
        )
    return results


def merge_slots(slots, split_axis):
    shape = list(slots.shape)
    shape[split_axis : split_axis + 2] = [shape[split_axis] * shape[split_axis + 1]]
    return slots.reshape(shape)


def shards(
    tokens,
    cotangent,
    corpus_ids,
    corpus_weights,
    qkv_weight,
    qkv_bias,
    out_weight,
    out_bias,
    up_weight,
    up_bias,
    down_weight,
    down_bias,
    norm_gains,
    norm_biases,
):
    shard_rows = tokens.shape[0]
    group_rows = shard_rows * lax.axis_size("narrow")
    seq_count = corpus_ids.shape[0]
    length = group_rows // seq_count
    block_rows = min(512, length)
    inner = qkv_weight.shape[2]
    first_row = lax.axis_index("narrow") * shard_rows
    cos_table, sine_table = rotary_tables(length, HEAD)
    layer_in = tokens.astype(jnp.float32)
    normed_first, inverse_first = norm_stats(layer_in)
    low_first = (normed_first * norm_gains[0] + norm_biases[0]).astype(jnp.bfloat16)
    core = lax.axis_index("wide") % 2
    model = layer_in.shape[1]
    heads_here = inner // HEAD
    bias_flat = jnp.concatenate([qkv_bias.reshape(-1), up_bias])
    bias_full = lax.all_gather(bias_flat, "narrow", axis=0)
    qkv_gathered = gather_mine(qkv_weight, core, 1, 2)
    out_gathered = gather_mine(out_weight, core, 1, 0)
    qkv_gathered, out_gathered, up_weight, down_weight, bias_full = lax.optimization_barrier(
        (qkv_gathered, out_gathered, up_weight, down_weight, bias_full)
    )
    qkv_full = join_halves(qkv_gathered, core, 1)
    qkv_bias_full = jnp.swapaxes(bias_full[:, : 3 * inner].reshape(-1, 3, inner), 0, 1).reshape(
        3, model
    )
    up_bias_full = bias_full[:, 3 * inner :].reshape(-1)
    position_start = first_row % length
    cos_rows = lax.dynamic_slice_in_dim(cos_table, position_start, shard_rows, 0)
    sine_rows = lax.dynamic_slice_in_dim(sine_table, position_start, shard_rows, 0)
    qkv_rows = (
        jnp.einsum("sd,tde->tse", low_first, qkv_full, preferred_element_type=jnp.float32)
        + qkv_bias_full[:, None, :]
    )
    shaped = qkv_rows.reshape(3, shard_rows, model // HEAD, HEAD)
    qkv_tok = (
        jnp.stack(
            [
                rotate(shaped[0], cos_rows, sine_rows),
                rotate(shaped[1], cos_rows, sine_rows),
                shaped[2],
            ]
        )
        .astype(jnp.bfloat16)
        .reshape(3, shard_rows, model)
    )
    qkv_heads = lax.all_to_all(qkv_tok, "narrow", 2, 1, tiled=True)
    qkv_heads, up_weight, down_weight = lax.optimization_barrier((qkv_heads, up_weight, down_weight))
    qkv_heads = qkv_heads.reshape(3, seq_count, length, heads_here, HEAD)
    query, key_rows, values = qkv_heads[0], qkv_heads[1], qkv_heads[2]
    attn_heads, totals = attend_forward(query, key_rows, values, block_rows)
    attn_low = attn_heads.reshape(group_rows, inner).astype(jnp.bfloat16)
    attn_rows = lax.all_to_all(attn_low, "narrow", 0, 1, tiled=True)
    out_full = join_halves(out_gathered, core, 1)
    pre_attn = jnp.dot(attn_rows, out_full, preferred_element_type=jnp.float32) + out_bias
    normed_second, inverse_second = norm_stats(pre_attn)
    residual = layer_in + normed_second * norm_gains[1] + norm_biases[1]
    normed_third, inverse_third = norm_stats(residual)
    low_third = (normed_third * norm_gains[2] + norm_biases[2]).astype(jnp.bfloat16)
    up_full = gather_halves(up_weight, core, 0, 1)
    down_full = gather_halves(down_weight, core, 1, 0)
    hidden = jnp.dot(low_third, up_full, preferred_element_type=jnp.float32) + up_bias_full
    act_low = gelu_value(hidden).astype(jnp.bfloat16)
    pre_mlp = jnp.dot(act_low, down_full, preferred_element_type=jnp.float32) + down_bias
    normed_fourth, inverse_fourth = norm_stats(pre_mlp)
    final_sum = residual + normed_fourth * norm_gains[3] + norm_biases[3]
    layer_out = final_sum.astype(jnp.bfloat16)
    row_sequence = (first_row + jnp.arange(shard_rows, dtype=jnp.int32)) // length
    row_corpus = jnp.sum(
        jnp.where(
            row_sequence[:, None] == jnp.arange(seq_count, dtype=jnp.int32)[None, :],
            corpus_ids[None, :],
            0,
        ),
        axis=1,
    )
    row_weight = jnp.sum(
        jnp.where(
            row_corpus[:, None] == jnp.arange(corpus_weights.shape[0], dtype=jnp.int32)[None, :],
            corpus_weights[None, :],
            0.0,
        ),
        axis=1,
    )
    upstream = cotangent.astype(jnp.float32) * row_weight[:, None]
    mlp_grad = norm_back(normed_fourth, inverse_fourth, norm_gains[3], upstream).astype(
        jnp.bfloat16
    )
    down_wgrad_rows = lax.dot_general(
        act_low, mlp_grad, (((0,), (0,)), ((), ())), preferred_element_type=jnp.float32
    )
    act_grad = lax.dot_general(
        mlp_grad, down_full, (((1,), (1,)), ((), ())), preferred_element_type=jnp.float32
    )
    hidden_grad = (act_grad * gelu_slope(hidden)).astype(jnp.bfloat16)
    up_bgrad_rows = jnp.sum(hidden_grad.astype(jnp.float32), axis=0)
    up_wgrad_rows = lax.dot_general(
        low_third, hidden_grad, (((0,), (0,)), ((), ())), preferred_element_type=jnp.float32
    )
    third_grad = lax.dot_general(
        hidden_grad, up_full, (((1,), (1,)), ((), ())), preferred_element_type=jnp.float32
    )
    up_chip = chip_half(up_wgrad_rows, core, 0)
    down_chip = chip_half(down_wgrad_rows, core, 1)
    residual_grad = upstream + norm_back(normed_third, inverse_third, norm_gains[2], third_grad)
    branch_grad = norm_back(normed_second, inverse_second, norm_gains[1], residual_grad).astype(
        jnp.bfloat16
    )
    attn_grad_rows = lax.dot_general(
        branch_grad, out_full, (((1,), (1,)), ((), ())), preferred_element_type=jnp.float32
    ).astype(jnp.bfloat16)
    attn_grad_rows, up_chip, down_chip = lax.optimization_barrier(
        (attn_grad_rows, up_chip, down_chip)
    )
    up_slots = scatter_slots(up_chip, core, 0, 1)
    down_slots = scatter_slots(down_chip, core, 1, 0)
    attn_grad = lax.all_to_all(attn_grad_rows, "narrow", 1, 0, tiled=True)
    attn_grad = attn_grad.reshape(query.shape)
    query_grad, keys_grad, values_grad = attend_backward(
        query, key_rows, values, attn_grad, totals, block_rows
    )
    out_wgrad_rows = lax.dot_general(
        attn_rows, branch_grad, (((0,), (0,)), ((), ())), preferred_element_type=jnp.float32
    )
    out_chip = chip_half(out_wgrad_rows, core, 1)
    qkv_grad = jnp.stack(
        [
            rotate_back(query_grad, cos_table, sine_table),
            rotate_back(keys_grad, cos_table, sine_table),
            values_grad,
        ]
    )
    qkv_grad = qkv_grad.reshape(3, group_rows, inner).astype(jnp.bfloat16)
    qkv_bgrad = jnp.sum(qkv_grad.astype(jnp.float32), axis=1)
    qkv_grad_rows = lax.all_to_all(qkv_grad, "narrow", 1, 2, tiled=True)
    qkv_grad_rows, out_chip = lax.optimization_barrier((qkv_grad_rows, out_chip))
    out_slots = scatter_slots(out_chip, core, 1, 0)
    qkv_wgrad_rows = jnp.einsum(
        "sd,tse->tde", low_first, qkv_grad_rows, preferred_element_type=jnp.float32
    )
    first_grad = jnp.einsum(
        "tse,tde->sd", qkv_grad_rows, qkv_full, preferred_element_type=jnp.float32
    )
    qkv_slots = reduce_halves(qkv_wgrad_rows, core, 1, 2)
    input_grad = (
        residual_grad + norm_back(normed_first, inverse_first, norm_gains[0], first_grad)
    ).astype(jnp.bfloat16)
    gain_local = jnp.stack(
        [
            jnp.sum(first_grad * normed_first, axis=0),
            jnp.sum(residual_grad * normed_second, axis=0),
            jnp.sum(third_grad * normed_third, axis=0),
            jnp.sum(upstream * normed_fourth, axis=0),
        ]
    )
    bias_local = jnp.stack(
        [
            jnp.sum(first_grad, axis=0),
            jnp.sum(residual_grad, axis=0),
            jnp.sum(third_grad, axis=0),
            jnp.sum(upstream, axis=0),
        ]
    )
    out_blocal = jnp.sum(branch_grad.astype(jnp.float32), axis=0)
    down_blocal = jnp.sum(mlp_grad.astype(jnp.float32), axis=0)
    weight_sums = (
        lax.psum(qkv_slots, "wide").astype(jnp.float32),
        lax.psum(qkv_bgrad.astype(jnp.bfloat16), "wide").astype(jnp.float32),
        lax.psum(out_slots, "wide").astype(jnp.float32),
        lax.psum(up_slots, "wide").astype(jnp.float32),
        None,
        lax.psum(down_slots, "wide").astype(jnp.float32),
    )
    small_sums = lax.psum(
        (gain_local, bias_local, out_blocal, down_blocal, up_bgrad_rows), ("wide", "narrow")
    )
    units = up_bias.shape[0]
    up_bgrad = lax.dynamic_slice_in_dim(small_sums[4], lax.axis_index("narrow") * units, units)
    up_wgrad = merge_slots(weight_sums[3], 0)
    down_wgrad = merge_slots(weight_sums[5], 1)
    out_wgrad = merge_slots(weight_sums[2], 1)
    qkv_wgrad = merge_slots(weight_sums[0], 1)
    return (
        layer_out,
        input_grad,
        qkv_wgrad,
        weight_sums[1],
        out_wgrad,
        small_sums[2],
        up_wgrad,
        up_bgrad,
        down_wgrad,
        small_sums[3],
        small_sums[0],
        small_sums[1],
    )


def solution(mesh):
    return jax.shard_map(
        shards,
        mesh=mesh,
        in_specs=(
            P(("wide", "narrow"), None),
            P(("wide", "narrow"), None),
            P("wide"),
            P(),
            P(None, None, "narrow"),
            P(None, "narrow"),
            P("narrow", None),
            P(),
            P(None, "narrow"),
            P("narrow"),
            P("narrow", None),
            P(),
            P(),
            P(),
        ),
        out_specs=(
            P(("wide", "narrow"), None),
            P(("wide", "narrow"), None),
            P(None, None, "narrow"),
            P(None, "narrow"),
            P("narrow", None),
            P(),
            P(None, "narrow"),
            P("narrow"),
            P("narrow", None),
            P(),
            P(),
            P(),
        ),
        check_vma=False,
    )
```

```python
import math

import jax
import jax.numpy as jnp
from jax import lax
from jax.sharding import PartitionSpec as P

HEAD = 64


epsilon = 1e-05
root_half = 0.7071067811865476
gauss_norm = 0.3989422804014327
masked_score = -1e30


def norm_stats(vec_in):
    center = vec_in - jnp.mean(vec_in, axis=-1, keepdims=True)
    inverse = lax.rsqrt(jnp.mean(center * center, axis=-1, keepdims=True) + epsilon)
    return (center * inverse, inverse)


def norm_back(normed, inverse, gain_row, upstream):
    scaled = upstream * gain_row
    return inverse * (
        scaled
        - jnp.mean(scaled, axis=-1, keepdims=True)
        - normed * jnp.mean(scaled * normed, axis=-1, keepdims=True)
    )


def rotary_tables(length, head_size):
    half_size = head_size // 2
    inv_freq = jnp.exp(jnp.arange(half_size, dtype=jnp.float32) * (-math.log(10000.0) / half_size))
    angles = jnp.arange(length, dtype=jnp.float32)[:, None] * inv_freq[None, :]
    return (jnp.cos(angles), jnp.sin(angles))


def rotate(vectors, cos_table, sine_table):
    half_size = vectors.shape[-1] // 2
    front_half = vectors[..., :half_size]
    back_half = vectors[..., half_size:]
    cos_grid = cos_table[:, None, :]
    sin_grid = sine_table[:, None, :]
    return jnp.concatenate(
        [
            front_half * cos_grid - back_half * sin_grid,
            front_half * sin_grid + back_half * cos_grid,
        ],
        axis=-1,
    )


def rotate_back(vectors, cos_table, sine_table):
    half_size = vectors.shape[-1] // 2
    front_half = vectors[..., :half_size]
    back_half = vectors[..., half_size:]
    cos_grid = cos_table[:, None, :]
    sin_grid = sine_table[:, None, :]
    return jnp.concatenate(
        [
            front_half * cos_grid + back_half * sin_grid,
            back_half * cos_grid - front_half * sin_grid,
        ],
        axis=-1,
    )


def gelu_value(hidden):
    return 0.5 * hidden * (1.0 + lax.erf(hidden * root_half))


def gelu_slope(hidden):
    return (
        0.5 * (1.0 + lax.erf(hidden * root_half))
        + hidden * jnp.exp(-0.5 * hidden * hidden) * gauss_norm
    )


def project_qkv(gathered, qkv_weight, qkv_bias, cos_table, sine_table, seq_count, length):
    heads_here = qkv_weight.shape[2] // HEAD
    qkv_pre = (
        jnp.einsum("sd,tde->tse", gathered, qkv_weight, preferred_element_type=jnp.float32)
        + qkv_bias[:, None, :]
    )
    shaped = qkv_pre.reshape(3, seq_count, length, heads_here, HEAD)
    query = rotate(shaped[0], cos_table, sine_table).astype(jnp.bfloat16)
    key_rows = rotate(shaped[1], cos_table, sine_table).astype(jnp.bfloat16)
    values = shaped[2].astype(jnp.bfloat16)
    return (query, key_rows, values)


def block_scores(query, key_rows, block_start, block_rows):
    key_stop = block_start + block_rows
    query_block = query[:, block_start:key_stop]
    key_block = key_rows[:, :key_stop]
    scores = jnp.einsum(
        "bqhd,bkhd->bhqk", query_block, key_block, preferred_element_type=jnp.float32
    ) * (1.0 / math.sqrt(HEAD))
    query_pos = block_start + jnp.arange(block_rows)
    key_pos = jnp.arange(key_stop)
    allowed = key_pos[None, :] <= query_pos[:, None]
    return (jnp.where(allowed[None, None], scores, masked_score), query_block, key_block)


def attend_forward(query, key_rows, values, block_rows):
    length = query.shape[1]
    outputs = []
    totals = []
    for block_start in range(0, length, block_rows):
        key_stop = block_start + block_rows
        scores, query_block, key_block = block_scores(query, key_rows, block_start, block_rows)
        row_max = jnp.max(scores, axis=-1, keepdims=True)
        log_total = row_max + jnp.log(jnp.sum(jnp.exp(scores - row_max), axis=-1, keepdims=True))
        probs_low = jnp.exp(scores - log_total).astype(jnp.bfloat16)
        outputs.append(
            jnp.einsum(
                "bhqk,bkhd->bqhd",
                probs_low,
                values[:, :key_stop],
                preferred_element_type=jnp.float32,
            )
        )
        totals.append(log_total)
    return (jnp.concatenate(outputs, axis=1), totals)


def attend_backward(query, key_rows, values, attn_grad, totals, block_rows, sidecar, finish):
    length = query.shape[1]
    score_scale = 1.0 / math.sqrt(HEAD)
    keys_grad = jnp.zeros(key_rows.shape, jnp.float32)
    values_grad = jnp.zeros(values.shape, jnp.float32)
    query_grads = []
    for block_number, block_start in enumerate(range(0, length, block_rows)):
        key_stop = block_start + block_rows
        scores, query_block, key_block = block_scores(query, key_rows, block_start, block_rows)
        value_block = values[:, :key_stop]
        grad_block = attn_grad[:, block_start:key_stop]
        probs_full = jnp.exp(scores - totals[block_number])
        probs_low = probs_full.astype(jnp.bfloat16)
        probs_grad = jnp.einsum(
            "bqhd,bkhd->bhqk", grad_block, value_block, preferred_element_type=jnp.float32
        )
        row_dot = jnp.sum(probs_full * probs_grad, axis=-1, keepdims=True)
        scores_grad = (probs_full * (probs_grad - row_dot)).astype(jnp.bfloat16)
        query_grads.append(
            jnp.einsum(
                "bhqk,bkhd->bqhd", scores_grad, key_block, preferred_element_type=jnp.float32
            )
            * score_scale
        )
        pad_rows = ((0, 0), (0, length - key_stop), (0, 0), (0, 0))
        keys_grad = keys_grad + jnp.pad(
            jnp.einsum(
                "bhqk,bqhd->bkhd", scores_grad, query_block, preferred_element_type=jnp.float32
            )
            * score_scale,
            pad_rows,
        )
        values_grad = values_grad + jnp.pad(
            jnp.einsum(
                "bhqk,bqhd->bkhd", probs_low, grad_block, preferred_element_type=jnp.float32
            ),
            pad_rows,
        )
        if block_number == min(2, length // block_rows - 1):
            keys_grad, values_grad, sidecar = lax.optimization_barrier(
                (keys_grad, values_grad, sidecar)
            )
            sidecar = finish(sidecar)
    keys_grad, values_grad, sidecar = lax.optimization_barrier((keys_grad, values_grad, sidecar))
    return (
        jnp.concatenate(query_grads, axis=1),
        keys_grad,
        values_grad,
        sidecar,
    )


def swap(block, bit):
    count = lax.axis_size("wide")
    return lax.ppermute(block, "wide", [(index, index ^ bit) for index in range(count)])


def order_pair(low_bit, mine, theirs, axis):
    first = jnp.where(low_bit == 0, mine, theirs)
    second = jnp.where(low_bit == 0, theirs, mine)
    return jnp.concatenate([first, second], axis=axis)


def gather_quarter(shard, core, pair, split_axis, gather_axis):
    quarter = shard.shape[split_axis] // 4
    mine = lax.dynamic_slice_in_dim(shard, (2 * core + pair) * quarter, quarter, axis=split_axis)
    return lax.all_gather(mine, "narrow", axis=gather_axis, tiled=True)


def join_quarters(gathered, core, pair, split_axis):
    half = order_pair(pair, gathered, swap(gathered, 2), split_axis)
    return order_pair(core, half, swap(half, 1), split_axis)


def gather_halves(shard, core, split_axis, gather_axis):
    half = shard.shape[split_axis] // 2
    mine = lax.dynamic_slice_in_dim(shard, core * half, half, axis=split_axis)
    gathered = lax.all_gather(mine, "narrow", axis=gather_axis, tiled=True)
    return gathered


def join_halves(gathered, core, split_axis):
    return order_pair(core, gathered, swap(gathered, 1), split_axis)


def core_step(rows, core, split_axis):
    half = rows.shape[split_axis] // 2
    mine = lax.dynamic_slice_in_dim(rows, core * half, half, axis=split_axis)
    other = lax.dynamic_slice_in_dim(rows, (1 - core) * half, half, axis=split_axis)
    return mine + swap(other.astype(jnp.bfloat16), 1).astype(jnp.float32)


def pair_step(chip_sum, pair, split_axis):
    quarter = chip_sum.shape[split_axis] // 2
    keep = lax.dynamic_slice_in_dim(chip_sum, pair * quarter, quarter, axis=split_axis)
    give = lax.dynamic_slice_in_dim(chip_sum, (1 - pair) * quarter, quarter, axis=split_axis)
    return (keep + swap(give.astype(jnp.bfloat16), 2).astype(jnp.float32)).astype(jnp.bfloat16)


def finish_quarter(quarter_sum, core, pair, split_axis, scatter_axis):
    part = lax.psum_scatter(quarter_sum, "narrow", scatter_dimension=scatter_axis, tiled=True)
    return spread_quarters(part, core, pair, split_axis)


def reduce_quarters(rows, core, pair, split_axis):
    half = rows.shape[split_axis] // 2
    mine = lax.dynamic_slice_in_dim(rows, core * half, half, axis=split_axis)
    other = lax.dynamic_slice_in_dim(rows, (1 - core) * half, half, axis=split_axis)
    chip_sum = mine + swap(other.astype(jnp.bfloat16), 1).astype(jnp.float32)
    quarter = half // 2
    keep = lax.dynamic_slice_in_dim(chip_sum, pair * quarter, quarter, axis=split_axis)
    give = lax.dynamic_slice_in_dim(chip_sum, (1 - pair) * quarter, quarter, axis=split_axis)
    return (keep + swap(give.astype(jnp.bfloat16), 2).astype(jnp.float32)).astype(jnp.bfloat16)


def spread_quarters(part, core, pair, split_axis):
    if lax.axis_size("wide") == 4:
        return join_quarters(part, core, pair, split_axis).astype(jnp.float32)
    slot = 2 * core + pair
    empty = jnp.zeros_like(part)
    slots = jnp.stack([jnp.where(slot == index, part, empty) for index in range(4)], axis=split_axis)
    total = lax.psum(slots, "wide")
    shape = list(part.shape)
    shape[split_axis] *= 4
    return total.reshape(shape).astype(jnp.float32)


def reduce_weight(rows, core, pair, split_axis, scatter_axis):
    part = lax.psum_scatter(
        reduce_quarters(rows, core, pair, split_axis),
        "narrow",
        scatter_dimension=scatter_axis,
        tiled=True,
    )
    return spread_quarters(part, core, pair, split_axis)


def reduce_column_weights(mats, core, pair):
    count = lax.axis_size("narrow")
    pieces = [reduce_quarters(rows, core, pair, 1) for rows in mats]
    joined = lax.psum_scatter(
        jnp.concatenate([piece.reshape(count, -1, piece.shape[1]) for piece in pieces], axis=1),
        "narrow",
        scatter_dimension=0,
        tiled=True,
    )[0]
    results = []
    start = 0
    for piece in pieces:
        rows_here = piece.shape[0] // count
        results.append(spread_quarters(joined[start : start + rows_here], core, pair, 1))
        start += rows_here
    return results


def shards(
    tokens,
    cotangent,
    corpus_ids,
    corpus_weights,
    qkv_weight,
    qkv_bias,
    out_weight,
    out_bias,
    up_weight,
    up_bias,
    down_weight,
    down_bias,
    norm_gains,
    norm_biases,
):
    shard_rows = tokens.shape[0]
    group_rows = shard_rows * lax.axis_size("narrow")
    seq_count = corpus_ids.shape[0]
    length = group_rows // seq_count
    block_rows = min(512, length)
    inner = qkv_weight.shape[2]
    first_row = lax.axis_index("narrow") * shard_rows
    cos_table, sine_table = rotary_tables(length, HEAD)
    layer_in = tokens.astype(jnp.float32)
    normed_first, inverse_first = norm_stats(layer_in)
    low_first = (normed_first * norm_gains[0] + norm_biases[0]).astype(jnp.bfloat16)
    core = lax.axis_index("wide") % 2
    model = layer_in.shape[1]
    heads_here = inner // HEAD
    bias_flat = jnp.concatenate([qkv_bias.reshape(-1), up_bias])
    bias_full = lax.all_gather(bias_flat, "narrow", axis=0)
    pair = (lax.axis_index("wide") // 2) % 2
    qkv_gathered = gather_halves(qkv_weight, core, 1, 2)
    qkv_gathered, up_weight, down_weight, bias_full = lax.optimization_barrier(
        (qkv_gathered, up_weight, down_weight, bias_full)
    )
    qkv_full = join_halves(qkv_gathered, core, 1)
    qkv_bias_full = jnp.swapaxes(bias_full[:, : 3 * inner].reshape(-1, 3, inner), 0, 1).reshape(
        3, model
    )
    up_bias_full = bias_full[:, 3 * inner :].reshape(-1)
    position_start = first_row % length
    cos_rows = lax.dynamic_slice_in_dim(cos_table, position_start, shard_rows, 0)
    sine_rows = lax.dynamic_slice_in_dim(sine_table, position_start, shard_rows, 0)
    qkv_rows = (
        jnp.einsum("sd,tde->tse", low_first, qkv_full, preferred_element_type=jnp.float32)
        + qkv_bias_full[:, None, :]
    )
    shaped = qkv_rows.reshape(3, shard_rows, model // HEAD, HEAD)
    qkv_tok = jnp.stack(
        [
            rotate(shaped[0], cos_rows, sine_rows),
            rotate(shaped[1], cos_rows, sine_rows),
            shaped[2],
        ]
    ).astype(jnp.bfloat16)
    qkv_heads = lax.all_to_all(qkv_tok, "narrow", 2, 1, tiled=True)
    qkv_heads = qkv_heads.reshape(3, seq_count, length, heads_here, HEAD)
    query, key_rows, values = qkv_heads[0], qkv_heads[1], qkv_heads[2]
    attn_heads, totals = attend_forward(query, key_rows, values, block_rows)
    attn_low = attn_heads.reshape(group_rows, inner).astype(jnp.bfloat16)
    attn_rows = lax.all_to_all(attn_low, "narrow", 0, 1, tiled=True)
    out_full = lax.all_gather(out_weight, "narrow", axis=0, tiled=True)
    pre_attn = jnp.dot(attn_rows, out_full, preferred_element_type=jnp.float32) + out_bias
    normed_second, inverse_second = norm_stats(pre_attn)
    residual = layer_in + normed_second * norm_gains[1] + norm_biases[1]
    normed_third, inverse_third = norm_stats(residual)
    low_third = (normed_third * norm_gains[2] + norm_biases[2]).astype(jnp.bfloat16)
    up_full = join_halves(gather_halves(up_weight, core, 0, 1), core, 0)
    down_full = join_halves(gather_halves(down_weight, core, 1, 0), core, 1)
    hidden = jnp.dot(low_third, up_full, preferred_element_type=jnp.float32) + up_bias_full
    act_low = gelu_value(hidden).astype(jnp.bfloat16)
    pre_mlp = jnp.dot(act_low, down_full, preferred_element_type=jnp.float32) + down_bias
    normed_fourth, inverse_fourth = norm_stats(pre_mlp)
    final_sum = residual + normed_fourth * norm_gains[3] + norm_biases[3]
    layer_out = final_sum.astype(jnp.bfloat16)
    row_sequence = (first_row + jnp.arange(shard_rows, dtype=jnp.int32)) // length
    row_corpus = jnp.sum(
        jnp.where(
            row_sequence[:, None] == jnp.arange(seq_count, dtype=jnp.int32)[None, :],
            corpus_ids[None, :],
            0,
        ),
        axis=1,
    )
    row_weight = jnp.sum(
        jnp.where(
            row_corpus[:, None] == jnp.arange(corpus_weights.shape[0], dtype=jnp.int32)[None, :],
            corpus_weights[None, :],
            0.0,
        ),
        axis=1,
    )
    upstream = cotangent.astype(jnp.float32) * row_weight[:, None]
    mlp_grad = norm_back(normed_fourth, inverse_fourth, norm_gains[3], upstream).astype(
        jnp.bfloat16
    )
    down_wgrad_rows = lax.dot_general(
        act_low, mlp_grad, (((0,), (0,)), ((), ())), preferred_element_type=jnp.float32
    )
    act_grad = lax.dot_general(
        mlp_grad, down_full, (((1,), (1,)), ((), ())), preferred_element_type=jnp.float32
    )
    hidden_grad = (act_grad * gelu_slope(hidden)).astype(jnp.bfloat16)
    up_bgrad_rows = jnp.sum(hidden_grad.astype(jnp.float32), axis=0)
    up_wgrad_rows = lax.dot_general(
        low_third, hidden_grad, (((0,), (0,)), ((), ())), preferred_element_type=jnp.float32
    )
    third_grad = lax.dot_general(
        hidden_grad, up_full, (((1,), (1,)), ((), ())), preferred_element_type=jnp.float32
    )
    up_chip = core_step(up_wgrad_rows, core, 0)
    down_chip = core_step(down_wgrad_rows, core, 1)
    residual_grad = upstream + norm_back(normed_third, inverse_third, norm_gains[2], third_grad)
    branch_grad = norm_back(normed_second, inverse_second, norm_gains[1], residual_grad).astype(
        jnp.bfloat16
    )
    attn_grad_rows = lax.dot_general(
        branch_grad, out_full, (((1,), (1,)), ((), ())), preferred_element_type=jnp.float32
    ).astype(jnp.bfloat16)
    attn_grad_rows, up_chip, down_chip = lax.optimization_barrier(
        (attn_grad_rows, up_chip, down_chip)
    )
    sidecar = (pair_step(up_chip, pair, 0), pair_step(down_chip, pair, 1))
    attn_grad = lax.all_to_all(attn_grad_rows, "narrow", 1, 0, tiled=True)
    attn_grad = attn_grad.reshape(query.shape)
    def scatter_pair(pieces):
        return (
            lax.psum_scatter(pieces[0], "narrow", scatter_dimension=1, tiled=True),
            lax.psum_scatter(pieces[1], "narrow", scatter_dimension=0, tiled=True),
        )

    query_grad, keys_grad, values_grad, sidecar = attend_backward(
        query, key_rows, values, attn_grad, totals, block_rows, sidecar, scatter_pair
    )
    up_wgrad = spread_quarters(sidecar[0], core, pair, 0)
    down_wgrad = spread_quarters(sidecar[1], core, pair, 1)
    out_wgrad_rows = lax.dot_general(
        attn_rows, branch_grad, (((0,), (0,)), ((), ())), preferred_element_type=jnp.float32
    )
    out_wgrad = reduce_weight(out_wgrad_rows, core, pair, 1, 0)
    qkv_grad = jnp.stack(
        [
            rotate_back(query_grad, cos_table, sine_table),
            rotate_back(keys_grad, cos_table, sine_table),
            values_grad,
        ]
    )
    qkv_grad = qkv_grad.reshape(3, group_rows, inner).astype(jnp.bfloat16)
    qkv_bgrad = jnp.sum(qkv_grad.astype(jnp.float32), axis=1)
    qkv_grad_rows = lax.all_to_all(
        qkv_grad.reshape(3, group_rows, heads_here, HEAD), "narrow", 1, 2, tiled=True
    ).reshape(3, shard_rows, model)
    qkv_wgrad_rows = jnp.einsum(
        "sd,tse->tde", low_first, qkv_grad_rows, preferred_element_type=jnp.float32
    )
    first_grad = jnp.einsum(
        "tse,tde->sd", qkv_grad_rows, qkv_full, preferred_element_type=jnp.float32
    )
    qkv_wgrad = reduce_weight(qkv_wgrad_rows, core, pair, 1, 2)
    input_grad = (
        residual_grad + norm_back(normed_first, inverse_first, norm_gains[0], first_grad)
    ).astype(jnp.bfloat16)
    gain_local = jnp.stack(
        [
            jnp.sum(first_grad * normed_first, axis=0),
            jnp.sum(residual_grad * normed_second, axis=0),
            jnp.sum(third_grad * normed_third, axis=0),
            jnp.sum(upstream * normed_fourth, axis=0),
        ]
    )
    bias_local = jnp.stack(
        [
            jnp.sum(first_grad, axis=0),
            jnp.sum(residual_grad, axis=0),
            jnp.sum(third_grad, axis=0),
            jnp.sum(upstream, axis=0),
        ]
    )
    out_blocal = jnp.sum(branch_grad.astype(jnp.float32), axis=0)
    down_blocal = jnp.sum(mlp_grad.astype(jnp.float32), axis=0)
    qkv_bgrad = lax.psum(qkv_bgrad.astype(jnp.bfloat16), "wide").astype(jnp.float32)
    small_sums = lax.psum(
        (gain_local, bias_local, out_blocal, down_blocal, up_bgrad_rows), ("wide", "narrow")
    )
    units = up_bias.shape[0]
    up_bgrad = lax.dynamic_slice_in_dim(small_sums[4], lax.axis_index("narrow") * units, units)
    return (
        layer_out,
        input_grad,
        qkv_wgrad,
        qkv_bgrad,
        out_wgrad,
        small_sums[2],
        up_wgrad,
        up_bgrad,
        down_wgrad,
        small_sums[3],
        small_sums[0],
        small_sums[1],
    )


def solution(mesh):
    return jax.shard_map(
        shards,
        mesh=mesh,
        in_specs=(
            P(("wide", "narrow"), None),
            P(("wide", "narrow"), None),
            P("wide"),
            P(),
            P(None, None, "narrow"),
            P(None, "narrow"),
            P("narrow", None),
            P(),
            P(None, "narrow"),
            P("narrow"),
            P("narrow", None),
            P(),
            P(),
            P(),
        ),
        out_specs=(
            P(("wide", "narrow"), None),
            P(("wide", "narrow"), None),
            P(None, None, "narrow"),
            P(None, "narrow"),
            P("narrow", None),
            P(),
            P(None, "narrow"),
            P("narrow"),
            P("narrow", None),
            P(),
            P(),
            P(),
        ),
        check_vma=False,
    )
```

```python
import math

import jax
import jax.numpy as jnp
from jax import lax
from jax.sharding import PartitionSpec as P

HEAD = 64


epsilon = 1e-05
root_half = 0.7071067811865476
gauss_norm = 0.3989422804014327
masked_score = -1e30


def norm_stats(vec_in):
    center = vec_in - jnp.mean(vec_in, axis=-1, keepdims=True)
    inverse = lax.rsqrt(jnp.mean(center * center, axis=-1, keepdims=True) + epsilon)
    return (center * inverse, inverse)


def norm_back(normed, inverse, gain_row, upstream):
    scaled = upstream * gain_row
    return inverse * (
        scaled
        - jnp.mean(scaled, axis=-1, keepdims=True)
        - normed * jnp.mean(scaled * normed, axis=-1, keepdims=True)
    )


def rotary_tables(length, head_size):
    half_size = head_size // 2
    inv_freq = jnp.exp(jnp.arange(half_size, dtype=jnp.float32) * (-math.log(10000.0) / half_size))
    angles = jnp.arange(length, dtype=jnp.float32)[:, None] * inv_freq[None, :]
    return (jnp.cos(angles), jnp.sin(angles))


def rotate(vectors, cos_table, sine_table):
    half_size = vectors.shape[-1] // 2
    front_half = vectors[..., :half_size]
    back_half = vectors[..., half_size:]
    cos_grid = cos_table[:, None, :]
    sin_grid = sine_table[:, None, :]
    return jnp.concatenate(
        [
            front_half * cos_grid - back_half * sin_grid,
            front_half * sin_grid + back_half * cos_grid,
        ],
        axis=-1,
    )


def rotate_back(vectors, cos_table, sine_table):
    half_size = vectors.shape[-1] // 2
    front_half = vectors[..., :half_size]
    back_half = vectors[..., half_size:]
    cos_grid = cos_table[:, None, :]
    sin_grid = sine_table[:, None, :]
    return jnp.concatenate(
        [
            front_half * cos_grid + back_half * sin_grid,
            back_half * cos_grid - front_half * sin_grid,
        ],
        axis=-1,
    )


def gelu_value(hidden):
    return 0.5 * hidden * (1.0 + lax.erf(hidden * root_half))


def gelu_slope(hidden):
    return (
        0.5 * (1.0 + lax.erf(hidden * root_half))
        + hidden * jnp.exp(-0.5 * hidden * hidden) * gauss_norm
    )


def project_qkv(gathered, qkv_weight, qkv_bias, cos_table, sine_table, seq_count, length):
    heads_here = qkv_weight.shape[2] // HEAD
    qkv_pre = (
        jnp.einsum("sd,tde->tse", gathered, qkv_weight, preferred_element_type=jnp.float32)
        + qkv_bias[:, None, :]
    )
    shaped = qkv_pre.reshape(3, seq_count, length, heads_here, HEAD)
    query = rotate(shaped[0], cos_table, sine_table).astype(jnp.bfloat16)
    key_rows = rotate(shaped[1], cos_table, sine_table).astype(jnp.bfloat16)
    values = shaped[2].astype(jnp.bfloat16)
    return (query, key_rows, values)


def block_scores(query, key_rows, block_start, block_rows):
    key_stop = block_start + block_rows
    query_block = query[:, block_start:key_stop]
    key_block = key_rows[:, :key_stop]
    scores = jnp.einsum(
        "bqhd,bkhd->bhqk", query_block, key_block, preferred_element_type=jnp.float32
    ) * (1.0 / math.sqrt(HEAD))
    query_pos = block_start + jnp.arange(block_rows)
    key_pos = jnp.arange(key_stop)
    allowed = key_pos[None, :] <= query_pos[:, None]
    return (jnp.where(allowed[None, None], scores, masked_score), query_block, key_block)


def attend_forward(query, key_rows, values, block_rows):
    length = query.shape[1]
    outputs = []
    totals = []
    for block_start in range(0, length, block_rows):
        key_stop = block_start + block_rows
        scores, query_block, key_block = block_scores(query, key_rows, block_start, block_rows)
        row_max = jnp.max(scores, axis=-1, keepdims=True)
        log_total = row_max + jnp.log(jnp.sum(jnp.exp(scores - row_max), axis=-1, keepdims=True))
        probs_low = jnp.exp(scores - log_total).astype(jnp.bfloat16)
        outputs.append(
            jnp.einsum(
                "bhqk,bkhd->bqhd",
                probs_low,
                values[:, :key_stop],
                preferred_element_type=jnp.float32,
            )
        )
        totals.append(log_total)
    return (jnp.concatenate(outputs, axis=1), totals)


def attend_backward(query, key_rows, values, attn_grad, totals, block_rows):
    length = query.shape[1]
    score_scale = 1.0 / math.sqrt(HEAD)
    keys_grad = jnp.zeros(key_rows.shape, jnp.float32)
    values_grad = jnp.zeros(values.shape, jnp.float32)
    query_grads = []
    for block_number, block_start in enumerate(range(0, length, block_rows)):
        key_stop = block_start + block_rows
        scores, query_block, key_block = block_scores(query, key_rows, block_start, block_rows)
        value_block = values[:, :key_stop]
        grad_block = attn_grad[:, block_start:key_stop]
        probs_full = jnp.exp(scores - totals[block_number])
        probs_low = probs_full.astype(jnp.bfloat16)
        probs_grad = jnp.einsum(
            "bqhd,bkhd->bhqk", grad_block, value_block, preferred_element_type=jnp.float32
        )
        row_dot = jnp.sum(probs_full * probs_grad, axis=-1, keepdims=True)
        scores_grad = (probs_full * (probs_grad - row_dot)).astype(jnp.bfloat16)
        query_grads.append(
            jnp.einsum(
                "bhqk,bkhd->bqhd", scores_grad, key_block, preferred_element_type=jnp.float32
            )
            * score_scale
        )
        pad_rows = ((0, 0), (0, length - key_stop), (0, 0), (0, 0))
        keys_grad = keys_grad + jnp.pad(
            jnp.einsum(
                "bhqk,bqhd->bkhd", scores_grad, query_block, preferred_element_type=jnp.float32
            )
            * score_scale,
            pad_rows,
        )
        values_grad = values_grad + jnp.pad(
            jnp.einsum(
                "bhqk,bqhd->bkhd", probs_low, grad_block, preferred_element_type=jnp.float32
            ),
            pad_rows,
        )
    return (
        jnp.concatenate(query_grads, axis=1),
        keys_grad,
        values_grad,
    )


def swap_cores(block):
    count = lax.axis_size("wide")
    return lax.ppermute(block, "wide", [(index, index ^ 1) for index in range(count)])


def gather_mine(shard, core, split_axis, gather_axis):
    half = shard.shape[split_axis] // 2
    mine = lax.dynamic_slice_in_dim(shard, core * half, half, axis=split_axis)
    return lax.all_gather(mine, "narrow", axis=gather_axis, tiled=True)


def gather_halves(shard, core, split_axis, gather_axis):
    return join_halves(gather_mine(shard, core, split_axis, gather_axis), core, split_axis)


def join_halves(gathered, core, split_axis):
    partner = swap_cores(gathered)
    first = jnp.where(core == 0, gathered, partner)
    second = jnp.where(core == 0, partner, gathered)
    return jnp.concatenate([first, second], axis=split_axis)


def reduce_halves(rows, core, split_axis, scatter_axis):
    half = rows.shape[split_axis] // 2
    mine = lax.dynamic_slice_in_dim(rows, core * half, half, axis=split_axis)
    other = lax.dynamic_slice_in_dim(rows, (1 - core) * half, half, axis=split_axis)
    chip_sum = mine + swap_cores(other.astype(jnp.bfloat16)).astype(jnp.float32)
    part = lax.psum_scatter(
        chip_sum.astype(jnp.bfloat16), "narrow", scatter_dimension=scatter_axis, tiled=True
    )
    empty = jnp.zeros_like(part)
    return jnp.stack(
        [jnp.where(core == 0, part, empty), jnp.where(core == 0, empty, part)], axis=split_axis
    )


def reduce_column_halves(mats, core):
    count = lax.axis_size("narrow")
    pieces = []
    for rows in mats:
        half = rows.shape[1] // 2
        mine = lax.dynamic_slice_in_dim(rows, core * half, half, axis=1)
        other = lax.dynamic_slice_in_dim(rows, (1 - core) * half, half, axis=1)
        chip_sum = mine + swap_cores(other.astype(jnp.bfloat16)).astype(jnp.float32)
        pieces.append(chip_sum.astype(jnp.bfloat16).reshape(count, -1, half))
    joined = lax.psum_scatter(
        jnp.concatenate(pieces, axis=1), "narrow", scatter_dimension=0, tiled=True
    )[0]
    results = []
    start = 0
    for piece in pieces:
        part = joined[start : start + piece.shape[1]]
        start += piece.shape[1]
        empty = jnp.zeros_like(part)
        results.append(
            jnp.stack([jnp.where(core == 0, part, empty), jnp.where(core == 0, empty, part)], axis=1)
        )
    return results


def merge_slots(slots, split_axis):
    shape = list(slots.shape)
    shape[split_axis : split_axis + 2] = [shape[split_axis] * shape[split_axis + 1]]
    return slots.reshape(shape)


def shards(
    tokens,
    cotangent,
    corpus_ids,
    corpus_weights,
    qkv_weight,
    qkv_bias,
    out_weight,
    out_bias,
    up_weight,
    up_bias,
    down_weight,
    down_bias,
    norm_gains,
    norm_biases,
):
    shard_rows = tokens.shape[0]
    group_rows = shard_rows * lax.axis_size("narrow")
    seq_count = corpus_ids.shape[0]
    length = group_rows // seq_count
    block_rows = min(512, length)
    inner = qkv_weight.shape[2]
    first_row = lax.axis_index("narrow") * shard_rows
    cos_table, sine_table = rotary_tables(length, HEAD)
    layer_in = tokens.astype(jnp.float32)
    normed_first, inverse_first = norm_stats(layer_in)
    low_first = (normed_first * norm_gains[0] + norm_biases[0]).astype(jnp.bfloat16)
    core = lax.axis_index("wide") % 2
    model = layer_in.shape[1]
    heads_here = inner // HEAD
    bias_flat = jnp.concatenate([qkv_bias.reshape(-1), up_bias])
    bias_full = lax.all_gather(bias_flat, "narrow", axis=0)
    qkv_gathered = gather_mine(qkv_weight, core, 1, 2)
    qkv_gathered, up_weight, down_weight, bias_full = lax.optimization_barrier(
        (qkv_gathered, up_weight, down_weight, bias_full)
    )
    qkv_full = join_halves(qkv_gathered, core, 1)
    qkv_bias_full = jnp.swapaxes(bias_full[:, : 3 * inner].reshape(-1, 3, inner), 0, 1).reshape(
        3, model
    )
    up_bias_full = bias_full[:, 3 * inner :].reshape(-1)
    position_start = first_row % length
    cos_rows = lax.dynamic_slice_in_dim(cos_table, position_start, shard_rows, 0)
    sine_rows = lax.dynamic_slice_in_dim(sine_table, position_start, shard_rows, 0)
    qkv_rows = (
        jnp.einsum("sd,tde->tse", low_first, qkv_full, preferred_element_type=jnp.float32)
        + qkv_bias_full[:, None, :]
    )
    shaped = qkv_rows.reshape(3, shard_rows, model // HEAD, HEAD)
    qkv_tok = (
        jnp.stack(
            [
                rotate(shaped[0], cos_rows, sine_rows),
                rotate(shaped[1], cos_rows, sine_rows),
                shaped[2],
            ]
        )
        .astype(jnp.bfloat16)
        .reshape(3, shard_rows, model)
    )
    qkv_heads = lax.all_to_all(qkv_tok, "narrow", 2, 1, tiled=True)
    qkv_heads = qkv_heads.reshape(3, seq_count, length, heads_here, HEAD)
    query, key_rows, values = qkv_heads[0], qkv_heads[1], qkv_heads[2]
    attn_heads, totals = attend_forward(query, key_rows, values, block_rows)
    attn_low = attn_heads.reshape(group_rows, inner).astype(jnp.bfloat16)
    attn_rows = lax.all_to_all(attn_low, "narrow", 0, 1, tiled=True)
    out_full = lax.all_gather(out_weight, "narrow", axis=0, tiled=True)
    pre_attn = jnp.dot(attn_rows, out_full, preferred_element_type=jnp.float32) + out_bias
    normed_second, inverse_second = norm_stats(pre_attn)
    residual = layer_in + normed_second * norm_gains[1] + norm_biases[1]
    normed_third, inverse_third = norm_stats(residual)
    low_third = (normed_third * norm_gains[2] + norm_biases[2]).astype(jnp.bfloat16)
    up_full = gather_halves(up_weight, core, 0, 1)
    down_full = gather_halves(down_weight, core, 1, 0)
    hidden = jnp.dot(low_third, up_full, preferred_element_type=jnp.float32) + up_bias_full
    act_low = gelu_value(hidden).astype(jnp.bfloat16)
    pre_mlp = jnp.dot(act_low, down_full, preferred_element_type=jnp.float32) + down_bias
    normed_fourth, inverse_fourth = norm_stats(pre_mlp)
    final_sum = residual + normed_fourth * norm_gains[3] + norm_biases[3]
    layer_out = final_sum.astype(jnp.bfloat16)
    row_sequence = (first_row + jnp.arange(shard_rows, dtype=jnp.int32)) // length
    row_corpus = jnp.sum(
        jnp.where(
            row_sequence[:, None] == jnp.arange(seq_count, dtype=jnp.int32)[None, :],
            corpus_ids[None, :],
            0,
        ),
        axis=1,
    )
    row_weight = jnp.sum(
        jnp.where(
            row_corpus[:, None] == jnp.arange(corpus_weights.shape[0], dtype=jnp.int32)[None, :],
            corpus_weights[None, :],
            0.0,
        ),
        axis=1,
    )
    upstream = cotangent.astype(jnp.float32) * row_weight[:, None]
    mlp_grad = norm_back(normed_fourth, inverse_fourth, norm_gains[3], upstream).astype(
        jnp.bfloat16
    )
    down_wgrad_rows = lax.dot_general(
        act_low, mlp_grad, (((0,), (0,)), ((), ())), preferred_element_type=jnp.float32
    )
    act_grad = lax.dot_general(
        mlp_grad, down_full, (((1,), (1,)), ((), ())), preferred_element_type=jnp.float32
    )
    hidden_grad = (act_grad * gelu_slope(hidden)).astype(jnp.bfloat16)
    up_bgrad_rows = jnp.sum(hidden_grad.astype(jnp.float32), axis=0)
    up_wgrad_rows = lax.dot_general(
        low_third, hidden_grad, (((0,), (0,)), ((), ())), preferred_element_type=jnp.float32
    )
    third_grad = lax.dot_general(
        hidden_grad, up_full, (((1,), (1,)), ((), ())), preferred_element_type=jnp.float32
    )
    up_slots = reduce_halves(up_wgrad_rows, core, 0, 1)
    residual_grad = upstream + norm_back(normed_third, inverse_third, norm_gains[2], third_grad)
    branch_grad = norm_back(normed_second, inverse_second, norm_gains[1], residual_grad).astype(
        jnp.bfloat16
    )
    attn_grad_rows = lax.dot_general(
        branch_grad, out_full, (((1,), (1,)), ((), ())), preferred_element_type=jnp.float32
    ).astype(jnp.bfloat16)
    attn_grad = lax.all_to_all(attn_grad_rows, "narrow", 1, 0, tiled=True)
    attn_grad = attn_grad.reshape(query.shape)
    query_grad, keys_grad, values_grad = attend_backward(
        query, key_rows, values, attn_grad, totals, block_rows
    )
    out_wgrad_rows = lax.dot_general(
        attn_rows, branch_grad, (((0,), (0,)), ((), ())), preferred_element_type=jnp.float32
    )
    down_slots, out_slots = reduce_column_halves((down_wgrad_rows, out_wgrad_rows), core)
    qkv_grad = jnp.stack(
        [
            rotate_back(query_grad, cos_table, sine_table),
            rotate_back(keys_grad, cos_table, sine_table),
            values_grad,
        ]
    )
    qkv_grad = qkv_grad.reshape(3, group_rows, inner).astype(jnp.bfloat16)
    qkv_bgrad = jnp.sum(qkv_grad.astype(jnp.float32), axis=1)
    qkv_grad_rows = lax.all_to_all(qkv_grad, "narrow", 1, 2, tiled=True)
    qkv_wgrad_rows = jnp.einsum(
        "sd,tse->tde", low_first, qkv_grad_rows, preferred_element_type=jnp.float32
    )
    first_grad = jnp.einsum(
        "tse,tde->sd", qkv_grad_rows, qkv_full, preferred_element_type=jnp.float32
    )
    qkv_slots = reduce_halves(qkv_wgrad_rows, core, 1, 2)
    input_grad = (
        residual_grad + norm_back(normed_first, inverse_first, norm_gains[0], first_grad)
    ).astype(jnp.bfloat16)
    gain_local = jnp.stack(
        [
            jnp.sum(first_grad * normed_first, axis=0),
            jnp.sum(residual_grad * normed_second, axis=0),
            jnp.sum(third_grad * normed_third, axis=0),
            jnp.sum(upstream * normed_fourth, axis=0),
        ]
    )
    bias_local = jnp.stack(
        [
            jnp.sum(first_grad, axis=0),
            jnp.sum(residual_grad, axis=0),
            jnp.sum(third_grad, axis=0),
            jnp.sum(upstream, axis=0),
        ]
    )
    out_blocal = jnp.sum(branch_grad.astype(jnp.float32), axis=0)
    down_blocal = jnp.sum(mlp_grad.astype(jnp.float32), axis=0)
    weight_sums = (
        lax.psum(qkv_slots, "wide").astype(jnp.float32),
        lax.psum(qkv_bgrad.astype(jnp.bfloat16), "wide").astype(jnp.float32),
        lax.psum(out_slots, "wide").astype(jnp.float32),
        lax.psum(up_slots, "wide").astype(jnp.float32),
        None,
        lax.psum(down_slots, "wide").astype(jnp.float32),
    )
    small_sums = lax.psum(
        (gain_local, bias_local, out_blocal, down_blocal, up_bgrad_rows), ("wide", "narrow")
    )
    units = up_bias.shape[0]
    up_bgrad = lax.dynamic_slice_in_dim(small_sums[4], lax.axis_index("narrow") * units, units)
    up_wgrad = merge_slots(weight_sums[3], 0)
    down_wgrad = merge_slots(weight_sums[5], 1)
    out_wgrad = merge_slots(weight_sums[2], 1)
    qkv_wgrad = merge_slots(weight_sums[0], 1)
    return (
        layer_out,
        input_grad,
        qkv_wgrad,
        weight_sums[1],
        out_wgrad,
        small_sums[2],
        up_wgrad,
        up_bgrad,
        down_wgrad,
        small_sums[3],
        small_sums[0],
        small_sums[1],
    )


def solution(mesh):
    return jax.shard_map(
        shards,
        mesh=mesh,
        in_specs=(
            P(("wide", "narrow"), None),
            P(("wide", "narrow"), None),
            P("wide"),
            P(),
            P(None, None, "narrow"),
            P(None, "narrow"),
            P("narrow", None),
            P(),
            P(None, "narrow"),
            P("narrow"),
            P("narrow", None),
            P(),
            P(),
            P(),
        ),
        out_specs=(
            P(("wide", "narrow"), None),
            P(("wide", "narrow"), None),
            P(None, None, "narrow"),
            P(None, "narrow"),
            P("narrow", None),
            P(),
            P(None, "narrow"),
            P("narrow"),
            P("narrow", None),
            P(),
            P(),
            P(),
        ),
        check_vma=False,
    )
```

```python
import math

import jax
import jax.numpy as jnp
from jax import lax
from jax.sharding import PartitionSpec as P

HEAD = 64


epsilon = 1e-05
root_half = 0.7071067811865476
gauss_norm = 0.3989422804014327
masked_score = -1e30


def norm_stats(vec_in):
    center = vec_in - jnp.mean(vec_in, axis=-1, keepdims=True)
    inverse = lax.rsqrt(jnp.mean(center * center, axis=-1, keepdims=True) + epsilon)
    return (center * inverse, inverse)


def norm_back(normed, inverse, gain_row, upstream):
    scaled = upstream * gain_row
    return inverse * (
        scaled
        - jnp.mean(scaled, axis=-1, keepdims=True)
        - normed * jnp.mean(scaled * normed, axis=-1, keepdims=True)
    )


def rotary_tables(length, head_size):
    half_size = head_size // 2
    inv_freq = jnp.exp(jnp.arange(half_size, dtype=jnp.float32) * (-math.log(10000.0) / half_size))
    angles = jnp.arange(length, dtype=jnp.float32)[:, None] * inv_freq[None, :]
    return (jnp.cos(angles), jnp.sin(angles))


def rotate(vectors, cos_table, sine_table):
    half_size = vectors.shape[-1] // 2
    front_half = vectors[..., :half_size]
    back_half = vectors[..., half_size:]
    cos_grid = cos_table[:, None, :]
    sin_grid = sine_table[:, None, :]
    return jnp.concatenate(
        [
            front_half * cos_grid - back_half * sin_grid,
            front_half * sin_grid + back_half * cos_grid,
        ],
        axis=-1,
    )


def rotate_back(vectors, cos_table, sine_table):
    half_size = vectors.shape[-1] // 2
    front_half = vectors[..., :half_size]
    back_half = vectors[..., half_size:]
    cos_grid = cos_table[:, None, :]
    sin_grid = sine_table[:, None, :]
    return jnp.concatenate(
        [
            front_half * cos_grid + back_half * sin_grid,
            back_half * cos_grid - front_half * sin_grid,
        ],
        axis=-1,
    )


def gelu_value(hidden):
    return 0.5 * hidden * (1.0 + lax.erf(hidden * root_half))


def gelu_slope(hidden):
    return (
        0.5 * (1.0 + lax.erf(hidden * root_half))
        + hidden * jnp.exp(-0.5 * hidden * hidden) * gauss_norm
    )


def project_qkv(gathered, qkv_weight, qkv_bias, cos_table, sine_table, seq_count, length):
    heads_here = qkv_weight.shape[2] // HEAD
    qkv_pre = (
        jnp.einsum("sd,tde->tse", gathered, qkv_weight, preferred_element_type=jnp.float32)
        + qkv_bias[:, None, :]
    )
    shaped = qkv_pre.reshape(3, seq_count, length, heads_here, HEAD)
    query = rotate(shaped[0], cos_table, sine_table).astype(jnp.bfloat16)
    key_rows = rotate(shaped[1], cos_table, sine_table).astype(jnp.bfloat16)
    values = shaped[2].astype(jnp.bfloat16)
    return (query, key_rows, values)


def block_scores(query, key_rows, block_start, block_rows):
    key_stop = block_start + block_rows
    query_block = query[:, block_start:key_stop]
    key_block = key_rows[:, :key_stop]
    scores = jnp.einsum(
        "bqhd,bkhd->bhqk", query_block, key_block, preferred_element_type=jnp.float32
    ) * (1.0 / math.sqrt(HEAD))
    query_pos = block_start + jnp.arange(block_rows)
    key_pos = jnp.arange(key_stop)
    allowed = key_pos[None, :] <= query_pos[:, None]
    return (jnp.where(allowed[None, None], scores, masked_score), query_block, key_block)


def attend_forward(query, key_rows, values, block_rows):
    length = query.shape[1]
    outputs = []
    totals = []
    for block_start in range(0, length, block_rows):
        key_stop = block_start + block_rows
        scores, query_block, key_block = block_scores(query, key_rows, block_start, block_rows)
        row_max = jnp.max(scores, axis=-1, keepdims=True)
        log_total = row_max + jnp.log(jnp.sum(jnp.exp(scores - row_max), axis=-1, keepdims=True))
        probs_low = jnp.exp(scores - log_total).astype(jnp.bfloat16)
        outputs.append(
            jnp.einsum(
                "bhqk,bkhd->bqhd",
                probs_low,
                values[:, :key_stop],
                preferred_element_type=jnp.float32,
            )
        )
        totals.append(log_total)
    return (jnp.concatenate(outputs, axis=1), totals)


def attend_backward(query, key_rows, values, attn_grad, totals, block_rows):
    length = query.shape[1]
    score_scale = 1.0 / math.sqrt(HEAD)
    keys_grad = jnp.zeros(key_rows.shape, jnp.float32)
    values_grad = jnp.zeros(values.shape, jnp.float32)
    query_grads = []
    for block_number, block_start in enumerate(range(0, length, block_rows)):
        key_stop = block_start + block_rows
        scores, query_block, key_block = block_scores(query, key_rows, block_start, block_rows)
        value_block = values[:, :key_stop]
        grad_block = attn_grad[:, block_start:key_stop]
        probs_full = jnp.exp(scores - totals[block_number])
        probs_low = probs_full.astype(jnp.bfloat16)
        probs_grad = jnp.einsum(
            "bqhd,bkhd->bhqk", grad_block, value_block, preferred_element_type=jnp.float32
        )
        row_dot = jnp.sum(probs_full * probs_grad, axis=-1, keepdims=True)
        scores_grad = (probs_full * (probs_grad - row_dot)).astype(jnp.bfloat16)
        query_grads.append(
            jnp.einsum(
                "bhqk,bkhd->bqhd", scores_grad, key_block, preferred_element_type=jnp.float32
            )
            * score_scale
        )
        pad_rows = ((0, 0), (0, length - key_stop), (0, 0), (0, 0))
        keys_grad = keys_grad + jnp.pad(
            jnp.einsum(
                "bhqk,bqhd->bkhd", scores_grad, query_block, preferred_element_type=jnp.float32
            )
            * score_scale,
            pad_rows,
        )
        values_grad = values_grad + jnp.pad(
            jnp.einsum(
                "bhqk,bqhd->bkhd", probs_low, grad_block, preferred_element_type=jnp.float32
            ),
            pad_rows,
        )
    return (
        jnp.concatenate(query_grads, axis=1),
        keys_grad,
        values_grad,
    )


def swap_cores(block):
    count = lax.axis_size("wide")
    return lax.ppermute(block, "wide", [(index, index ^ 1) for index in range(count)])


def gather_mine(shard, core, split_axis, gather_axis):
    half = shard.shape[split_axis] // 2
    mine = lax.dynamic_slice_in_dim(shard, core * half, half, axis=split_axis)
    return lax.all_gather(mine, "narrow", axis=gather_axis, tiled=True)


def gather_halves(shard, core, split_axis, gather_axis):
    return join_halves(gather_mine(shard, core, split_axis, gather_axis), core, split_axis)


def join_halves(gathered, core, split_axis):
    partner = swap_cores(gathered)
    first = jnp.where(core == 0, gathered, partner)
    second = jnp.where(core == 0, partner, gathered)
    return jnp.concatenate([first, second], axis=split_axis)


def reduce_halves(rows, core, split_axis, scatter_axis):
    half = rows.shape[split_axis] // 2
    mine = lax.dynamic_slice_in_dim(rows, core * half, half, axis=split_axis)
    other = lax.dynamic_slice_in_dim(rows, (1 - core) * half, half, axis=split_axis)
    chip_sum = mine + swap_cores(other.astype(jnp.bfloat16)).astype(jnp.float32)
    part = lax.psum_scatter(
        chip_sum.astype(jnp.bfloat16), "narrow", scatter_dimension=scatter_axis, tiled=True
    )
    empty = jnp.zeros_like(part)
    return jnp.stack(
        [jnp.where(core == 0, part, empty), jnp.where(core == 0, empty, part)], axis=split_axis
    )


def reduce_column_halves(mats, core):
    count = lax.axis_size("narrow")
    pieces = []
    for rows in mats:
        half = rows.shape[1] // 2
        mine = lax.dynamic_slice_in_dim(rows, core * half, half, axis=1)
        other = lax.dynamic_slice_in_dim(rows, (1 - core) * half, half, axis=1)
        chip_sum = mine + swap_cores(other.astype(jnp.bfloat16)).astype(jnp.float32)
        pieces.append(chip_sum.astype(jnp.bfloat16).reshape(count, -1, half))
    joined = lax.psum_scatter(
        jnp.concatenate(pieces, axis=1), "narrow", scatter_dimension=0, tiled=True
    )[0]
    results = []
    start = 0
    for piece in pieces:
        part = joined[start : start + piece.shape[1]]
        start += piece.shape[1]
        empty = jnp.zeros_like(part)
        results.append(
            jnp.stack([jnp.where(core == 0, part, empty), jnp.where(core == 0, empty, part)], axis=1)
        )
    return results


def merge_slots(slots, split_axis):
    shape = list(slots.shape)
    shape[split_axis : split_axis + 2] = [shape[split_axis] * shape[split_axis + 1]]
    return slots.reshape(shape)


def shards(
    tokens,
    cotangent,
    corpus_ids,
    corpus_weights,
    qkv_weight,
    qkv_bias,
    out_weight,
    out_bias,
    up_weight,
    up_bias,
    down_weight,
    down_bias,
    norm_gains,
    norm_biases,
):
    shard_rows = tokens.shape[0]
    group_rows = shard_rows * lax.axis_size("narrow")
    seq_count = corpus_ids.shape[0]
    length = group_rows // seq_count
    block_rows = min(512, length)
    inner = qkv_weight.shape[2]
    first_row = lax.axis_index("narrow") * shard_rows
    cos_table, sine_table = rotary_tables(length, HEAD)
    layer_in = tokens.astype(jnp.float32)
    normed_first, inverse_first = norm_stats(layer_in)
    low_first = (normed_first * norm_gains[0] + norm_biases[0]).astype(jnp.bfloat16)
    core = lax.axis_index("wide") % 2
    model = layer_in.shape[1]
    heads_here = inner // HEAD
    bias_flat = jnp.concatenate([qkv_bias.reshape(-1), up_bias])
    bias_full = lax.all_gather(bias_flat, "narrow", axis=0)
    qkv_gathered = gather_mine(qkv_weight, core, 1, 2)
    out_gathered = gather_mine(out_weight, core, 1, 0)
    qkv_gathered, out_gathered, up_weight, down_weight, bias_full = lax.optimization_barrier(
        (qkv_gathered, out_gathered, up_weight, down_weight, bias_full)
    )
    qkv_full = join_halves(qkv_gathered, core, 1)
    qkv_bias_full = jnp.swapaxes(bias_full[:, : 3 * inner].reshape(-1, 3, inner), 0, 1).reshape(
        3, model
    )
    up_bias_full = bias_full[:, 3 * inner :].reshape(-1)
    position_start = first_row % length
    cos_rows = lax.dynamic_slice_in_dim(cos_table, position_start, shard_rows, 0)
    sine_rows = lax.dynamic_slice_in_dim(sine_table, position_start, shard_rows, 0)
    qkv_rows = (
        jnp.einsum("sd,tde->tse", low_first, qkv_full, preferred_element_type=jnp.float32)
        + qkv_bias_full[:, None, :]
    )
    shaped = qkv_rows.reshape(3, shard_rows, model // HEAD, HEAD)
    qkv_tok = jnp.stack(
        [
            rotate(shaped[0], cos_rows, sine_rows),
            rotate(shaped[1], cos_rows, sine_rows),
            shaped[2],
        ]
    ).astype(jnp.bfloat16)
    qkv_heads = lax.all_to_all(qkv_tok, "narrow", 2, 1, tiled=True)
    qkv_heads = qkv_heads.reshape(3, seq_count, length, heads_here, HEAD)
    query, key_rows, values = qkv_heads[0], qkv_heads[1], qkv_heads[2]
    attn_heads, totals = attend_forward(query, key_rows, values, block_rows)
    attn_low = attn_heads.reshape(group_rows, inner).astype(jnp.bfloat16)
    attn_rows = lax.all_to_all(attn_low, "narrow", 0, 1, tiled=True)
    out_full = join_halves(out_gathered, core, 1)
    pre_attn = jnp.dot(attn_rows, out_full, preferred_element_type=jnp.float32) + out_bias
    normed_second, inverse_second = norm_stats(pre_attn)
    residual = layer_in + normed_second * norm_gains[1] + norm_biases[1]
    normed_third, inverse_third = norm_stats(residual)
    low_third = (normed_third * norm_gains[2] + norm_biases[2]).astype(jnp.bfloat16)
    up_full = gather_halves(up_weight, core, 0, 1)
    down_full = gather_halves(down_weight, core, 1, 0)
    hidden = jnp.dot(low_third, up_full, preferred_element_type=jnp.float32) + up_bias_full
    act_low = gelu_value(hidden).astype(jnp.bfloat16)
    pre_mlp = jnp.dot(act_low, down_full, preferred_element_type=jnp.float32) + down_bias
    normed_fourth, inverse_fourth = norm_stats(pre_mlp)
    final_sum = residual + normed_fourth * norm_gains[3] + norm_biases[3]
    layer_out = final_sum.astype(jnp.bfloat16)
    row_sequence = (first_row + jnp.arange(shard_rows, dtype=jnp.int32)) // length
    row_corpus = jnp.sum(
        jnp.where(
            row_sequence[:, None] == jnp.arange(seq_count, dtype=jnp.int32)[None, :],
            corpus_ids[None, :],
            0,
        ),
        axis=1,
    )
    row_weight = jnp.sum(
        jnp.where(
            row_corpus[:, None] == jnp.arange(corpus_weights.shape[0], dtype=jnp.int32)[None, :],
            corpus_weights[None, :],
            0.0,
        ),
        axis=1,
    )
    upstream = cotangent.astype(jnp.float32) * row_weight[:, None]
    mlp_grad = norm_back(normed_fourth, inverse_fourth, norm_gains[3], upstream).astype(
        jnp.bfloat16
    )
    down_wgrad_rows = lax.dot_general(
        act_low, mlp_grad, (((0,), (0,)), ((), ())), preferred_element_type=jnp.float32
    )
    act_grad = lax.dot_general(
        mlp_grad, down_full, (((1,), (1,)), ((), ())), preferred_element_type=jnp.float32
    )
    hidden_grad = (act_grad * gelu_slope(hidden)).astype(jnp.bfloat16)
    up_bgrad_rows = jnp.sum(hidden_grad.astype(jnp.float32), axis=0)
    up_wgrad_rows = lax.dot_general(
        low_third, hidden_grad, (((0,), (0,)), ((), ())), preferred_element_type=jnp.float32
    )
    third_grad = lax.dot_general(
        hidden_grad, up_full, (((1,), (1,)), ((), ())), preferred_element_type=jnp.float32
    )
    up_slots = reduce_halves(up_wgrad_rows, core, 0, 1)
    residual_grad = upstream + norm_back(normed_third, inverse_third, norm_gains[2], third_grad)
    branch_grad = norm_back(normed_second, inverse_second, norm_gains[1], residual_grad).astype(
        jnp.bfloat16
    )
    attn_grad_rows = lax.dot_general(
        branch_grad, out_full, (((1,), (1,)), ((), ())), preferred_element_type=jnp.float32
    ).astype(jnp.bfloat16)
    attn_grad = lax.all_to_all(attn_grad_rows, "narrow", 1, 0, tiled=True)
    attn_grad = attn_grad.reshape(query.shape)
    query_grad, keys_grad, values_grad = attend_backward(
        query, key_rows, values, attn_grad, totals, block_rows
    )
    out_wgrad_rows = lax.dot_general(
        attn_rows, branch_grad, (((0,), (0,)), ((), ())), preferred_element_type=jnp.float32
    )
    down_slots, out_slots = reduce_column_halves((down_wgrad_rows, out_wgrad_rows), core)
    qkv_grad = jnp.stack(
        [
            rotate_back(query_grad, cos_table, sine_table),
            rotate_back(keys_grad, cos_table, sine_table),
            values_grad,
        ]
    )
    qkv_grad = qkv_grad.reshape(3, group_rows, inner).astype(jnp.bfloat16)
    qkv_bgrad = jnp.sum(qkv_grad.astype(jnp.float32), axis=1)
    qkv_grad_rows = lax.all_to_all(
        qkv_grad.reshape(3, group_rows, heads_here, HEAD), "narrow", 1, 2, tiled=True
    ).reshape(3, shard_rows, model)
    qkv_wgrad_rows = jnp.einsum(
        "sd,tse->tde", low_first, qkv_grad_rows, preferred_element_type=jnp.float32
    )
    first_grad = jnp.einsum(
        "tse,tde->sd", qkv_grad_rows, qkv_full, preferred_element_type=jnp.float32
    )
    qkv_slots = reduce_halves(qkv_wgrad_rows, core, 1, 2)
    input_grad = (
        residual_grad + norm_back(normed_first, inverse_first, norm_gains[0], first_grad)
    ).astype(jnp.bfloat16)
    gain_local = jnp.stack(
        [
            jnp.sum(first_grad * normed_first, axis=0),
            jnp.sum(residual_grad * normed_second, axis=0),
            jnp.sum(third_grad * normed_third, axis=0),
            jnp.sum(upstream * normed_fourth, axis=0),
        ]
    )
    bias_local = jnp.stack(
        [
            jnp.sum(first_grad, axis=0),
            jnp.sum(residual_grad, axis=0),
            jnp.sum(third_grad, axis=0),
            jnp.sum(upstream, axis=0),
        ]
    )
    out_blocal = jnp.sum(branch_grad.astype(jnp.float32), axis=0)
    down_blocal = jnp.sum(mlp_grad.astype(jnp.float32), axis=0)
    weight_sums = (
        lax.psum(qkv_slots, "wide").astype(jnp.float32),
        lax.psum(qkv_bgrad.astype(jnp.bfloat16), "wide").astype(jnp.float32),
        lax.psum(out_slots, "wide").astype(jnp.float32),
        lax.psum(up_slots, "wide").astype(jnp.float32),
        None,
        lax.psum(down_slots, "wide").astype(jnp.float32),
    )
    small_sums = lax.psum(
        (gain_local, bias_local, out_blocal, down_blocal, up_bgrad_rows), ("wide", "narrow")
    )
    units = up_bias.shape[0]
    up_bgrad = lax.dynamic_slice_in_dim(small_sums[4], lax.axis_index("narrow") * units, units)
    up_wgrad = merge_slots(weight_sums[3], 0)
    down_wgrad = merge_slots(weight_sums[5], 1)
    out_wgrad = merge_slots(weight_sums[2], 1)
    qkv_wgrad = merge_slots(weight_sums[0], 1)
    return (
        layer_out,
        input_grad,
        qkv_wgrad,
        weight_sums[1],
        out_wgrad,
        small_sums[2],
        up_wgrad,
        up_bgrad,
        down_wgrad,
        small_sums[3],
        small_sums[0],
        small_sums[1],
    )


def solution(mesh):
    return jax.shard_map(
        shards,
        mesh=mesh,
        in_specs=(
            P(("wide", "narrow"), None),
            P(("wide", "narrow"), None),
            P("wide"),
            P(),
            P(None, None, "narrow"),
            P(None, "narrow"),
            P("narrow", None),
            P(),
            P(None, "narrow"),
            P("narrow"),
            P("narrow", None),
            P(),
            P(),
            P(),
        ),
        out_specs=(
            P(("wide", "narrow"), None),
            P(("wide", "narrow"), None),
            P(None, None, "narrow"),
            P(None, "narrow"),
            P("narrow", None),
            P(),
            P(None, "narrow"),
            P("narrow"),
            P("narrow", None),
            P(),
            P(),
            P(),
        ),
        check_vma=False,
    )
```

```python
import math

import jax
import jax.numpy as jnp
from jax import lax
from jax.sharding import PartitionSpec as P

HEAD = 64


epsilon = 1e-05
root_half = 0.7071067811865476
gauss_norm = 0.3989422804014327
masked_score = -1e30


def norm_stats(vec_in):
    center = vec_in - jnp.mean(vec_in, axis=-1, keepdims=True)
    inverse = lax.rsqrt(jnp.mean(center * center, axis=-1, keepdims=True) + epsilon)
    return (center * inverse, inverse)


def norm_back(normed, inverse, gain_row, upstream):
    scaled = upstream * gain_row
    return inverse * (
        scaled
        - jnp.mean(scaled, axis=-1, keepdims=True)
        - normed * jnp.mean(scaled * normed, axis=-1, keepdims=True)
    )


def rotary_tables(length, head_size):
    half_size = head_size // 2
    inv_freq = jnp.exp(jnp.arange(half_size, dtype=jnp.float32) * (-math.log(10000.0) / half_size))
    angles = jnp.arange(length, dtype=jnp.float32)[:, None] * inv_freq[None, :]
    return (jnp.cos(angles), jnp.sin(angles))


def rotate(vectors, cos_table, sine_table):
    half_size = vectors.shape[-1] // 2
    front_half = vectors[..., :half_size]
    back_half = vectors[..., half_size:]
    cos_grid = cos_table[:, None, :]
    sin_grid = sine_table[:, None, :]
    return jnp.concatenate(
        [
            front_half * cos_grid - back_half * sin_grid,
            front_half * sin_grid + back_half * cos_grid,
        ],
        axis=-1,
    )


def rotate_back(vectors, cos_table, sine_table):
    half_size = vectors.shape[-1] // 2
    front_half = vectors[..., :half_size]
    back_half = vectors[..., half_size:]
    cos_grid = cos_table[:, None, :]
    sin_grid = sine_table[:, None, :]
    return jnp.concatenate(
        [
            front_half * cos_grid + back_half * sin_grid,
            back_half * cos_grid - front_half * sin_grid,
        ],
        axis=-1,
    )


def gelu_value(hidden):
    return 0.5 * hidden * (1.0 + lax.erf(hidden * root_half))


def gelu_slope(hidden):
    return (
        0.5 * (1.0 + lax.erf(hidden * root_half))
        + hidden * jnp.exp(-0.5 * hidden * hidden) * gauss_norm
    )


def project_qkv(gathered, qkv_weight, qkv_bias, cos_table, sine_table, seq_count, length):
    heads_here = qkv_weight.shape[2] // HEAD
    qkv_pre = (
        jnp.einsum("sd,tde->tse", gathered, qkv_weight, preferred_element_type=jnp.float32)
        + qkv_bias[:, None, :]
    )
    shaped = qkv_pre.reshape(3, seq_count, length, heads_here, HEAD)
    query = rotate(shaped[0], cos_table, sine_table).astype(jnp.bfloat16)
    key_rows = rotate(shaped[1], cos_table, sine_table).astype(jnp.bfloat16)
    values = shaped[2].astype(jnp.bfloat16)
    return (query, key_rows, values)


def block_scores(query, key_rows, block_start, block_rows):
    key_stop = block_start + block_rows
    query_block = query[:, block_start:key_stop]
    key_block = key_rows[:, :key_stop]
    scores = jnp.einsum(
        "bqhd,bkhd->bhqk", query_block, key_block, preferred_element_type=jnp.float32
    ) * (1.0 / math.sqrt(HEAD))
    query_pos = block_start + jnp.arange(block_rows)
    key_pos = jnp.arange(key_stop)
    allowed = key_pos[None, :] <= query_pos[:, None]
    return (jnp.where(allowed[None, None], scores, masked_score), query_block, key_block)


def attend_forward(query, key_rows, values, block_rows):
    length = query.shape[1]
    outputs = []
    totals = []
    for block_start in range(0, length, block_rows):
        key_stop = block_start + block_rows
        scores, query_block, key_block = block_scores(query, key_rows, block_start, block_rows)
        row_max = jnp.max(scores, axis=-1, keepdims=True)
        log_total = row_max + jnp.log(jnp.sum(jnp.exp(scores - row_max), axis=-1, keepdims=True))
        probs_low = jnp.exp(scores - log_total).astype(jnp.bfloat16)
        outputs.append(
            jnp.einsum(
                "bhqk,bkhd->bqhd",
                probs_low,
                values[:, :key_stop],
                preferred_element_type=jnp.float32,
            )
        )
        totals.append(log_total)
    return (jnp.concatenate(outputs, axis=1), totals)


def attend_backward(query, key_rows, values, attn_grad, totals, block_rows):
    length = query.shape[1]
    score_scale = 1.0 / math.sqrt(HEAD)
    keys_grad = jnp.zeros(key_rows.shape, jnp.float32)
    values_grad = jnp.zeros(values.shape, jnp.float32)
    query_grads = []
    for block_number, block_start in enumerate(range(0, length, block_rows)):
        key_stop = block_start + block_rows
        scores, query_block, key_block = block_scores(query, key_rows, block_start, block_rows)
        value_block = values[:, :key_stop]
        grad_block = attn_grad[:, block_start:key_stop]
        probs_full = jnp.exp(scores - totals[block_number])
        probs_low = probs_full.astype(jnp.bfloat16)
        probs_grad = jnp.einsum(
            "bqhd,bkhd->bhqk", grad_block, value_block, preferred_element_type=jnp.float32
        )
        row_dot = jnp.sum(probs_full * probs_grad, axis=-1, keepdims=True)
        scores_grad = (probs_full * (probs_grad - row_dot)).astype(jnp.bfloat16)
        query_grads.append(
            jnp.einsum(
                "bhqk,bkhd->bqhd", scores_grad, key_block, preferred_element_type=jnp.float32
            )
            * score_scale
        )
        pad_rows = ((0, 0), (0, length - key_stop), (0, 0), (0, 0))
        keys_grad = keys_grad + jnp.pad(
            jnp.einsum(
                "bhqk,bqhd->bkhd", scores_grad, query_block, preferred_element_type=jnp.float32
            )
            * score_scale,
            pad_rows,
        )
        values_grad = values_grad + jnp.pad(
            jnp.einsum(
                "bhqk,bqhd->bkhd", probs_low, grad_block, preferred_element_type=jnp.float32
            ),
            pad_rows,
        )
    return (
        jnp.concatenate(query_grads, axis=1),
        keys_grad,
        values_grad,
    )


def swap_cores(block):
    count = lax.axis_size("wide")
    return lax.ppermute(block, "wide", [(index, index ^ 1) for index in range(count)])


def gather_mine(shard, core, split_axis, gather_axis):
    half = shard.shape[split_axis] // 2
    mine = lax.dynamic_slice_in_dim(shard, core * half, half, axis=split_axis)
    return lax.all_gather(mine, "narrow", axis=gather_axis, tiled=True)


def gather_halves(shard, core, split_axis, gather_axis):
    return join_halves(gather_mine(shard, core, split_axis, gather_axis), core, split_axis)


def join_halves(gathered, core, split_axis):
    partner = swap_cores(gathered)
    first = jnp.where(core == 0, gathered, partner)
    second = jnp.where(core == 0, partner, gathered)
    return jnp.concatenate([first, second], axis=split_axis)


def reduce_halves(rows, core, split_axis, scatter_axis):
    half = rows.shape[split_axis] // 2
    mine = lax.dynamic_slice_in_dim(rows, core * half, half, axis=split_axis)
    other = lax.dynamic_slice_in_dim(rows, (1 - core) * half, half, axis=split_axis)
    chip_sum = mine + swap_cores(other.astype(jnp.bfloat16)).astype(jnp.float32)
    part = lax.psum_scatter(
        chip_sum.astype(jnp.bfloat16), "narrow", scatter_dimension=scatter_axis, tiled=True
    )
    empty = jnp.zeros_like(part)
    return jnp.stack(
        [jnp.where(core == 0, part, empty), jnp.where(core == 0, empty, part)], axis=split_axis
    )


def reduce_column_halves(mats, core):
    count = lax.axis_size("narrow")
    pieces = []
    for rows in mats:
        half = rows.shape[1] // 2
        mine = lax.dynamic_slice_in_dim(rows, core * half, half, axis=1)
        other = lax.dynamic_slice_in_dim(rows, (1 - core) * half, half, axis=1)
        chip_sum = mine + swap_cores(other.astype(jnp.bfloat16)).astype(jnp.float32)
        pieces.append(chip_sum.astype(jnp.bfloat16).reshape(count, -1, half))
    joined = lax.psum_scatter(
        jnp.concatenate(pieces, axis=1), "narrow", scatter_dimension=0, tiled=True
    )[0]
    results = []
    start = 0
    for piece in pieces:
        part = joined[start : start + piece.shape[1]]
        start += piece.shape[1]
        empty = jnp.zeros_like(part)
        results.append(
            jnp.stack([jnp.where(core == 0, part, empty), jnp.where(core == 0, empty, part)], axis=1)
        )
    return results


def merge_slots(slots, split_axis):
    shape = list(slots.shape)
    shape[split_axis : split_axis + 2] = [shape[split_axis] * shape[split_axis + 1]]
    return slots.reshape(shape)


def shards(
    tokens,
    cotangent,
    corpus_ids,
    corpus_weights,
    qkv_weight,
    qkv_bias,
    out_weight,
    out_bias,
    up_weight,
    up_bias,
    down_weight,
    down_bias,
    norm_gains,
    norm_biases,
):
    shard_rows = tokens.shape[0]
    group_rows = shard_rows * lax.axis_size("narrow")
    seq_count = corpus_ids.shape[0]
    length = group_rows // seq_count
    block_rows = min(512, length)
    inner = qkv_weight.shape[2]
    first_row = lax.axis_index("narrow") * shard_rows
    cos_table, sine_table = rotary_tables(length, HEAD)
    layer_in = tokens.astype(jnp.float32)
    normed_first, inverse_first = norm_stats(layer_in)
    low_first = (normed_first * norm_gains[0] + norm_biases[0]).astype(jnp.bfloat16)
    core = lax.axis_index("wide") % 2
    model = layer_in.shape[1]
    heads_here = inner // HEAD
    bias_flat = jnp.concatenate([qkv_bias.reshape(-1), up_bias])
    bias_full = lax.all_gather(bias_flat, "narrow", axis=0)
    qkv_gathered = gather_mine(qkv_weight, core, 1, 2)
    qkv_gathered, out_weight, bias_full = lax.optimization_barrier(
        (qkv_gathered, out_weight, bias_full)
    )
    out_gathered = gather_mine(out_weight, core, 1, 0)
    out_gathered, up_weight, down_weight = lax.optimization_barrier(
        (out_gathered, up_weight, down_weight)
    )
    up_gathered = gather_mine(up_weight, core, 0, 1)
    down_gathered = gather_mine(down_weight, core, 1, 0)
    qkv_full = join_halves(qkv_gathered, core, 1)
    qkv_bias_full = jnp.swapaxes(bias_full[:, : 3 * inner].reshape(-1, 3, inner), 0, 1).reshape(
        3, model
    )
    up_bias_full = bias_full[:, 3 * inner :].reshape(-1)
    position_start = first_row % length
    cos_rows = lax.dynamic_slice_in_dim(cos_table, position_start, shard_rows, 0)
    sine_rows = lax.dynamic_slice_in_dim(sine_table, position_start, shard_rows, 0)
    qkv_rows = (
        jnp.einsum("sd,tde->tse", low_first, qkv_full, preferred_element_type=jnp.float32)
        + qkv_bias_full[:, None, :]
    )
    shaped = qkv_rows.reshape(3, shard_rows, model // HEAD, HEAD)
    qkv_tok = jnp.stack(
        [
            rotate(shaped[0], cos_rows, sine_rows),
            rotate(shaped[1], cos_rows, sine_rows),
            shaped[2],
        ]
    ).astype(jnp.bfloat16)
    qkv_heads = lax.all_to_all(qkv_tok, "narrow", 2, 1, tiled=True)
    qkv_heads = qkv_heads.reshape(3, seq_count, length, heads_here, HEAD)
    query, key_rows, values = qkv_heads[0], qkv_heads[1], qkv_heads[2]
    attn_heads, totals = attend_forward(query, key_rows, values, block_rows)
    attn_heads, up_gathered, down_gathered = lax.optimization_barrier(
        (attn_heads, up_gathered, down_gathered)
    )
    attn_low = attn_heads.reshape(group_rows, inner).astype(jnp.bfloat16)
    attn_rows = lax.all_to_all(attn_low, "narrow", 0, 1, tiled=True)
    out_full = join_halves(out_gathered, core, 1)
    pre_attn = jnp.dot(attn_rows, out_full, preferred_element_type=jnp.float32) + out_bias
    normed_second, inverse_second = norm_stats(pre_attn)
    residual = layer_in + normed_second * norm_gains[1] + norm_biases[1]
    normed_third, inverse_third = norm_stats(residual)
    low_third = (normed_third * norm_gains[2] + norm_biases[2]).astype(jnp.bfloat16)
    up_full = join_halves(up_gathered, core, 0)
    down_full = join_halves(down_gathered, core, 1)
    hidden = jnp.dot(low_third, up_full, preferred_element_type=jnp.float32) + up_bias_full
    act_low = gelu_value(hidden).astype(jnp.bfloat16)
    pre_mlp = jnp.dot(act_low, down_full, preferred_element_type=jnp.float32) + down_bias
    normed_fourth, inverse_fourth = norm_stats(pre_mlp)
    final_sum = residual + normed_fourth * norm_gains[3] + norm_biases[3]
    layer_out = final_sum.astype(jnp.bfloat16)
    row_sequence = (first_row + jnp.arange(shard_rows, dtype=jnp.int32)) // length
    row_corpus = jnp.sum(
        jnp.where(
            row_sequence[:, None] == jnp.arange(seq_count, dtype=jnp.int32)[None, :],
            corpus_ids[None, :],
            0,
        ),
        axis=1,
    )
    row_weight = jnp.sum(
        jnp.where(
            row_corpus[:, None] == jnp.arange(corpus_weights.shape[0], dtype=jnp.int32)[None, :],
            corpus_weights[None, :],
            0.0,
        ),
        axis=1,
    )
    upstream = cotangent.astype(jnp.float32) * row_weight[:, None]
    mlp_grad = norm_back(normed_fourth, inverse_fourth, norm_gains[3], upstream).astype(
        jnp.bfloat16
    )
    down_wgrad_rows = lax.dot_general(
        act_low, mlp_grad, (((0,), (0,)), ((), ())), preferred_element_type=jnp.float32
    )
    act_grad = lax.dot_general(
        mlp_grad, down_full, (((1,), (1,)), ((), ())), preferred_element_type=jnp.float32
    )
    hidden_grad = (act_grad * gelu_slope(hidden)).astype(jnp.bfloat16)
    up_bgrad_rows = jnp.sum(hidden_grad.astype(jnp.float32), axis=0)
    up_wgrad_rows = lax.dot_general(
        low_third, hidden_grad, (((0,), (0,)), ((), ())), preferred_element_type=jnp.float32
    )
    third_grad = lax.dot_general(
        hidden_grad, up_full, (((1,), (1,)), ((), ())), preferred_element_type=jnp.float32
    )
    up_slots = reduce_halves(up_wgrad_rows, core, 0, 1)
    residual_grad = upstream + norm_back(normed_third, inverse_third, norm_gains[2], third_grad)
    branch_grad = norm_back(normed_second, inverse_second, norm_gains[1], residual_grad).astype(
        jnp.bfloat16
    )
    attn_grad_rows = lax.dot_general(
        branch_grad, out_full, (((1,), (1,)), ((), ())), preferred_element_type=jnp.float32
    ).astype(jnp.bfloat16)
    attn_grad = lax.all_to_all(attn_grad_rows, "narrow", 1, 0, tiled=True)
    attn_grad = attn_grad.reshape(query.shape)
    query_grad, keys_grad, values_grad = attend_backward(
        query, key_rows, values, attn_grad, totals, block_rows
    )
    out_wgrad_rows = lax.dot_general(
        attn_rows, branch_grad, (((0,), (0,)), ((), ())), preferred_element_type=jnp.float32
    )
    down_slots, out_slots = reduce_column_halves((down_wgrad_rows, out_wgrad_rows), core)
    qkv_grad = jnp.stack(
        [
            rotate_back(query_grad, cos_table, sine_table),
            rotate_back(keys_grad, cos_table, sine_table),
            values_grad,
        ]
    )
    qkv_grad = qkv_grad.reshape(3, group_rows, inner).astype(jnp.bfloat16)
    qkv_bgrad = jnp.sum(qkv_grad.astype(jnp.float32), axis=1)
    qkv_grad_rows = lax.all_to_all(
        qkv_grad.reshape(3, group_rows, heads_here, HEAD), "narrow", 1, 2, tiled=True
    ).reshape(3, shard_rows, model)
    qkv_wgrad_rows = jnp.einsum(
        "sd,tse->tde", low_first, qkv_grad_rows, preferred_element_type=jnp.float32
    )
    first_grad = jnp.einsum(
        "tse,tde->sd", qkv_grad_rows, qkv_full, preferred_element_type=jnp.float32
    )
    qkv_slots = reduce_halves(qkv_wgrad_rows, core, 1, 2)
    input_grad = (
        residual_grad + norm_back(normed_first, inverse_first, norm_gains[0], first_grad)
    ).astype(jnp.bfloat16)
    gain_local = jnp.stack(
        [
            jnp.sum(first_grad * normed_first, axis=0),
            jnp.sum(residual_grad * normed_second, axis=0),
            jnp.sum(third_grad * normed_third, axis=0),
            jnp.sum(upstream * normed_fourth, axis=0),
        ]
    )
    bias_local = jnp.stack(
        [
            jnp.sum(first_grad, axis=0),
            jnp.sum(residual_grad, axis=0),
            jnp.sum(third_grad, axis=0),
            jnp.sum(upstream, axis=0),
        ]
    )
    out_blocal = jnp.sum(branch_grad.astype(jnp.float32), axis=0)
    down_blocal = jnp.sum(mlp_grad.astype(jnp.float32), axis=0)
    weight_sums = (
        lax.psum(qkv_slots, "wide").astype(jnp.float32),
        lax.psum(qkv_bgrad.astype(jnp.bfloat16), "wide").astype(jnp.float32),
        lax.psum(out_slots, "wide").astype(jnp.float32),
        lax.psum(up_slots, "wide").astype(jnp.float32),
        None,
        lax.psum(down_slots, "wide").astype(jnp.float32),
    )
    small_sums = lax.psum(
        (gain_local, bias_local, out_blocal, down_blocal, up_bgrad_rows), ("wide", "narrow")
    )
    units = up_bias.shape[0]
    up_bgrad = lax.dynamic_slice_in_dim(small_sums[4], lax.axis_index("narrow") * units, units)
    up_wgrad = merge_slots(weight_sums[3], 0)
    down_wgrad = merge_slots(weight_sums[5], 1)
    out_wgrad = merge_slots(weight_sums[2], 1)
    qkv_wgrad = merge_slots(weight_sums[0], 1)
    return (
        layer_out,
        input_grad,
        qkv_wgrad,
        weight_sums[1],
        out_wgrad,
        small_sums[2],
        up_wgrad,
        up_bgrad,
        down_wgrad,
        small_sums[3],
        small_sums[0],
        small_sums[1],
    )


def solution(mesh):
    return jax.shard_map(
        shards,
        mesh=mesh,
        in_specs=(
            P(("wide", "narrow"), None),
            P(("wide", "narrow"), None),
            P("wide"),
            P(),
            P(None, None, "narrow"),
            P(None, "narrow"),
            P("narrow", None),
            P(),
            P(None, "narrow"),
            P("narrow"),
            P("narrow", None),
            P(),
            P(),
            P(),
        ),
        out_specs=(
            P(("wide", "narrow"), None),
            P(("wide", "narrow"), None),
            P(None, None, "narrow"),
            P(None, "narrow"),
            P("narrow", None),
            P(),
            P(None, "narrow"),
            P("narrow"),
            P("narrow", None),
            P(),
            P(),
            P(),
        ),
        check_vma=False,
    )
```

```python
import math

import jax
import jax.numpy as jnp
from jax import lax
from jax.sharding import PartitionSpec as P

HEAD = 64


epsilon = 1e-05
root_half = 0.7071067811865476
gauss_norm = 0.3989422804014327
masked_score = -1e30


def norm_stats(vec_in):
    center = vec_in - jnp.mean(vec_in, axis=-1, keepdims=True)
    inverse = lax.rsqrt(jnp.mean(center * center, axis=-1, keepdims=True) + epsilon)
    return (center * inverse, inverse)


def norm_back(normed, inverse, gain_row, upstream):
    scaled = upstream * gain_row
    return inverse * (
        scaled
        - jnp.mean(scaled, axis=-1, keepdims=True)
        - normed * jnp.mean(scaled * normed, axis=-1, keepdims=True)
    )


def rotary_tables(length, head_size):
    half_size = head_size // 2
    inv_freq = jnp.exp(jnp.arange(half_size, dtype=jnp.float32) * (-math.log(10000.0) / half_size))
    angles = jnp.arange(length, dtype=jnp.float32)[:, None] * inv_freq[None, :]
    return (jnp.cos(angles), jnp.sin(angles))


def rotate(vectors, cos_table, sine_table):
    half_size = vectors.shape[-1] // 2
    front_half = vectors[..., :half_size]
    back_half = vectors[..., half_size:]
    cos_grid = cos_table[:, None, :]
    sin_grid = sine_table[:, None, :]
    return jnp.concatenate(
        [
            front_half * cos_grid - back_half * sin_grid,
            front_half * sin_grid + back_half * cos_grid,
        ],
        axis=-1,
    )


def rotate_back(vectors, cos_table, sine_table):
    half_size = vectors.shape[-1] // 2
    front_half = vectors[..., :half_size]
    back_half = vectors[..., half_size:]
    cos_grid = cos_table[:, None, :]
    sin_grid = sine_table[:, None, :]
    return jnp.concatenate(
        [
            front_half * cos_grid + back_half * sin_grid,
            back_half * cos_grid - front_half * sin_grid,
        ],
        axis=-1,
    )


def gelu_value(hidden):
    return 0.5 * hidden * (1.0 + lax.erf(hidden * root_half))


def gelu_slope(hidden):
    return (
        0.5 * (1.0 + lax.erf(hidden * root_half))
        + hidden * jnp.exp(-0.5 * hidden * hidden) * gauss_norm
    )


def project_qkv(gathered, qkv_weight, qkv_bias, cos_table, sine_table, seq_count, length):
    heads_here = qkv_weight.shape[2] // HEAD
    qkv_pre = (
        jnp.einsum("sd,tde->tse", gathered, qkv_weight, preferred_element_type=jnp.float32)
        + qkv_bias[:, None, :]
    )
    shaped = qkv_pre.reshape(3, seq_count, length, heads_here, HEAD)
    query = rotate(shaped[0], cos_table, sine_table).astype(jnp.bfloat16)
    key_rows = rotate(shaped[1], cos_table, sine_table).astype(jnp.bfloat16)
    values = shaped[2].astype(jnp.bfloat16)
    return (query, key_rows, values)


def block_scores(query, key_rows, block_start, block_rows):
    key_stop = block_start + block_rows
    query_block = query[:, block_start:key_stop]
    key_block = key_rows[:, :key_stop]
    scores = jnp.einsum(
        "bqhd,bkhd->bhqk", query_block, key_block, preferred_element_type=jnp.float32
    ) * (1.0 / math.sqrt(HEAD))
    query_pos = block_start + jnp.arange(block_rows)
    key_pos = jnp.arange(key_stop)
    allowed = key_pos[None, :] <= query_pos[:, None]
    return (jnp.where(allowed[None, None], scores, masked_score), query_block, key_block)


def attend_forward(query, key_rows, values, block_rows):
    length = query.shape[1]
    outputs = []
    totals = []
    for block_start in range(0, length, block_rows):
        key_stop = block_start + block_rows
        scores, query_block, key_block = block_scores(query, key_rows, block_start, block_rows)
        row_max = jnp.max(scores, axis=-1, keepdims=True)
        log_total = row_max + jnp.log(jnp.sum(jnp.exp(scores - row_max), axis=-1, keepdims=True))
        probs_low = jnp.exp(scores - log_total).astype(jnp.bfloat16)
        outputs.append(
            jnp.einsum(
                "bhqk,bkhd->bqhd",
                probs_low,
                values[:, :key_stop],
                preferred_element_type=jnp.float32,
            )
        )
        totals.append(log_total)
    return (jnp.concatenate(outputs, axis=1), totals)


def attend_backward(query, key_rows, values, attn_grad, totals, block_rows):
    length = query.shape[1]
    score_scale = 1.0 / math.sqrt(HEAD)
    keys_grad = jnp.zeros(key_rows.shape, jnp.float32)
    values_grad = jnp.zeros(values.shape, jnp.float32)
    query_grads = []
    for block_number, block_start in enumerate(range(0, length, block_rows)):
        key_stop = block_start + block_rows
        scores, query_block, key_block = block_scores(query, key_rows, block_start, block_rows)
        value_block = values[:, :key_stop]
        grad_block = attn_grad[:, block_start:key_stop]
        probs_full = jnp.exp(scores - totals[block_number])
        probs_low = probs_full.astype(jnp.bfloat16)
        probs_grad = jnp.einsum(
            "bqhd,bkhd->bhqk", grad_block, value_block, preferred_element_type=jnp.float32
        )
        row_dot = jnp.sum(probs_full * probs_grad, axis=-1, keepdims=True)
        scores_grad = (probs_full * (probs_grad - row_dot)).astype(jnp.bfloat16)
        query_grads.append(
            jnp.einsum(
                "bhqk,bkhd->bqhd", scores_grad, key_block, preferred_element_type=jnp.float32
            )
            * score_scale
        )
        pad_rows = ((0, 0), (0, length - key_stop), (0, 0), (0, 0))
        keys_grad = keys_grad + jnp.pad(
            jnp.einsum(
                "bhqk,bqhd->bkhd", scores_grad, query_block, preferred_element_type=jnp.float32
            )
            * score_scale,
            pad_rows,
        )
        values_grad = values_grad + jnp.pad(
            jnp.einsum(
                "bhqk,bqhd->bkhd", probs_low, grad_block, preferred_element_type=jnp.float32
            ),
            pad_rows,
        )
    return (
        jnp.concatenate(query_grads, axis=1),
        keys_grad,
        values_grad,
    )


def swap_cores(block):
    count = lax.axis_size("wide")
    return lax.ppermute(block, "wide", [(index, index ^ 1) for index in range(count)])


def gather_mine(shard, core, split_axis, gather_axis):
    half = shard.shape[split_axis] // 2
    mine = lax.dynamic_slice_in_dim(shard, core * half, half, axis=split_axis)
    return lax.all_gather(mine, "narrow", axis=gather_axis, tiled=True)


def gather_halves(shard, core, split_axis, gather_axis):
    return join_halves(gather_mine(shard, core, split_axis, gather_axis), core, split_axis)


def join_halves(gathered, core, split_axis):
    partner = swap_cores(gathered)
    first = jnp.where(core == 0, gathered, partner)
    second = jnp.where(core == 0, partner, gathered)
    return jnp.concatenate([first, second], axis=split_axis)


def reduce_halves(rows, core, split_axis, scatter_axis):
    half = rows.shape[split_axis] // 2
    mine = lax.dynamic_slice_in_dim(rows, core * half, half, axis=split_axis)
    other = lax.dynamic_slice_in_dim(rows, (1 - core) * half, half, axis=split_axis)
    chip_sum = mine + swap_cores(other.astype(jnp.bfloat16)).astype(jnp.float32)
    part = lax.psum_scatter(
        chip_sum.astype(jnp.bfloat16), "narrow", scatter_dimension=scatter_axis, tiled=True
    )
    empty = jnp.zeros_like(part)
    return jnp.stack(
        [jnp.where(core == 0, part, empty), jnp.where(core == 0, empty, part)], axis=split_axis
    )


def reduce_column_halves(mats, core):
    count = lax.axis_size("narrow")
    pieces = []
    for rows in mats:
        half = rows.shape[1] // 2
        mine = lax.dynamic_slice_in_dim(rows, core * half, half, axis=1)
        other = lax.dynamic_slice_in_dim(rows, (1 - core) * half, half, axis=1)
        chip_sum = mine + swap_cores(other.astype(jnp.bfloat16)).astype(jnp.float32)
        pieces.append(chip_sum.astype(jnp.bfloat16).reshape(count, -1, half))
    joined = lax.psum_scatter(
        jnp.concatenate(pieces, axis=1), "narrow", scatter_dimension=0, tiled=True
    )[0]
    results = []
    start = 0
    for piece in pieces:
        part = joined[start : start + piece.shape[1]]
        start += piece.shape[1]
        empty = jnp.zeros_like(part)
        results.append(
            jnp.stack([jnp.where(core == 0, part, empty), jnp.where(core == 0, empty, part)], axis=1)
        )
    return results


def merge_slots(slots, split_axis):
    shape = list(slots.shape)
    shape[split_axis : split_axis + 2] = [shape[split_axis] * shape[split_axis + 1]]
    return slots.reshape(shape)


def shards(
    tokens,
    cotangent,
    corpus_ids,
    corpus_weights,
    qkv_weight,
    qkv_bias,
    out_weight,
    out_bias,
    up_weight,
    up_bias,
    down_weight,
    down_bias,
    norm_gains,
    norm_biases,
):
    shard_rows = tokens.shape[0]
    group_rows = shard_rows * lax.axis_size("narrow")
    seq_count = corpus_ids.shape[0]
    length = group_rows // seq_count
    block_rows = min(512, length)
    inner = qkv_weight.shape[2]
    first_row = lax.axis_index("narrow") * shard_rows
    cos_table, sine_table = rotary_tables(length, HEAD)
    layer_in = tokens.astype(jnp.float32)
    normed_first, inverse_first = norm_stats(layer_in)
    low_first = (normed_first * norm_gains[0] + norm_biases[0]).astype(jnp.bfloat16)
    core = lax.axis_index("wide") % 2
    model = layer_in.shape[1]
    heads_here = inner // HEAD
    bias_flat = jnp.concatenate([qkv_bias.reshape(-1), up_bias])
    bias_full = lax.all_gather(bias_flat, "narrow", axis=0)
    gathered_first = lax.all_gather(low_first, "narrow", axis=0, tiled=True)
    gathered_first, up_weight, down_weight, bias_full = lax.optimization_barrier(
        (gathered_first, up_weight, down_weight, bias_full)
    )
    up_bias_full = bias_full[:, 3 * inner :].reshape(-1)
    query, key_rows, values = project_qkv(
        gathered_first, qkv_weight, qkv_bias, cos_table, sine_table, seq_count, length
    )
    attn_heads, totals = attend_forward(query, key_rows, values, block_rows)
    attn_low = attn_heads.reshape(group_rows, inner).astype(jnp.bfloat16)
    attn_rows = lax.all_to_all(attn_low, "narrow", 0, 1, tiled=True)
    out_full = lax.all_gather(out_weight, "narrow", axis=0, tiled=True)
    pre_attn = jnp.dot(attn_rows, out_full, preferred_element_type=jnp.float32) + out_bias
    normed_second, inverse_second = norm_stats(pre_attn)
    residual = layer_in + normed_second * norm_gains[1] + norm_biases[1]
    normed_third, inverse_third = norm_stats(residual)
    low_third = (normed_third * norm_gains[2] + norm_biases[2]).astype(jnp.bfloat16)
    up_full = gather_halves(up_weight, core, 0, 1)
    down_full = gather_halves(down_weight, core, 1, 0)
    hidden = jnp.dot(low_third, up_full, preferred_element_type=jnp.float32) + up_bias_full
    act_low = gelu_value(hidden).astype(jnp.bfloat16)
    act_low, qkv_late = lax.optimization_barrier((act_low, qkv_weight))
    qkv_full = join_halves(gather_mine(qkv_late, core, 1, 2), core, 1)
    pre_mlp = jnp.dot(act_low, down_full, preferred_element_type=jnp.float32) + down_bias
    normed_fourth, inverse_fourth = norm_stats(pre_mlp)
    final_sum = residual + normed_fourth * norm_gains[3] + norm_biases[3]
    layer_out = final_sum.astype(jnp.bfloat16)
    row_sequence = (first_row + jnp.arange(shard_rows, dtype=jnp.int32)) // length
    row_corpus = jnp.sum(
        jnp.where(
            row_sequence[:, None] == jnp.arange(seq_count, dtype=jnp.int32)[None, :],
            corpus_ids[None, :],
            0,
        ),
        axis=1,
    )
    row_weight = jnp.sum(
        jnp.where(
            row_corpus[:, None] == jnp.arange(corpus_weights.shape[0], dtype=jnp.int32)[None, :],
            corpus_weights[None, :],
            0.0,
        ),
        axis=1,
    )
    upstream = cotangent.astype(jnp.float32) * row_weight[:, None]
    mlp_grad = norm_back(normed_fourth, inverse_fourth, norm_gains[3], upstream).astype(
        jnp.bfloat16
    )
    down_wgrad_rows = lax.dot_general(
        act_low, mlp_grad, (((0,), (0,)), ((), ())), preferred_element_type=jnp.float32
    )
    act_grad = lax.dot_general(
        mlp_grad, down_full, (((1,), (1,)), ((), ())), preferred_element_type=jnp.float32
    )
    hidden_grad = (act_grad * gelu_slope(hidden)).astype(jnp.bfloat16)
    up_bgrad_rows = jnp.sum(hidden_grad.astype(jnp.float32), axis=0)
    up_wgrad_rows = lax.dot_general(
        low_third, hidden_grad, (((0,), (0,)), ((), ())), preferred_element_type=jnp.float32
    )
    third_grad = lax.dot_general(
        hidden_grad, up_full, (((1,), (1,)), ((), ())), preferred_element_type=jnp.float32
    )
    up_slots = reduce_halves(up_wgrad_rows, core, 0, 1)
    residual_grad = upstream + norm_back(normed_third, inverse_third, norm_gains[2], third_grad)
    branch_grad = norm_back(normed_second, inverse_second, norm_gains[1], residual_grad).astype(
        jnp.bfloat16
    )
    attn_grad_rows = lax.dot_general(
        branch_grad, out_full, (((1,), (1,)), ((), ())), preferred_element_type=jnp.float32
    ).astype(jnp.bfloat16)
    attn_grad = lax.all_to_all(attn_grad_rows, "narrow", 1, 0, tiled=True)
    attn_grad = attn_grad.reshape(query.shape)
    query_grad, keys_grad, values_grad = attend_backward(
        query, key_rows, values, attn_grad, totals, block_rows
    )
    out_wgrad_rows = lax.dot_general(
        attn_rows, branch_grad, (((0,), (0,)), ((), ())), preferred_element_type=jnp.float32
    )
    down_slots, out_slots = reduce_column_halves((down_wgrad_rows, out_wgrad_rows), core)
    qkv_grad = jnp.stack(
        [
            rotate_back(query_grad, cos_table, sine_table),
            rotate_back(keys_grad, cos_table, sine_table),
            values_grad,
        ]
    )
    qkv_grad = qkv_grad.reshape(3, group_rows, inner).astype(jnp.bfloat16)
    qkv_bgrad = jnp.sum(qkv_grad.astype(jnp.float32), axis=1)
    qkv_grad_rows = lax.all_to_all(
        qkv_grad.reshape(3, group_rows, heads_here, HEAD), "narrow", 1, 2, tiled=True
    ).reshape(3, shard_rows, model)
    qkv_wgrad = jnp.einsum(
        "sd,tse->tde", gathered_first, qkv_grad, preferred_element_type=jnp.float32
    )
    first_grad = jnp.einsum(
        "tse,tde->sd", qkv_grad_rows, qkv_full, preferred_element_type=jnp.float32
    )
    input_grad = (
        residual_grad + norm_back(normed_first, inverse_first, norm_gains[0], first_grad)
    ).astype(jnp.bfloat16)
    gain_local = jnp.stack(
        [
            jnp.sum(first_grad * normed_first, axis=0),
            jnp.sum(residual_grad * normed_second, axis=0),
            jnp.sum(third_grad * normed_third, axis=0),
            jnp.sum(upstream * normed_fourth, axis=0),
        ]
    )
    bias_local = jnp.stack(
        [
            jnp.sum(first_grad, axis=0),
            jnp.sum(residual_grad, axis=0),
            jnp.sum(third_grad, axis=0),
            jnp.sum(upstream, axis=0),
        ]
    )
    out_blocal = jnp.sum(branch_grad.astype(jnp.float32), axis=0)
    down_blocal = jnp.sum(mlp_grad.astype(jnp.float32), axis=0)
    weight_sums = (
        lax.psum(qkv_wgrad.astype(jnp.bfloat16), "wide").astype(jnp.float32),
        lax.psum(qkv_bgrad.astype(jnp.bfloat16), "wide").astype(jnp.float32),
        lax.psum(out_slots, "wide").astype(jnp.float32),
        lax.psum(up_slots, "wide").astype(jnp.float32),
        None,
        lax.psum(down_slots, "wide").astype(jnp.float32),
    )
    small_sums = lax.psum(
        (gain_local, bias_local, out_blocal, down_blocal, up_bgrad_rows), ("wide", "narrow")
    )
    units = up_bias.shape[0]
    up_bgrad = lax.dynamic_slice_in_dim(small_sums[4], lax.axis_index("narrow") * units, units)
    up_wgrad = merge_slots(weight_sums[3], 0)
    down_wgrad = merge_slots(weight_sums[5], 1)
    out_wgrad = merge_slots(weight_sums[2], 1)
    qkv_wgrad = weight_sums[0]
    return (
        layer_out,
        input_grad,
        qkv_wgrad,
        weight_sums[1],
        out_wgrad,
        small_sums[2],
        up_wgrad,
        up_bgrad,
        down_wgrad,
        small_sums[3],
        small_sums[0],
        small_sums[1],
    )


def solution(mesh):
    return jax.shard_map(
        shards,
        mesh=mesh,
        in_specs=(
            P(("wide", "narrow"), None),
            P(("wide", "narrow"), None),
            P("wide"),
            P(),
            P(None, None, "narrow"),
            P(None, "narrow"),
            P("narrow", None),
            P(),
            P(None, "narrow"),
            P("narrow"),
            P("narrow", None),
            P(),
            P(),
            P(),
        ),
        out_specs=(
            P(("wide", "narrow"), None),
            P(("wide", "narrow"), None),
            P(None, None, "narrow"),
            P(None, "narrow"),
            P("narrow", None),
            P(),
            P(None, "narrow"),
            P("narrow"),
            P("narrow", None),
            P(),
            P(),
            P(),
        ),
        check_vma=False,
    )
```

```python
import math

import jax
import jax.numpy as jnp
from jax import lax
from jax.sharding import PartitionSpec as P

HEAD = 64


epsilon = 1e-05
root_half = 0.7071067811865476
gauss_norm = 0.3989422804014327
masked_score = -1e30


def norm_stats(vec_in):
    center = vec_in - jnp.mean(vec_in, axis=-1, keepdims=True)
    inverse = lax.rsqrt(jnp.mean(center * center, axis=-1, keepdims=True) + epsilon)
    return (center * inverse, inverse)


def norm_back(normed, inverse, gain_row, upstream):
    scaled = upstream * gain_row
    return inverse * (
        scaled
        - jnp.mean(scaled, axis=-1, keepdims=True)
        - normed * jnp.mean(scaled * normed, axis=-1, keepdims=True)
    )


def rotary_tables(length, head_size):
    half_size = head_size // 2
    inv_freq = jnp.exp(jnp.arange(half_size, dtype=jnp.float32) * (-math.log(10000.0) / half_size))
    angles = jnp.arange(length, dtype=jnp.float32)[:, None] * inv_freq[None, :]
    return (jnp.cos(angles), jnp.sin(angles))


def rotate(vectors, cos_table, sine_table):
    half_size = vectors.shape[-1] // 2
    front_half = vectors[..., :half_size]
    back_half = vectors[..., half_size:]
    cos_grid = cos_table[:, None, :]
    sin_grid = sine_table[:, None, :]
    return jnp.concatenate(
        [
            front_half * cos_grid - back_half * sin_grid,
            front_half * sin_grid + back_half * cos_grid,
        ],
        axis=-1,
    )


def rotate_back(vectors, cos_table, sine_table):
    half_size = vectors.shape[-1] // 2
    front_half = vectors[..., :half_size]
    back_half = vectors[..., half_size:]
    cos_grid = cos_table[:, None, :]
    sin_grid = sine_table[:, None, :]
    return jnp.concatenate(
        [
            front_half * cos_grid + back_half * sin_grid,
            back_half * cos_grid - front_half * sin_grid,
        ],
        axis=-1,
    )


def gelu_value(hidden):
    return 0.5 * hidden * (1.0 + lax.erf(hidden * root_half))


def gelu_slope(hidden):
    return (
        0.5 * (1.0 + lax.erf(hidden * root_half))
        + hidden * jnp.exp(-0.5 * hidden * hidden) * gauss_norm
    )


def project_qkv(gathered, qkv_weight, qkv_bias, cos_table, sine_table, seq_count, length):
    heads_here = qkv_weight.shape[2] // HEAD
    qkv_pre = (
        jnp.einsum("sd,tde->tse", gathered, qkv_weight, preferred_element_type=jnp.float32)
        + qkv_bias[:, None, :]
    )
    shaped = qkv_pre.reshape(3, seq_count, length, heads_here, HEAD)
    query = rotate(shaped[0], cos_table, sine_table).astype(jnp.bfloat16)
    key_rows = rotate(shaped[1], cos_table, sine_table).astype(jnp.bfloat16)
    values = shaped[2].astype(jnp.bfloat16)
    return (query, key_rows, values)


def block_scores(query, key_rows, block_start, block_rows):
    key_stop = block_start + block_rows
    query_block = query[:, block_start:key_stop]
    key_block = key_rows[:, :key_stop]
    scores = jnp.einsum(
        "bqhd,bkhd->bhqk", query_block, key_block, preferred_element_type=jnp.float32
    ) * (1.0 / math.sqrt(HEAD))
    query_pos = block_start + jnp.arange(block_rows)
    key_pos = jnp.arange(key_stop)
    allowed = key_pos[None, :] <= query_pos[:, None]
    return (jnp.where(allowed[None, None], scores, masked_score), query_block, key_block)


def attend_forward(query, key_rows, values, block_rows):
    length = query.shape[1]
    outputs = []
    totals = []
    for block_start in range(0, length, block_rows):
        key_stop = block_start + block_rows
        scores, query_block, key_block = block_scores(query, key_rows, block_start, block_rows)
        row_max = jnp.max(scores, axis=-1, keepdims=True)
        log_total = row_max + jnp.log(jnp.sum(jnp.exp(scores - row_max), axis=-1, keepdims=True))
        probs_low = jnp.exp(scores - log_total).astype(jnp.bfloat16)
        outputs.append(
            jnp.einsum(
                "bhqk,bkhd->bqhd",
                probs_low,
                values[:, :key_stop],
                preferred_element_type=jnp.float32,
            )
        )
        totals.append(log_total)
    return (jnp.concatenate(outputs, axis=1), totals)


def attend_backward(query, key_rows, values, attn_grad, totals, block_rows):
    length = query.shape[1]
    score_scale = 1.0 / math.sqrt(HEAD)
    keys_grad = jnp.zeros(key_rows.shape, jnp.float32)
    values_grad = jnp.zeros(values.shape, jnp.float32)
    query_grads = []
    for block_number, block_start in enumerate(range(0, length, block_rows)):
        key_stop = block_start + block_rows
        scores, query_block, key_block = block_scores(query, key_rows, block_start, block_rows)
        value_block = values[:, :key_stop]
        grad_block = attn_grad[:, block_start:key_stop]
        probs_full = jnp.exp(scores - totals[block_number])
        probs_low = probs_full.astype(jnp.bfloat16)
        probs_grad = jnp.einsum(
            "bqhd,bkhd->bhqk", grad_block, value_block, preferred_element_type=jnp.float32
        )
        row_dot = jnp.sum(probs_full * probs_grad, axis=-1, keepdims=True)
        scores_grad = (probs_full * (probs_grad - row_dot)).astype(jnp.bfloat16)
        query_grads.append(
            jnp.einsum(
                "bhqk,bkhd->bqhd", scores_grad, key_block, preferred_element_type=jnp.float32
            )
            * score_scale
        )
        pad_rows = ((0, 0), (0, length - key_stop), (0, 0), (0, 0))
        keys_grad = keys_grad + jnp.pad(
            jnp.einsum(
                "bhqk,bqhd->bkhd", scores_grad, query_block, preferred_element_type=jnp.float32
            )
            * score_scale,
            pad_rows,
        )
        values_grad = values_grad + jnp.pad(
            jnp.einsum(
                "bhqk,bqhd->bkhd", probs_low, grad_block, preferred_element_type=jnp.float32
            ),
            pad_rows,
        )
    return (
        jnp.concatenate(query_grads, axis=1),
        keys_grad,
        values_grad,
    )


def swap_cores(block):
    count = lax.axis_size("wide")
    return lax.ppermute(block, "wide", [(index, index ^ 1) for index in range(count)])


def gather_mine(shard, core, split_axis, gather_axis):
    half = shard.shape[split_axis] // 2
    mine = lax.dynamic_slice_in_dim(shard, core * half, half, axis=split_axis)
    return lax.all_gather(mine, "narrow", axis=gather_axis, tiled=True)


def gather_halves(shard, core, split_axis, gather_axis):
    return join_halves(gather_mine(shard, core, split_axis, gather_axis), core, split_axis)


def join_halves(gathered, core, split_axis):
    partner = swap_cores(gathered)
    first = jnp.where(core == 0, gathered, partner)
    second = jnp.where(core == 0, partner, gathered)
    return jnp.concatenate([first, second], axis=split_axis)


def reduce_halves(rows, core, split_axis, scatter_axis):
    half = rows.shape[split_axis] // 2
    mine = lax.dynamic_slice_in_dim(rows, core * half, half, axis=split_axis)
    other = lax.dynamic_slice_in_dim(rows, (1 - core) * half, half, axis=split_axis)
    chip_sum = mine + swap_cores(other.astype(jnp.bfloat16)).astype(jnp.float32)
    part = lax.psum_scatter(
        chip_sum.astype(jnp.bfloat16), "narrow", scatter_dimension=scatter_axis, tiled=True
    )
    empty = jnp.zeros_like(part)
    return jnp.stack(
        [jnp.where(core == 0, part, empty), jnp.where(core == 0, empty, part)], axis=split_axis
    )


def reduce_column_halves(mats, core):
    count = lax.axis_size("narrow")
    pieces = []
    for rows in mats:
        half = rows.shape[1] // 2
        mine = lax.dynamic_slice_in_dim(rows, core * half, half, axis=1)
        other = lax.dynamic_slice_in_dim(rows, (1 - core) * half, half, axis=1)
        chip_sum = mine + swap_cores(other.astype(jnp.bfloat16)).astype(jnp.float32)
        pieces.append(chip_sum.astype(jnp.bfloat16).reshape(count, -1, half))
    joined = lax.psum_scatter(
        jnp.concatenate(pieces, axis=1), "narrow", scatter_dimension=0, tiled=True
    )[0]
    results = []
    start = 0
    for piece in pieces:
        part = joined[start : start + piece.shape[1]]
        start += piece.shape[1]
        empty = jnp.zeros_like(part)
        results.append(
            jnp.stack([jnp.where(core == 0, part, empty), jnp.where(core == 0, empty, part)], axis=1)
        )
    return results


def merge_slots(slots, split_axis):
    shape = list(slots.shape)
    shape[split_axis : split_axis + 2] = [shape[split_axis] * shape[split_axis + 1]]
    return slots.reshape(shape)


def shards(
    tokens,
    cotangent,
    corpus_ids,
    corpus_weights,
    qkv_weight,
    qkv_bias,
    out_weight,
    out_bias,
    up_weight,
    up_bias,
    down_weight,
    down_bias,
    norm_gains,
    norm_biases,
):
    shard_rows = tokens.shape[0]
    group_rows = shard_rows * lax.axis_size("narrow")
    seq_count = corpus_ids.shape[0]
    length = group_rows // seq_count
    block_rows = min(512, length)
    inner = qkv_weight.shape[2]
    first_row = lax.axis_index("narrow") * shard_rows
    cos_table, sine_table = rotary_tables(length, HEAD)
    layer_in = tokens.astype(jnp.float32)
    normed_first, inverse_first = norm_stats(layer_in)
    low_first = (normed_first * norm_gains[0] + norm_biases[0]).astype(jnp.bfloat16)
    core = lax.axis_index("wide") % 2
    model = layer_in.shape[1]
    heads_here = inner // HEAD
    bias_flat = jnp.concatenate([qkv_bias.reshape(-1), up_bias])
    bias_full = lax.all_gather(bias_flat, "narrow", axis=0)
    gathered_first = lax.all_gather(low_first, "narrow", axis=0, tiled=True)
    gathered_first, up_weight, down_weight, bias_full = lax.optimization_barrier(
        (gathered_first, up_weight, down_weight, bias_full)
    )
    up_bias_full = bias_full[:, 3 * inner :].reshape(-1)
    query, key_rows, values = project_qkv(
        gathered_first, qkv_weight, qkv_bias, cos_table, sine_table, seq_count, length
    )
    attn_heads, totals = attend_forward(query, key_rows, values, block_rows)
    attn_low = attn_heads.reshape(group_rows, inner).astype(jnp.bfloat16)
    attn_rows = lax.all_to_all(attn_low, "narrow", 0, 1, tiled=True)
    out_full = lax.all_gather(out_weight, "narrow", axis=0, tiled=True)
    pre_attn = jnp.dot(attn_rows, out_full, preferred_element_type=jnp.float32) + out_bias
    normed_second, inverse_second = norm_stats(pre_attn)
    residual = layer_in + normed_second * norm_gains[1] + norm_biases[1]
    normed_third, inverse_third = norm_stats(residual)
    low_third = (normed_third * norm_gains[2] + norm_biases[2]).astype(jnp.bfloat16)
    up_full = gather_halves(up_weight, core, 0, 1)
    down_full = gather_halves(down_weight, core, 1, 0)
    hidden = jnp.dot(low_third, up_full, preferred_element_type=jnp.float32) + up_bias_full
    act_low = gelu_value(hidden).astype(jnp.bfloat16)
    act_low, qkv_late = lax.optimization_barrier((act_low, qkv_weight))
    qkv_full = join_halves(gather_mine(qkv_late, core, 1, 2), core, 1)
    pre_mlp = jnp.dot(act_low, down_full, preferred_element_type=jnp.float32) + down_bias
    normed_fourth, inverse_fourth = norm_stats(pre_mlp)
    final_sum = residual + normed_fourth * norm_gains[3] + norm_biases[3]
    layer_out = final_sum.astype(jnp.bfloat16)
    row_sequence = (first_row + jnp.arange(shard_rows, dtype=jnp.int32)) // length
    row_corpus = jnp.sum(
        jnp.where(
            row_sequence[:, None] == jnp.arange(seq_count, dtype=jnp.int32)[None, :],
            corpus_ids[None, :],
            0,
        ),
        axis=1,
    )
    row_weight = jnp.sum(
        jnp.where(
            row_corpus[:, None] == jnp.arange(corpus_weights.shape[0], dtype=jnp.int32)[None, :],
            corpus_weights[None, :],
            0.0,
        ),
        axis=1,
    )
    upstream = cotangent.astype(jnp.float32) * row_weight[:, None]
    mlp_grad = norm_back(normed_fourth, inverse_fourth, norm_gains[3], upstream).astype(
        jnp.bfloat16
    )
    down_wgrad_rows = lax.dot_general(
        act_low, mlp_grad, (((0,), (0,)), ((), ())), preferred_element_type=jnp.float32
    )
    act_grad = lax.dot_general(
        mlp_grad, down_full, (((1,), (1,)), ((), ())), preferred_element_type=jnp.float32
    )
    hidden_grad = (act_grad * gelu_slope(hidden)).astype(jnp.bfloat16)
    up_bgrad_rows = jnp.sum(hidden_grad.astype(jnp.float32), axis=0)
    up_wgrad_rows = lax.dot_general(
        low_third, hidden_grad, (((0,), (0,)), ((), ())), preferred_element_type=jnp.float32
    )
    third_grad = lax.dot_general(
        hidden_grad, up_full, (((1,), (1,)), ((), ())), preferred_element_type=jnp.float32
    )
    up_slots = reduce_halves(up_wgrad_rows, core, 0, 1)
    residual_grad = upstream + norm_back(normed_third, inverse_third, norm_gains[2], third_grad)
    branch_grad = norm_back(normed_second, inverse_second, norm_gains[1], residual_grad).astype(
        jnp.bfloat16
    )
    attn_grad_rows = lax.dot_general(
        branch_grad, out_full, (((1,), (1,)), ((), ())), preferred_element_type=jnp.float32
    ).astype(jnp.bfloat16)
    attn_grad = lax.all_to_all(attn_grad_rows, "narrow", 1, 0, tiled=True)
    attn_grad = attn_grad.reshape(query.shape)
    query_grad, keys_grad, values_grad = attend_backward(
        query, key_rows, values, attn_grad, totals, block_rows
    )
    out_wgrad_rows = lax.dot_general(
        attn_rows, branch_grad, (((0,), (0,)), ((), ())), preferred_element_type=jnp.float32
    )
    down_slots, out_slots = reduce_column_halves((down_wgrad_rows, out_wgrad_rows), core)
    qkv_grad = jnp.stack(
        [
            rotate_back(query_grad, cos_table, sine_table),
            rotate_back(keys_grad, cos_table, sine_table),
            values_grad,
        ]
    )
    qkv_grad = qkv_grad.reshape(3, group_rows, inner).astype(jnp.bfloat16)
    qkv_bgrad = jnp.sum(qkv_grad.astype(jnp.float32), axis=1)
    qkv_grad_rows = lax.all_to_all(qkv_grad, "narrow", 1, 2, tiled=True)
    qkv_wgrad = jnp.einsum(
        "sd,tse->tde", gathered_first, qkv_grad, preferred_element_type=jnp.float32
    )
    first_grad = jnp.einsum(
        "tse,tde->sd", qkv_grad_rows, qkv_full, preferred_element_type=jnp.float32
    )
    input_grad = (
        residual_grad + norm_back(normed_first, inverse_first, norm_gains[0], first_grad)
    ).astype(jnp.bfloat16)
    gain_local = jnp.stack(
        [
            jnp.sum(first_grad * normed_first, axis=0),
            jnp.sum(residual_grad * normed_second, axis=0),
            jnp.sum(third_grad * normed_third, axis=0),
            jnp.sum(upstream * normed_fourth, axis=0),
        ]
    )
    bias_local = jnp.stack(
        [
            jnp.sum(first_grad, axis=0),
            jnp.sum(residual_grad, axis=0),
            jnp.sum(third_grad, axis=0),
            jnp.sum(upstream, axis=0),
        ]
    )
    out_blocal = jnp.sum(branch_grad.astype(jnp.float32), axis=0)
    down_blocal = jnp.sum(mlp_grad.astype(jnp.float32), axis=0)
    weight_sums = (
        lax.psum(qkv_wgrad.astype(jnp.bfloat16), "wide").astype(jnp.float32),
        lax.psum(qkv_bgrad.astype(jnp.bfloat16), "wide").astype(jnp.float32),
        lax.psum(out_slots, "wide").astype(jnp.float32),
        lax.psum(up_slots, "wide").astype(jnp.float32),
        None,
        lax.psum(down_slots, "wide").astype(jnp.float32),
    )
    small_sums = lax.psum(
        (gain_local, bias_local, out_blocal, down_blocal, up_bgrad_rows), ("wide", "narrow")
    )
    units = up_bias.shape[0]
    up_bgrad = lax.dynamic_slice_in_dim(small_sums[4], lax.axis_index("narrow") * units, units)
    up_wgrad = merge_slots(weight_sums[3], 0)
    down_wgrad = merge_slots(weight_sums[5], 1)
    out_wgrad = merge_slots(weight_sums[2], 1)
    qkv_wgrad = weight_sums[0]
    return (
        layer_out,
        input_grad,
        qkv_wgrad,
        weight_sums[1],
        out_wgrad,
        small_sums[2],
        up_wgrad,
        up_bgrad,
        down_wgrad,
        small_sums[3],
        small_sums[0],
        small_sums[1],
    )


def solution(mesh):
    return jax.shard_map(
        shards,
        mesh=mesh,
        in_specs=(
            P(("wide", "narrow"), None),
            P(("wide", "narrow"), None),
            P("wide"),
            P(),
            P(None, None, "narrow"),
            P(None, "narrow"),
            P("narrow", None),
            P(),
            P(None, "narrow"),
            P("narrow"),
            P("narrow", None),
            P(),
            P(),
            P(),
        ),
        out_specs=(
            P(("wide", "narrow"), None),
            P(("wide", "narrow"), None),
            P(None, None, "narrow"),
            P(None, "narrow"),
            P("narrow", None),
            P(),
            P(None, "narrow"),
            P("narrow"),
            P("narrow", None),
            P(),
            P(),
            P(),
        ),
        check_vma=False,
    )
```

```python
import math

import jax
import jax.numpy as jnp
from jax import lax
from jax.sharding import PartitionSpec as P

HEAD = 64


epsilon = 1e-05
root_half = 0.7071067811865476
gauss_norm = 0.3989422804014327
masked_score = -1e30


def norm_stats(vec_in):
    center = vec_in - jnp.mean(vec_in, axis=-1, keepdims=True)
    inverse = lax.rsqrt(jnp.mean(center * center, axis=-1, keepdims=True) + epsilon)
    return (center * inverse, inverse)


def norm_back(normed, inverse, gain_row, upstream):
    scaled = upstream * gain_row
    return inverse * (
        scaled
        - jnp.mean(scaled, axis=-1, keepdims=True)
        - normed * jnp.mean(scaled * normed, axis=-1, keepdims=True)
    )


def rotary_tables(length, head_size):
    half_size = head_size // 2
    inv_freq = jnp.exp(jnp.arange(half_size, dtype=jnp.float32) * (-math.log(10000.0) / half_size))
    angles = jnp.arange(length, dtype=jnp.float32)[:, None] * inv_freq[None, :]
    return (jnp.cos(angles), jnp.sin(angles))


def rotate(vectors, cos_table, sine_table):
    half_size = vectors.shape[-1] // 2
    front_half = vectors[..., :half_size]
    back_half = vectors[..., half_size:]
    cos_grid = cos_table[:, None, :]
    sin_grid = sine_table[:, None, :]
    return jnp.concatenate(
        [
            front_half * cos_grid - back_half * sin_grid,
            front_half * sin_grid + back_half * cos_grid,
        ],
        axis=-1,
    )


def rotate_back(vectors, cos_table, sine_table):
    half_size = vectors.shape[-1] // 2
    front_half = vectors[..., :half_size]
    back_half = vectors[..., half_size:]
    cos_grid = cos_table[:, None, :]
    sin_grid = sine_table[:, None, :]
    return jnp.concatenate(
        [
            front_half * cos_grid + back_half * sin_grid,
            back_half * cos_grid - front_half * sin_grid,
        ],
        axis=-1,
    )


def gelu_value(hidden):
    return 0.5 * hidden * (1.0 + lax.erf(hidden * root_half))


def gelu_slope(hidden):
    return (
        0.5 * (1.0 + lax.erf(hidden * root_half))
        + hidden * jnp.exp(-0.5 * hidden * hidden) * gauss_norm
    )


def project_qkv(gathered, qkv_weight, qkv_bias, cos_table, sine_table, seq_count, length):
    heads_here = qkv_weight.shape[2] // HEAD
    qkv_pre = (
        jnp.einsum("sd,tde->tse", gathered, qkv_weight, preferred_element_type=jnp.float32)
        + qkv_bias[:, None, :]
    )
    shaped = qkv_pre.reshape(3, seq_count, length, heads_here, HEAD)
    query = rotate(shaped[0], cos_table, sine_table).astype(jnp.bfloat16)
    key_rows = rotate(shaped[1], cos_table, sine_table).astype(jnp.bfloat16)
    values = shaped[2].astype(jnp.bfloat16)
    return (query, key_rows, values)


def block_scores(query, key_rows, block_start, block_rows):
    key_stop = block_start + block_rows
    query_block = query[:, block_start:key_stop]
    key_block = key_rows[:, :key_stop]
    scores = jnp.einsum(
        "bqhd,bkhd->bhqk", query_block, key_block, preferred_element_type=jnp.float32
    ) * (1.0 / math.sqrt(HEAD))
    query_pos = block_start + jnp.arange(block_rows)
    key_pos = jnp.arange(key_stop)
    allowed = key_pos[None, :] <= query_pos[:, None]
    return (jnp.where(allowed[None, None], scores, masked_score), query_block, key_block)


def attend_forward(query, key_rows, values, block_rows):
    length = query.shape[1]
    outputs = []
    totals = []
    for block_start in range(0, length, block_rows):
        key_stop = block_start + block_rows
        scores, query_block, key_block = block_scores(query, key_rows, block_start, block_rows)
        row_max = jnp.max(scores, axis=-1, keepdims=True)
        log_total = row_max + jnp.log(jnp.sum(jnp.exp(scores - row_max), axis=-1, keepdims=True))
        probs_low = jnp.exp(scores - log_total).astype(jnp.bfloat16)
        outputs.append(
            jnp.einsum(
                "bhqk,bkhd->bqhd",
                probs_low,
                values[:, :key_stop],
                preferred_element_type=jnp.float32,
            )
        )
        totals.append(log_total)
    return (jnp.concatenate(outputs, axis=1), totals)


def attend_backward(query, key_rows, values, attn_grad, totals, block_rows):
    length = query.shape[1]
    score_scale = 1.0 / math.sqrt(HEAD)
    keys_grad = jnp.zeros(key_rows.shape, jnp.float32)
    values_grad = jnp.zeros(values.shape, jnp.float32)
    query_grads = []
    for block_number, block_start in enumerate(range(0, length, block_rows)):
        key_stop = block_start + block_rows
        scores, query_block, key_block = block_scores(query, key_rows, block_start, block_rows)
        value_block = values[:, :key_stop]
        grad_block = attn_grad[:, block_start:key_stop]
        probs_full = jnp.exp(scores - totals[block_number])
        probs_low = probs_full.astype(jnp.bfloat16)
        probs_grad = jnp.einsum(
            "bqhd,bkhd->bhqk", grad_block, value_block, preferred_element_type=jnp.float32
        )
        row_dot = jnp.sum(probs_full * probs_grad, axis=-1, keepdims=True)
        scores_grad = (probs_full * (probs_grad - row_dot)).astype(jnp.bfloat16)
        query_grads.append(
            jnp.einsum(
                "bhqk,bkhd->bqhd", scores_grad, key_block, preferred_element_type=jnp.float32
            )
            * score_scale
        )
        pad_rows = ((0, 0), (0, length - key_stop), (0, 0), (0, 0))
        keys_grad = keys_grad + jnp.pad(
            jnp.einsum(
                "bhqk,bqhd->bkhd", scores_grad, query_block, preferred_element_type=jnp.float32
            )
            * score_scale,
            pad_rows,
        )
        values_grad = values_grad + jnp.pad(
            jnp.einsum(
                "bhqk,bqhd->bkhd", probs_low, grad_block, preferred_element_type=jnp.float32
            ),
            pad_rows,
        )
    return (
        jnp.concatenate(query_grads, axis=1),
        keys_grad,
        values_grad,
    )


def swap_cores(block):
    count = lax.axis_size("wide")
    return lax.ppermute(block, "wide", [(index, index ^ 1) for index in range(count)])


def gather_mine(shard, core, split_axis, gather_axis):
    half = shard.shape[split_axis] // 2
    mine = lax.dynamic_slice_in_dim(shard, core * half, half, axis=split_axis)
    return lax.all_gather(mine, "narrow", axis=gather_axis, tiled=True)


def gather_halves(shard, core, split_axis, gather_axis):
    return join_halves(gather_mine(shard, core, split_axis, gather_axis), core, split_axis)


def join_halves(gathered, core, split_axis):
    partner = swap_cores(gathered)
    first = jnp.where(core == 0, gathered, partner)
    second = jnp.where(core == 0, partner, gathered)
    return jnp.concatenate([first, second], axis=split_axis)


def reduce_halves(rows, core, split_axis, scatter_axis):
    half = rows.shape[split_axis] // 2
    mine = lax.dynamic_slice_in_dim(rows, core * half, half, axis=split_axis)
    other = lax.dynamic_slice_in_dim(rows, (1 - core) * half, half, axis=split_axis)
    chip_sum = mine + swap_cores(other.astype(jnp.bfloat16)).astype(jnp.float32)
    part = lax.psum_scatter(
        chip_sum.astype(jnp.bfloat16), "narrow", scatter_dimension=scatter_axis, tiled=True
    )
    empty = jnp.zeros_like(part)
    return jnp.stack(
        [jnp.where(core == 0, part, empty), jnp.where(core == 0, empty, part)], axis=split_axis
    )


def reduce_column_halves(mats, core):
    count = lax.axis_size("narrow")
    pieces = []
    for rows in mats:
        half = rows.shape[1] // 2
        mine = lax.dynamic_slice_in_dim(rows, core * half, half, axis=1)
        other = lax.dynamic_slice_in_dim(rows, (1 - core) * half, half, axis=1)
        chip_sum = mine + swap_cores(other.astype(jnp.bfloat16)).astype(jnp.float32)
        pieces.append(chip_sum.astype(jnp.bfloat16).reshape(count, -1, half))
    joined = lax.psum_scatter(
        jnp.concatenate(pieces, axis=1), "narrow", scatter_dimension=0, tiled=True
    )[0]
    results = []
    start = 0
    for piece in pieces:
        part = joined[start : start + piece.shape[1]]
        start += piece.shape[1]
        empty = jnp.zeros_like(part)
        results.append(
            jnp.stack([jnp.where(core == 0, part, empty), jnp.where(core == 0, empty, part)], axis=1)
        )
    return results


def merge_slots(slots, split_axis):
    shape = list(slots.shape)
    shape[split_axis : split_axis + 2] = [shape[split_axis] * shape[split_axis + 1]]
    return slots.reshape(shape)


def shards(
    tokens,
    cotangent,
    corpus_ids,
    corpus_weights,
    qkv_weight,
    qkv_bias,
    out_weight,
    out_bias,
    up_weight,
    up_bias,
    down_weight,
    down_bias,
    norm_gains,
    norm_biases,
):
    shard_rows = tokens.shape[0]
    group_rows = shard_rows * lax.axis_size("narrow")
    seq_count = corpus_ids.shape[0]
    length = group_rows // seq_count
    block_rows = min(512, length)
    inner = qkv_weight.shape[2]
    first_row = lax.axis_index("narrow") * shard_rows
    cos_table, sine_table = rotary_tables(length, HEAD)
    layer_in = tokens.astype(jnp.float32)
    normed_first, inverse_first = norm_stats(layer_in)
    low_first = (normed_first * norm_gains[0] + norm_biases[0]).astype(jnp.bfloat16)
    core = lax.axis_index("wide") % 2
    model = layer_in.shape[1]
    heads_here = inner // HEAD
    bias_flat = jnp.concatenate([qkv_bias.reshape(-1), up_bias])
    bias_full = lax.all_gather(bias_flat, "narrow", axis=0)
    gathered_first = lax.all_gather(low_first, "narrow", axis=0, tiled=True)
    gathered_first, up_weight, down_weight, out_weight, bias_full = lax.optimization_barrier(
        (gathered_first, up_weight, down_weight, out_weight, bias_full)
    )
    up_bias_full = bias_full[:, 3 * inner :].reshape(-1)
    query, key_rows, values = project_qkv(
        gathered_first, qkv_weight, qkv_bias, cos_table, sine_table, seq_count, length
    )
    attn_heads, totals = attend_forward(query, key_rows, values, block_rows)
    attn_low = attn_heads.reshape(group_rows, inner).astype(jnp.bfloat16)
    attn_rows = lax.all_to_all(attn_low, "narrow", 0, 1, tiled=True)
    out_full = join_halves(gather_mine(out_weight, core, 1, 0), core, 1)
    pre_attn = jnp.dot(attn_rows, out_full, preferred_element_type=jnp.float32) + out_bias
    normed_second, inverse_second = norm_stats(pre_attn)
    residual = layer_in + normed_second * norm_gains[1] + norm_biases[1]
    normed_third, inverse_third = norm_stats(residual)
    low_third = (normed_third * norm_gains[2] + norm_biases[2]).astype(jnp.bfloat16)
    up_full = gather_halves(up_weight, core, 0, 1)
    down_full = gather_halves(down_weight, core, 1, 0)
    hidden = jnp.dot(low_third, up_full, preferred_element_type=jnp.float32) + up_bias_full
    act_low = gelu_value(hidden).astype(jnp.bfloat16)
    act_low, qkv_late = lax.optimization_barrier((act_low, qkv_weight))
    qkv_full = join_halves(gather_mine(qkv_late, core, 1, 2), core, 1)
    pre_mlp = jnp.dot(act_low, down_full, preferred_element_type=jnp.float32) + down_bias
    normed_fourth, inverse_fourth = norm_stats(pre_mlp)
    final_sum = residual + normed_fourth * norm_gains[3] + norm_biases[3]
    layer_out = final_sum.astype(jnp.bfloat16)
    row_sequence = (first_row + jnp.arange(shard_rows, dtype=jnp.int32)) // length
    row_corpus = jnp.sum(
        jnp.where(
            row_sequence[:, None] == jnp.arange(seq_count, dtype=jnp.int32)[None, :],
            corpus_ids[None, :],
            0,
        ),
        axis=1,
    )
    row_weight = jnp.sum(
        jnp.where(
            row_corpus[:, None] == jnp.arange(corpus_weights.shape[0], dtype=jnp.int32)[None, :],
            corpus_weights[None, :],
            0.0,
        ),
        axis=1,
    )
    upstream = cotangent.astype(jnp.float32) * row_weight[:, None]
    mlp_grad = norm_back(normed_fourth, inverse_fourth, norm_gains[3], upstream).astype(
        jnp.bfloat16
    )
    down_wgrad_rows = lax.dot_general(
        act_low, mlp_grad, (((0,), (0,)), ((), ())), preferred_element_type=jnp.float32
    )
    act_grad = lax.dot_general(
        mlp_grad, down_full, (((1,), (1,)), ((), ())), preferred_element_type=jnp.float32
    )
    hidden_grad = (act_grad * gelu_slope(hidden)).astype(jnp.bfloat16)
    up_bgrad_rows = jnp.sum(hidden_grad.astype(jnp.float32), axis=0)
    up_wgrad_rows = lax.dot_general(
        low_third, hidden_grad, (((0,), (0,)), ((), ())), preferred_element_type=jnp.float32
    )
    third_grad = lax.dot_general(
        hidden_grad, up_full, (((1,), (1,)), ((), ())), preferred_element_type=jnp.float32
    )
    up_slots = reduce_halves(up_wgrad_rows, core, 0, 1)
    residual_grad = upstream + norm_back(normed_third, inverse_third, norm_gains[2], third_grad)
    branch_grad = norm_back(normed_second, inverse_second, norm_gains[1], residual_grad).astype(
        jnp.bfloat16
    )
    attn_grad_rows = lax.dot_general(
        branch_grad, out_full, (((1,), (1,)), ((), ())), preferred_element_type=jnp.float32
    ).astype(jnp.bfloat16)
    attn_grad = lax.all_to_all(attn_grad_rows, "narrow", 1, 0, tiled=True)
    attn_grad = attn_grad.reshape(query.shape)
    query_grad, keys_grad, values_grad = attend_backward(
        query, key_rows, values, attn_grad, totals, block_rows
    )
    out_wgrad_rows = lax.dot_general(
        attn_rows, branch_grad, (((0,), (0,)), ((), ())), preferred_element_type=jnp.float32
    )
    down_slots, out_slots = reduce_column_halves((down_wgrad_rows, out_wgrad_rows), core)
    qkv_grad = jnp.stack(
        [
            rotate_back(query_grad, cos_table, sine_table),
            rotate_back(keys_grad, cos_table, sine_table),
            values_grad,
        ]
    )
    qkv_grad = qkv_grad.reshape(3, group_rows, inner).astype(jnp.bfloat16)
    qkv_bgrad = jnp.sum(qkv_grad.astype(jnp.float32), axis=1)
    qkv_grad_rows = lax.all_to_all(
        qkv_grad.reshape(3, group_rows, heads_here, HEAD), "narrow", 1, 2, tiled=True
    ).reshape(3, shard_rows, model)
    qkv_wgrad = jnp.einsum(
        "sd,tse->tde", gathered_first, qkv_grad, preferred_element_type=jnp.float32
    )
    first_grad = jnp.einsum(
        "tse,tde->sd", qkv_grad_rows, qkv_full, preferred_element_type=jnp.float32
    )
    input_grad = (
        residual_grad + norm_back(normed_first, inverse_first, norm_gains[0], first_grad)
    ).astype(jnp.bfloat16)
    gain_local = jnp.stack(
        [
            jnp.sum(first_grad * normed_first, axis=0),
            jnp.sum(residual_grad * normed_second, axis=0),
            jnp.sum(third_grad * normed_third, axis=0),
            jnp.sum(upstream * normed_fourth, axis=0),
        ]
    )
    bias_local = jnp.stack(
        [
            jnp.sum(first_grad, axis=0),
            jnp.sum(residual_grad, axis=0),
            jnp.sum(third_grad, axis=0),
            jnp.sum(upstream, axis=0),
        ]
    )
    out_blocal = jnp.sum(branch_grad.astype(jnp.float32), axis=0)
    down_blocal = jnp.sum(mlp_grad.astype(jnp.float32), axis=0)
    weight_sums = (
        lax.psum(qkv_wgrad.astype(jnp.bfloat16), "wide").astype(jnp.float32),
        lax.psum(qkv_bgrad.astype(jnp.bfloat16), "wide").astype(jnp.float32),
        lax.psum(out_slots, "wide").astype(jnp.float32),
        lax.psum(up_slots, "wide").astype(jnp.float32),
        None,
        lax.psum(down_slots, "wide").astype(jnp.float32),
    )
    small_sums = lax.psum(
        (gain_local, bias_local, out_blocal, down_blocal, up_bgrad_rows), ("wide", "narrow")
    )
    units = up_bias.shape[0]
    up_bgrad = lax.dynamic_slice_in_dim(small_sums[4], lax.axis_index("narrow") * units, units)
    up_wgrad = merge_slots(weight_sums[3], 0)
    down_wgrad = merge_slots(weight_sums[5], 1)
    out_wgrad = merge_slots(weight_sums[2], 1)
    qkv_wgrad = weight_sums[0]
    return (
        layer_out,
        input_grad,
        qkv_wgrad,
        weight_sums[1],
        out_wgrad,
        small_sums[2],
        up_wgrad,
        up_bgrad,
        down_wgrad,
        small_sums[3],
        small_sums[0],
        small_sums[1],
    )


def solution(mesh):
    return jax.shard_map(
        shards,
        mesh=mesh,
        in_specs=(
            P(("wide", "narrow"), None),
            P(("wide", "narrow"), None),
            P("wide"),
            P(),
            P(None, None, "narrow"),
            P(None, "narrow"),
            P("narrow", None),
            P(),
            P(None, "narrow"),
            P("narrow"),
            P("narrow", None),
            P(),
            P(),
            P(),
        ),
        out_specs=(
            P(("wide", "narrow"), None),
            P(("wide", "narrow"), None),
            P(None, None, "narrow"),
            P(None, "narrow"),
            P("narrow", None),
            P(),
            P(None, "narrow"),
            P("narrow"),
            P("narrow", None),
            P(),
            P(),
            P(),
        ),
        check_vma=False,
    )
```

```python
import math

import jax
import jax.numpy as jnp
from jax import lax
from jax.sharding import PartitionSpec as P

HEAD = 64


epsilon = 1e-05
root_half = 0.7071067811865476
gauss_norm = 0.3989422804014327
masked_score = -1e30


def norm_stats(vec_in):
    center = vec_in - jnp.mean(vec_in, axis=-1, keepdims=True)
    inverse = lax.rsqrt(jnp.mean(center * center, axis=-1, keepdims=True) + epsilon)
    return (center * inverse, inverse)


def norm_back(normed, inverse, gain_row, upstream):
    scaled = upstream * gain_row
    return inverse * (
        scaled
        - jnp.mean(scaled, axis=-1, keepdims=True)
        - normed * jnp.mean(scaled * normed, axis=-1, keepdims=True)
    )


def rotary_tables(length, head_size):
    half_size = head_size // 2
    inv_freq = jnp.exp(jnp.arange(half_size, dtype=jnp.float32) * (-math.log(10000.0) / half_size))
    angles = jnp.arange(length, dtype=jnp.float32)[:, None] * inv_freq[None, :]
    return (jnp.cos(angles), jnp.sin(angles))


def rotate(vectors, cos_table, sine_table):
    half_size = vectors.shape[-1] // 2
    front_half = vectors[..., :half_size]
    back_half = vectors[..., half_size:]
    cos_grid = cos_table[:, None, :]
    sin_grid = sine_table[:, None, :]
    return jnp.concatenate(
        [
            front_half * cos_grid - back_half * sin_grid,
            front_half * sin_grid + back_half * cos_grid,
        ],
        axis=-1,
    )


def rotate_back(vectors, cos_table, sine_table):
    half_size = vectors.shape[-1] // 2
    front_half = vectors[..., :half_size]
    back_half = vectors[..., half_size:]
    cos_grid = cos_table[:, None, :]
    sin_grid = sine_table[:, None, :]
    return jnp.concatenate(
        [
            front_half * cos_grid + back_half * sin_grid,
            back_half * cos_grid - front_half * sin_grid,
        ],
        axis=-1,
    )


def gelu_value(hidden):
    return 0.5 * hidden * (1.0 + lax.erf(hidden * root_half))


def gelu_slope(hidden):
    return (
        0.5 * (1.0 + lax.erf(hidden * root_half))
        + hidden * jnp.exp(-0.5 * hidden * hidden) * gauss_norm
    )


def project_qkv(gathered, qkv_weight, qkv_bias, cos_table, sine_table, seq_count, length):
    heads_here = qkv_weight.shape[2] // HEAD
    qkv_pre = (
        jnp.einsum("sd,tde->tse", gathered, qkv_weight, preferred_element_type=jnp.float32)
        + qkv_bias[:, None, :]
    )
    shaped = qkv_pre.reshape(3, seq_count, length, heads_here, HEAD)
    query = rotate(shaped[0], cos_table, sine_table).astype(jnp.bfloat16)
    key_rows = rotate(shaped[1], cos_table, sine_table).astype(jnp.bfloat16)
    values = shaped[2].astype(jnp.bfloat16)
    return (query, key_rows, values)


def block_scores(query, key_rows, block_start, block_rows):
    key_stop = block_start + block_rows
    query_block = query[:, block_start:key_stop]
    key_block = key_rows[:, :key_stop]
    scores = jnp.einsum(
        "bqhd,bkhd->bhqk", query_block, key_block, preferred_element_type=jnp.float32
    ) * (1.0 / math.sqrt(HEAD))
    query_pos = block_start + jnp.arange(block_rows)
    key_pos = jnp.arange(key_stop)
    allowed = key_pos[None, :] <= query_pos[:, None]
    return (jnp.where(allowed[None, None], scores, masked_score), query_block, key_block)


def attend_forward(query, key_rows, values, block_rows):
    length = query.shape[1]
    outputs = []
    totals = []
    for block_start in range(0, length, block_rows):
        key_stop = block_start + block_rows
        scores, query_block, key_block = block_scores(query, key_rows, block_start, block_rows)
        row_max = jnp.max(scores, axis=-1, keepdims=True)
        log_total = row_max + jnp.log(jnp.sum(jnp.exp(scores - row_max), axis=-1, keepdims=True))
        probs_low = jnp.exp(scores - log_total).astype(jnp.bfloat16)
        outputs.append(
            jnp.einsum(
                "bhqk,bkhd->bqhd",
                probs_low,
                values[:, :key_stop],
                preferred_element_type=jnp.float32,
            )
        )
        totals.append(log_total)
    return (jnp.concatenate(outputs, axis=1), totals)


def attend_backward(query, key_rows, values, attn_grad, totals, block_rows):
    length = query.shape[1]
    score_scale = 1.0 / math.sqrt(HEAD)
    keys_grad = jnp.zeros(key_rows.shape, jnp.float32)
    values_grad = jnp.zeros(values.shape, jnp.float32)
    query_grads = []
    for block_number, block_start in enumerate(range(0, length, block_rows)):
        key_stop = block_start + block_rows
        scores, query_block, key_block = block_scores(query, key_rows, block_start, block_rows)
        value_block = values[:, :key_stop]
        grad_block = attn_grad[:, block_start:key_stop]
        probs_full = jnp.exp(scores - totals[block_number])
        probs_low = probs_full.astype(jnp.bfloat16)
        probs_grad = jnp.einsum(
            "bqhd,bkhd->bhqk", grad_block, value_block, preferred_element_type=jnp.float32
        )
        row_dot = jnp.sum(probs_full * probs_grad, axis=-1, keepdims=True)
        scores_grad = (probs_full * (probs_grad - row_dot)).astype(jnp.bfloat16)
        query_grads.append(
            jnp.einsum(
                "bhqk,bkhd->bqhd", scores_grad, key_block, preferred_element_type=jnp.float32
            )
            * score_scale
        )
        pad_rows = ((0, 0), (0, length - key_stop), (0, 0), (0, 0))
        keys_grad = keys_grad + jnp.pad(
            jnp.einsum(
                "bhqk,bqhd->bkhd", scores_grad, query_block, preferred_element_type=jnp.float32
            )
            * score_scale,
            pad_rows,
        )
        values_grad = values_grad + jnp.pad(
            jnp.einsum(
                "bhqk,bqhd->bkhd", probs_low, grad_block, preferred_element_type=jnp.float32
            ),
            pad_rows,
        )
    return (
        jnp.concatenate(query_grads, axis=1),
        keys_grad,
        values_grad,
    )


def swap_cores(block):
    count = lax.axis_size("wide")
    return lax.ppermute(block, "wide", [(index, index ^ 1) for index in range(count)])


def gather_mine(shard, core, split_axis, gather_axis):
    half = shard.shape[split_axis] // 2
    mine = lax.dynamic_slice_in_dim(shard, core * half, half, axis=split_axis)
    return lax.all_gather(mine, "narrow", axis=gather_axis, tiled=True)


def gather_halves(shard, core, split_axis, gather_axis):
    return join_halves(gather_mine(shard, core, split_axis, gather_axis), core, split_axis)


def join_halves(gathered, core, split_axis):
    partner = swap_cores(gathered)
    first = jnp.where(core == 0, gathered, partner)
    second = jnp.where(core == 0, partner, gathered)
    return jnp.concatenate([first, second], axis=split_axis)


def reduce_halves(rows, core, split_axis, scatter_axis):
    half = rows.shape[split_axis] // 2
    mine = lax.dynamic_slice_in_dim(rows, core * half, half, axis=split_axis)
    other = lax.dynamic_slice_in_dim(rows, (1 - core) * half, half, axis=split_axis)
    chip_sum = mine + swap_cores(other.astype(jnp.bfloat16)).astype(jnp.float32)
    part = lax.psum_scatter(
        chip_sum.astype(jnp.bfloat16), "narrow", scatter_dimension=scatter_axis, tiled=True
    )
    empty = jnp.zeros_like(part)
    return jnp.stack(
        [jnp.where(core == 0, part, empty), jnp.where(core == 0, empty, part)], axis=split_axis
    )


def reduce_column_halves(mats, core):
    count = lax.axis_size("narrow")
    pieces = []
    for rows in mats:
        half = rows.shape[1] // 2
        mine = lax.dynamic_slice_in_dim(rows, core * half, half, axis=1)
        other = lax.dynamic_slice_in_dim(rows, (1 - core) * half, half, axis=1)
        chip_sum = mine + swap_cores(other.astype(jnp.bfloat16)).astype(jnp.float32)
        pieces.append(chip_sum.astype(jnp.bfloat16).reshape(count, -1, half))
    joined = lax.psum_scatter(
        jnp.concatenate(pieces, axis=1), "narrow", scatter_dimension=0, tiled=True
    )[0]
    results = []
    start = 0
    for piece in pieces:
        part = joined[start : start + piece.shape[1]]
        start += piece.shape[1]
        empty = jnp.zeros_like(part)
        results.append(
            jnp.stack([jnp.where(core == 0, part, empty), jnp.where(core == 0, empty, part)], axis=1)
        )
    return results


def merge_slots(slots, split_axis):
    shape = list(slots.shape)
    shape[split_axis : split_axis + 2] = [shape[split_axis] * shape[split_axis + 1]]
    return slots.reshape(shape)


def shards(
    tokens,
    cotangent,
    corpus_ids,
    corpus_weights,
    qkv_weight,
    qkv_bias,
    out_weight,
    out_bias,
    up_weight,
    up_bias,
    down_weight,
    down_bias,
    norm_gains,
    norm_biases,
):
    shard_rows = tokens.shape[0]
    group_rows = shard_rows * lax.axis_size("narrow")
    seq_count = corpus_ids.shape[0]
    length = group_rows // seq_count
    block_rows = min(512, length)
    inner = qkv_weight.shape[2]
    first_row = lax.axis_index("narrow") * shard_rows
    cos_table, sine_table = rotary_tables(length, HEAD)
    layer_in = tokens.astype(jnp.float32)
    normed_first, inverse_first = norm_stats(layer_in)
    low_first = (normed_first * norm_gains[0] + norm_biases[0]).astype(jnp.bfloat16)
    core = lax.axis_index("wide") % 2
    model = layer_in.shape[1]
    heads_here = inner // HEAD
    bias_flat = jnp.concatenate([qkv_bias.reshape(-1), up_bias])
    bias_full = lax.all_gather(bias_flat, "narrow", axis=0)
    gathered_first = lax.all_gather(low_first, "narrow", axis=0, tiled=True)
    gathered_first, up_weight, down_weight, bias_full = lax.optimization_barrier(
        (gathered_first, up_weight, down_weight, bias_full)
    )
    up_bias_full = bias_full[:, 3 * inner :].reshape(-1)
    query, key_rows, values = project_qkv(
        gathered_first, qkv_weight, qkv_bias, cos_table, sine_table, seq_count, length
    )
    attn_heads, totals = attend_forward(query, key_rows, values, block_rows)
    attn_low = attn_heads.reshape(group_rows, inner).astype(jnp.bfloat16)
    attn_rows = lax.all_to_all(attn_low, "narrow", 0, 1, tiled=True)
    out_full = lax.all_gather(out_weight, "narrow", axis=0, tiled=True)
    pre_attn = jnp.dot(attn_rows, out_full, preferred_element_type=jnp.float32) + out_bias
    normed_second, inverse_second = norm_stats(pre_attn)
    residual = layer_in + normed_second * norm_gains[1] + norm_biases[1]
    normed_third, inverse_third = norm_stats(residual)
    low_third = (normed_third * norm_gains[2] + norm_biases[2]).astype(jnp.bfloat16)
    up_full = gather_halves(up_weight, core, 0, 1)
    down_full = gather_halves(down_weight, core, 1, 0)
    hidden = jnp.dot(low_third, up_full, preferred_element_type=jnp.float32) + up_bias_full
    act_low = gelu_value(hidden).astype(jnp.bfloat16)
    act_low, qkv_late = lax.optimization_barrier((act_low, qkv_weight))
    qkv_full = join_halves(gather_mine(qkv_late, core, 1, 2), core, 1)
    pre_mlp = jnp.dot(act_low, down_full, preferred_element_type=jnp.float32) + down_bias
    normed_fourth, inverse_fourth = norm_stats(pre_mlp)
    final_sum = residual + normed_fourth * norm_gains[3] + norm_biases[3]
    layer_out = final_sum.astype(jnp.bfloat16)
    row_sequence = (first_row + jnp.arange(shard_rows, dtype=jnp.int32)) // length
    row_corpus = jnp.sum(
        jnp.where(
            row_sequence[:, None] == jnp.arange(seq_count, dtype=jnp.int32)[None, :],
            corpus_ids[None, :],
            0,
        ),
        axis=1,
    )
    row_weight = jnp.sum(
        jnp.where(
            row_corpus[:, None] == jnp.arange(corpus_weights.shape[0], dtype=jnp.int32)[None, :],
            corpus_weights[None, :],
            0.0,
        ),
        axis=1,
    )
    upstream = cotangent.astype(jnp.float32) * row_weight[:, None]
    mlp_grad = norm_back(normed_fourth, inverse_fourth, norm_gains[3], upstream).astype(
        jnp.bfloat16
    )
    down_wgrad_rows = lax.dot_general(
        act_low, mlp_grad, (((0,), (0,)), ((), ())), preferred_element_type=jnp.float32
    )
    act_grad = lax.dot_general(
        mlp_grad, down_full, (((1,), (1,)), ((), ())), preferred_element_type=jnp.float32
    )
    hidden_grad = (act_grad * gelu_slope(hidden)).astype(jnp.bfloat16)
    up_bgrad_rows = jnp.sum(hidden_grad.astype(jnp.float32), axis=0)
    up_wgrad_rows = lax.dot_general(
        low_third, hidden_grad, (((0,), (0,)), ((), ())), preferred_element_type=jnp.float32
    )
    third_grad = lax.dot_general(
        hidden_grad, up_full, (((1,), (1,)), ((), ())), preferred_element_type=jnp.float32
    )
    up_slots = reduce_halves(up_wgrad_rows, core, 0, 1)
    down_slots = reduce_halves(down_wgrad_rows, core, 1, 0)
    residual_grad = upstream + norm_back(normed_third, inverse_third, norm_gains[2], third_grad)
    branch_grad = norm_back(normed_second, inverse_second, norm_gains[1], residual_grad).astype(
        jnp.bfloat16
    )
    attn_grad_rows = lax.dot_general(
        branch_grad, out_full, (((1,), (1,)), ((), ())), preferred_element_type=jnp.float32
    ).astype(jnp.bfloat16)
    attn_grad = lax.all_to_all(attn_grad_rows, "narrow", 1, 0, tiled=True)
    attn_grad = attn_grad.reshape(query.shape)
    query_grad, keys_grad, values_grad = attend_backward(
        query, key_rows, values, attn_grad, totals, block_rows
    )
    out_wgrad_rows = lax.dot_general(
        attn_rows, branch_grad, (((0,), (0,)), ((), ())), preferred_element_type=jnp.float32
    )
    out_slots = reduce_halves(out_wgrad_rows, core, 1, 0)
    qkv_grad = jnp.stack(
        [
            rotate_back(query_grad, cos_table, sine_table),
            rotate_back(keys_grad, cos_table, sine_table),
            values_grad,
        ]
    )
    qkv_grad = qkv_grad.reshape(3, group_rows, inner).astype(jnp.bfloat16)
    qkv_bgrad = jnp.sum(qkv_grad.astype(jnp.float32), axis=1)
    qkv_grad_rows = lax.all_to_all(
        qkv_grad.reshape(3, group_rows, heads_here, HEAD), "narrow", 1, 2, tiled=True
    ).reshape(3, shard_rows, model)
    qkv_wgrad = jnp.einsum(
        "sd,tse->tde", gathered_first, qkv_grad, preferred_element_type=jnp.float32
    )
    first_grad = jnp.einsum(
        "tse,tde->sd", qkv_grad_rows, qkv_full, preferred_element_type=jnp.float32
    )
    input_grad = (
        residual_grad + norm_back(normed_first, inverse_first, norm_gains[0], first_grad)
    ).astype(jnp.bfloat16)
    gain_local = jnp.stack(
        [
            jnp.sum(first_grad * normed_first, axis=0),
            jnp.sum(residual_grad * normed_second, axis=0),
            jnp.sum(third_grad * normed_third, axis=0),
            jnp.sum(upstream * normed_fourth, axis=0),
        ]
    )
    bias_local = jnp.stack(
        [
            jnp.sum(first_grad, axis=0),
            jnp.sum(residual_grad, axis=0),
            jnp.sum(third_grad, axis=0),
            jnp.sum(upstream, axis=0),
        ]
    )
    out_blocal = jnp.sum(branch_grad.astype(jnp.float32), axis=0)
    down_blocal = jnp.sum(mlp_grad.astype(jnp.float32), axis=0)
    weight_sums = (
        lax.psum(qkv_wgrad.astype(jnp.bfloat16), "wide").astype(jnp.float32),
        lax.psum(qkv_bgrad.astype(jnp.bfloat16), "wide").astype(jnp.float32),
        lax.psum(out_slots, "wide").astype(jnp.float32),
        lax.psum(up_slots, "wide").astype(jnp.float32),
        None,
        lax.psum(down_slots, "wide").astype(jnp.float32),
    )
    small_sums = lax.psum(
        (gain_local, bias_local, out_blocal, down_blocal, up_bgrad_rows), ("wide", "narrow")
    )
    units = up_bias.shape[0]
    up_bgrad = lax.dynamic_slice_in_dim(small_sums[4], lax.axis_index("narrow") * units, units)
    up_wgrad = merge_slots(weight_sums[3], 0)
    down_wgrad = merge_slots(weight_sums[5], 1)
    out_wgrad = merge_slots(weight_sums[2], 1)
    qkv_wgrad = weight_sums[0]
    return (
        layer_out,
        input_grad,
        qkv_wgrad,
        weight_sums[1],
        out_wgrad,
        small_sums[2],
        up_wgrad,
        up_bgrad,
        down_wgrad,
        small_sums[3],
        small_sums[0],
        small_sums[1],
    )


def solution(mesh):
    return jax.shard_map(
        shards,
        mesh=mesh,
        in_specs=(
            P(("wide", "narrow"), None),
            P(("wide", "narrow"), None),
            P("wide"),
            P(),
            P(None, None, "narrow"),
            P(None, "narrow"),
            P("narrow", None),
            P(),
            P(None, "narrow"),
            P("narrow"),
            P("narrow", None),
            P(),
            P(),
            P(),
        ),
        out_specs=(
            P(("wide", "narrow"), None),
            P(("wide", "narrow"), None),
            P(None, None, "narrow"),
            P(None, "narrow"),
            P("narrow", None),
            P(),
            P(None, "narrow"),
            P("narrow"),
            P("narrow", None),
            P(),
            P(),
            P(),
        ),
        check_vma=False,
    )
```

```python
import math

import jax
import jax.numpy as jnp
from jax import lax
from jax.sharding import PartitionSpec as P

HEAD = 64


epsilon = 1e-05
root_half = 0.7071067811865476
gauss_norm = 0.3989422804014327
masked_score = -1e30


def norm_stats(vec_in):
    center = vec_in - jnp.mean(vec_in, axis=-1, keepdims=True)
    inverse = lax.rsqrt(jnp.mean(center * center, axis=-1, keepdims=True) + epsilon)
    return (center * inverse, inverse)


def norm_back(normed, inverse, gain_row, upstream):
    scaled = upstream * gain_row
    return inverse * (
        scaled
        - jnp.mean(scaled, axis=-1, keepdims=True)
        - normed * jnp.mean(scaled * normed, axis=-1, keepdims=True)
    )


def rotary_tables(length, head_size):
    half_size = head_size // 2
    inv_freq = jnp.exp(jnp.arange(half_size, dtype=jnp.float32) * (-math.log(10000.0) / half_size))
    angles = jnp.arange(length, dtype=jnp.float32)[:, None] * inv_freq[None, :]
    return (jnp.cos(angles), jnp.sin(angles))


def rotate(vectors, cos_table, sine_table):
    half_size = vectors.shape[-1] // 2
    front_half = vectors[..., :half_size]
    back_half = vectors[..., half_size:]
    cos_grid = cos_table[:, None, :]
    sin_grid = sine_table[:, None, :]
    return jnp.concatenate(
        [
            front_half * cos_grid - back_half * sin_grid,
            front_half * sin_grid + back_half * cos_grid,
        ],
        axis=-1,
    )


def rotate_back(vectors, cos_table, sine_table):
    half_size = vectors.shape[-1] // 2
    front_half = vectors[..., :half_size]
    back_half = vectors[..., half_size:]
    cos_grid = cos_table[:, None, :]
    sin_grid = sine_table[:, None, :]
    return jnp.concatenate(
        [
            front_half * cos_grid + back_half * sin_grid,
            back_half * cos_grid - front_half * sin_grid,
        ],
        axis=-1,
    )


def gelu_value(hidden):
    return 0.5 * hidden * (1.0 + lax.erf(hidden * root_half))


def gelu_slope(hidden):
    return (
        0.5 * (1.0 + lax.erf(hidden * root_half))
        + hidden * jnp.exp(-0.5 * hidden * hidden) * gauss_norm
    )


def project_qkv(gathered, qkv_weight, qkv_bias, cos_table, sine_table, seq_count, length):
    heads_here = qkv_weight.shape[2] // HEAD
    qkv_pre = (
        jnp.einsum("sd,tde->tse", gathered, qkv_weight, preferred_element_type=jnp.float32)
        + qkv_bias[:, None, :]
    )
    shaped = qkv_pre.reshape(3, seq_count, length, heads_here, HEAD)
    query = rotate(shaped[0], cos_table, sine_table).astype(jnp.bfloat16)
    key_rows = rotate(shaped[1], cos_table, sine_table).astype(jnp.bfloat16)
    values = shaped[2].astype(jnp.bfloat16)
    return (query, key_rows, values)


def block_scores(query, key_rows, block_start, block_rows):
    key_stop = block_start + block_rows
    query_block = query[:, block_start:key_stop]
    key_block = key_rows[:, :key_stop]
    scores = jnp.einsum(
        "bqhd,bkhd->bhqk", query_block, key_block, preferred_element_type=jnp.float32
    ) * (1.0 / math.sqrt(HEAD))
    query_pos = block_start + jnp.arange(block_rows)
    key_pos = jnp.arange(key_stop)
    allowed = key_pos[None, :] <= query_pos[:, None]
    return (jnp.where(allowed[None, None], scores, masked_score), query_block, key_block)


def attend_forward(query, key_rows, values, block_rows):
    length = query.shape[1]
    outputs = []
    totals = []
    for block_start in range(0, length, block_rows):
        key_stop = block_start + block_rows
        scores, query_block, key_block = block_scores(query, key_rows, block_start, block_rows)
        row_max = jnp.max(scores, axis=-1, keepdims=True)
        log_total = row_max + jnp.log(jnp.sum(jnp.exp(scores - row_max), axis=-1, keepdims=True))
        probs_low = jnp.exp(scores - log_total).astype(jnp.bfloat16)
        outputs.append(
            jnp.einsum(
                "bhqk,bkhd->bqhd",
                probs_low,
                values[:, :key_stop],
                preferred_element_type=jnp.float32,
            )
        )
        totals.append(log_total)
    return (jnp.concatenate(outputs, axis=1), totals)


def attend_backward(query, key_rows, values, attn_grad, totals, block_rows):
    length = query.shape[1]
    score_scale = 1.0 / math.sqrt(HEAD)
    keys_grad = jnp.zeros(key_rows.shape, jnp.float32)
    values_grad = jnp.zeros(values.shape, jnp.float32)
    query_grads = []
    for block_number, block_start in enumerate(range(0, length, block_rows)):
        key_stop = block_start + block_rows
        scores, query_block, key_block = block_scores(query, key_rows, block_start, block_rows)
        value_block = values[:, :key_stop]
        grad_block = attn_grad[:, block_start:key_stop]
        probs_full = jnp.exp(scores - totals[block_number])
        probs_low = probs_full.astype(jnp.bfloat16)
        probs_grad = jnp.einsum(
            "bqhd,bkhd->bhqk", grad_block, value_block, preferred_element_type=jnp.float32
        )
        row_dot = jnp.sum(probs_full * probs_grad, axis=-1, keepdims=True)
        scores_grad = (probs_full * (probs_grad - row_dot)).astype(jnp.bfloat16)
        query_grads.append(
            jnp.einsum(
                "bhqk,bkhd->bqhd", scores_grad, key_block, preferred_element_type=jnp.float32
            )
            * score_scale
        )
        pad_rows = ((0, 0), (0, length - key_stop), (0, 0), (0, 0))
        keys_grad = keys_grad + jnp.pad(
            jnp.einsum(
                "bhqk,bqhd->bkhd", scores_grad, query_block, preferred_element_type=jnp.float32
            )
            * score_scale,
            pad_rows,
        )
        values_grad = values_grad + jnp.pad(
            jnp.einsum(
                "bhqk,bqhd->bkhd", probs_low, grad_block, preferred_element_type=jnp.float32
            ),
            pad_rows,
        )
    return (
        jnp.concatenate(query_grads, axis=1),
        keys_grad,
        values_grad,
    )


def swap_cores(block):
    count = lax.axis_size("wide")
    return lax.ppermute(block, "wide", [(index, index ^ 1) for index in range(count)])


def gather_mine(shard, core, split_axis, gather_axis):
    half = shard.shape[split_axis] // 2
    mine = lax.dynamic_slice_in_dim(shard, core * half, half, axis=split_axis)
    return lax.all_gather(mine, "narrow", axis=gather_axis, tiled=True)


def gather_halves(shard, core, split_axis, gather_axis):
    return join_halves(gather_mine(shard, core, split_axis, gather_axis), core, split_axis)


def join_halves(gathered, core, split_axis):
    partner = swap_cores(gathered)
    first = jnp.where(core == 0, gathered, partner)
    second = jnp.where(core == 0, partner, gathered)
    return jnp.concatenate([first, second], axis=split_axis)


def reduce_halves(rows, core, split_axis, scatter_axis):
    half = rows.shape[split_axis] // 2
    mine = lax.dynamic_slice_in_dim(rows, core * half, half, axis=split_axis)
    other = lax.dynamic_slice_in_dim(rows, (1 - core) * half, half, axis=split_axis)
    chip_sum = mine + swap_cores(other.astype(jnp.bfloat16)).astype(jnp.float32)
    part = lax.psum_scatter(
        chip_sum.astype(jnp.bfloat16), "narrow", scatter_dimension=scatter_axis, tiled=True
    )
    empty = jnp.zeros_like(part)
    return jnp.stack(
        [jnp.where(core == 0, part, empty), jnp.where(core == 0, empty, part)], axis=split_axis
    )


def reduce_column_halves(mats, core):
    count = lax.axis_size("narrow")
    pieces = []
    for rows in mats:
        half = rows.shape[1] // 2
        mine = lax.dynamic_slice_in_dim(rows, core * half, half, axis=1)
        other = lax.dynamic_slice_in_dim(rows, (1 - core) * half, half, axis=1)
        chip_sum = mine + swap_cores(other.astype(jnp.bfloat16)).astype(jnp.float32)
        pieces.append(chip_sum.astype(jnp.bfloat16).reshape(count, -1, half))
    joined = lax.psum_scatter(
        jnp.concatenate(pieces, axis=1), "narrow", scatter_dimension=0, tiled=True
    )[0]
    results = []
    start = 0
    for piece in pieces:
        part = joined[start : start + piece.shape[1]]
        start += piece.shape[1]
        empty = jnp.zeros_like(part)
        results.append(
            jnp.stack([jnp.where(core == 0, part, empty), jnp.where(core == 0, empty, part)], axis=1)
        )
    return results


def swap_pairs(block):
    count = lax.axis_size("wide")
    return lax.ppermute(block, "wide", [(index, index ^ 2) for index in range(count)])


def sum_slots(slots, core, split_axis):
    if lax.axis_size("wide") != 4:
        return merge_slots(lax.psum(slots, "wide"), split_axis).astype(jnp.float32)
    part = lax.dynamic_index_in_dim(slots, core, axis=split_axis, keepdims=False)
    pair_sum = part.astype(jnp.float32) + swap_pairs(part).astype(jnp.float32)
    other = swap_cores(pair_sum)
    first = jnp.where(core == 0, pair_sum, other)
    second = jnp.where(core == 0, other, pair_sum)
    return jnp.concatenate([first, second], axis=split_axis)


def sum_wide(block):
    low_block = block.astype(jnp.bfloat16)
    if lax.axis_size("wide") != 4:
        return lax.psum(low_block, "wide").astype(jnp.float32)
    pair_sum = low_block.astype(jnp.float32) + swap_pairs(low_block).astype(jnp.float32)
    return pair_sum + swap_cores(pair_sum)


def merge_slots(slots, split_axis):
    shape = list(slots.shape)
    shape[split_axis : split_axis + 2] = [shape[split_axis] * shape[split_axis + 1]]
    return slots.reshape(shape)


def shards(
    tokens,
    cotangent,
    corpus_ids,
    corpus_weights,
    qkv_weight,
    qkv_bias,
    out_weight,
    out_bias,
    up_weight,
    up_bias,
    down_weight,
    down_bias,
    norm_gains,
    norm_biases,
):
    shard_rows = tokens.shape[0]
    group_rows = shard_rows * lax.axis_size("narrow")
    seq_count = corpus_ids.shape[0]
    length = group_rows // seq_count
    block_rows = min(512, length)
    inner = qkv_weight.shape[2]
    first_row = lax.axis_index("narrow") * shard_rows
    cos_table, sine_table = rotary_tables(length, HEAD)
    layer_in = tokens.astype(jnp.float32)
    normed_first, inverse_first = norm_stats(layer_in)
    low_first = (normed_first * norm_gains[0] + norm_biases[0]).astype(jnp.bfloat16)
    core = lax.axis_index("wide") % 2
    model = layer_in.shape[1]
    heads_here = inner // HEAD
    bias_flat = jnp.concatenate([qkv_bias.reshape(-1), up_bias])
    bias_full = lax.all_gather(bias_flat, "narrow", axis=0)
    gathered_first = lax.all_gather(low_first, "narrow", axis=0, tiled=True)
    gathered_first, up_weight, down_weight, bias_full = lax.optimization_barrier(
        (gathered_first, up_weight, down_weight, bias_full)
    )
    up_bias_full = bias_full[:, 3 * inner :].reshape(-1)
    query, key_rows, values = project_qkv(
        gathered_first, qkv_weight, qkv_bias, cos_table, sine_table, seq_count, length
    )
    attn_heads, totals = attend_forward(query, key_rows, values, block_rows)
    attn_low = attn_heads.reshape(group_rows, inner).astype(jnp.bfloat16)
    attn_rows = lax.all_to_all(attn_low, "narrow", 0, 1, tiled=True)
    out_full = lax.all_gather(out_weight, "narrow", axis=0, tiled=True)
    pre_attn = jnp.dot(attn_rows, out_full, preferred_element_type=jnp.float32) + out_bias
    normed_second, inverse_second = norm_stats(pre_attn)
    residual = layer_in + normed_second * norm_gains[1] + norm_biases[1]
    normed_third, inverse_third = norm_stats(residual)
    low_third = (normed_third * norm_gains[2] + norm_biases[2]).astype(jnp.bfloat16)
    up_full = gather_halves(up_weight, core, 0, 1)
    down_full = gather_halves(down_weight, core, 1, 0)
    hidden = jnp.dot(low_third, up_full, preferred_element_type=jnp.float32) + up_bias_full
    act_low = gelu_value(hidden).astype(jnp.bfloat16)
    act_low, qkv_late = lax.optimization_barrier((act_low, qkv_weight))
    qkv_full = join_halves(gather_mine(qkv_late, core, 1, 2), core, 1)
    pre_mlp = jnp.dot(act_low, down_full, preferred_element_type=jnp.float32) + down_bias
    normed_fourth, inverse_fourth = norm_stats(pre_mlp)
    final_sum = residual + normed_fourth * norm_gains[3] + norm_biases[3]
    layer_out = final_sum.astype(jnp.bfloat16)
    row_sequence = (first_row + jnp.arange(shard_rows, dtype=jnp.int32)) // length
    row_corpus = jnp.sum(
        jnp.where(
            row_sequence[:, None] == jnp.arange(seq_count, dtype=jnp.int32)[None, :],
            corpus_ids[None, :],
            0,
        ),
        axis=1,
    )
    row_weight = jnp.sum(
        jnp.where(
            row_corpus[:, None] == jnp.arange(corpus_weights.shape[0], dtype=jnp.int32)[None, :],
            corpus_weights[None, :],
            0.0,
        ),
        axis=1,
    )
    upstream = cotangent.astype(jnp.float32) * row_weight[:, None]
    mlp_grad = norm_back(normed_fourth, inverse_fourth, norm_gains[3], upstream).astype(
        jnp.bfloat16
    )
    down_wgrad_rows = lax.dot_general(
        act_low, mlp_grad, (((0,), (0,)), ((), ())), preferred_element_type=jnp.float32
    )
    act_grad = lax.dot_general(
        mlp_grad, down_full, (((1,), (1,)), ((), ())), preferred_element_type=jnp.float32
    )
    hidden_grad = (act_grad * gelu_slope(hidden)).astype(jnp.bfloat16)
    up_bgrad_rows = jnp.sum(hidden_grad.astype(jnp.float32), axis=0)
    up_wgrad_rows = lax.dot_general(
        low_third, hidden_grad, (((0,), (0,)), ((), ())), preferred_element_type=jnp.float32
    )
    third_grad = lax.dot_general(
        hidden_grad, up_full, (((1,), (1,)), ((), ())), preferred_element_type=jnp.float32
    )
    up_slots = reduce_halves(up_wgrad_rows, core, 0, 1)
    residual_grad = upstream + norm_back(normed_third, inverse_third, norm_gains[2], third_grad)
    branch_grad = norm_back(normed_second, inverse_second, norm_gains[1], residual_grad).astype(
        jnp.bfloat16
    )
    attn_grad_rows = lax.dot_general(
        branch_grad, out_full, (((1,), (1,)), ((), ())), preferred_element_type=jnp.float32
    ).astype(jnp.bfloat16)
    attn_grad = lax.all_to_all(attn_grad_rows, "narrow", 1, 0, tiled=True)
    attn_grad = attn_grad.reshape(query.shape)
    query_grad, keys_grad, values_grad = attend_backward(
        query, key_rows, values, attn_grad, totals, block_rows
    )
    out_wgrad_rows = lax.dot_general(
        attn_rows, branch_grad, (((0,), (0,)), ((), ())), preferred_element_type=jnp.float32
    )
    down_slots, out_slots = reduce_column_halves((down_wgrad_rows, out_wgrad_rows), core)
    qkv_grad = jnp.stack(
        [
            rotate_back(query_grad, cos_table, sine_table),
            rotate_back(keys_grad, cos_table, sine_table),
            values_grad,
        ]
    )
    qkv_grad = qkv_grad.reshape(3, group_rows, inner).astype(jnp.bfloat16)
    qkv_bgrad = jnp.sum(qkv_grad.astype(jnp.float32), axis=1)
    qkv_grad_rows = lax.all_to_all(
        qkv_grad.reshape(3, group_rows, heads_here, HEAD), "narrow", 1, 2, tiled=True
    ).reshape(3, shard_rows, model)
    qkv_wgrad = jnp.einsum(
        "sd,tse->tde", gathered_first, qkv_grad, preferred_element_type=jnp.float32
    )
    first_grad = jnp.einsum(
        "tse,tde->sd", qkv_grad_rows, qkv_full, preferred_element_type=jnp.float32
    )
    input_grad = (
        residual_grad + norm_back(normed_first, inverse_first, norm_gains[0], first_grad)
    ).astype(jnp.bfloat16)
    gain_local = jnp.stack(
        [
            jnp.sum(first_grad * normed_first, axis=0),
            jnp.sum(residual_grad * normed_second, axis=0),
            jnp.sum(third_grad * normed_third, axis=0),
            jnp.sum(upstream * normed_fourth, axis=0),
        ]
    )
    bias_local = jnp.stack(
        [
            jnp.sum(first_grad, axis=0),
            jnp.sum(residual_grad, axis=0),
            jnp.sum(third_grad, axis=0),
            jnp.sum(upstream, axis=0),
        ]
    )
    out_blocal = jnp.sum(branch_grad.astype(jnp.float32), axis=0)
    down_blocal = jnp.sum(mlp_grad.astype(jnp.float32), axis=0)
    weight_sums = (
        sum_wide(qkv_wgrad),
        sum_wide(qkv_bgrad),
        sum_slots(out_slots, core, 1),
        sum_slots(up_slots, core, 0),
        None,
        sum_slots(down_slots, core, 1),
    )
    small_sums = lax.psum(
        (gain_local, bias_local, out_blocal, down_blocal, up_bgrad_rows), ("wide", "narrow")
    )
    units = up_bias.shape[0]
    up_bgrad = lax.dynamic_slice_in_dim(small_sums[4], lax.axis_index("narrow") * units, units)
    up_wgrad = weight_sums[3]
    down_wgrad = weight_sums[5]
    out_wgrad = weight_sums[2]
    qkv_wgrad = weight_sums[0]
    return (
        layer_out,
        input_grad,
        qkv_wgrad,
        weight_sums[1],
        out_wgrad,
        small_sums[2],
        up_wgrad,
        up_bgrad,
        down_wgrad,
        small_sums[3],
        small_sums[0],
        small_sums[1],
    )


def solution(mesh):
    return jax.shard_map(
        shards,
        mesh=mesh,
        in_specs=(
            P(("wide", "narrow"), None),
            P(("wide", "narrow"), None),
            P("wide"),
            P(),
            P(None, None, "narrow"),
            P(None, "narrow"),
            P("narrow", None),
            P(),
            P(None, "narrow"),
            P("narrow"),
            P("narrow", None),
            P(),
            P(),
            P(),
        ),
        out_specs=(
            P(("wide", "narrow"), None),
            P(("wide", "narrow"), None),
            P(None, None, "narrow"),
            P(None, "narrow"),
            P("narrow", None),
            P(),
            P(None, "narrow"),
            P("narrow"),
            P("narrow", None),
            P(),
            P(),
            P(),
        ),
        check_vma=False,
    )
```

```python
import math

import jax
import jax.numpy as jnp
from jax import lax
from jax.sharding import PartitionSpec as P

HEAD = 64


epsilon = 1e-05
root_half = 0.7071067811865476
gauss_norm = 0.3989422804014327
masked_score = -1e30


def norm_stats(vec_in):
    center = vec_in - jnp.mean(vec_in, axis=-1, keepdims=True)
    inverse = lax.rsqrt(jnp.mean(center * center, axis=-1, keepdims=True) + epsilon)
    return (center * inverse, inverse)


def norm_back(normed, inverse, gain_row, upstream):
    scaled = upstream * gain_row
    return inverse * (
        scaled
        - jnp.mean(scaled, axis=-1, keepdims=True)
        - normed * jnp.mean(scaled * normed, axis=-1, keepdims=True)
    )


def rotary_tables(length, head_size):
    half_size = head_size // 2
    inv_freq = jnp.exp(jnp.arange(half_size, dtype=jnp.float32) * (-math.log(10000.0) / half_size))
    angles = jnp.arange(length, dtype=jnp.float32)[:, None] * inv_freq[None, :]
    return (jnp.cos(angles), jnp.sin(angles))


def rotate(vectors, cos_table, sine_table):
    half_size = vectors.shape[-1] // 2
    front_half = vectors[..., :half_size]
    back_half = vectors[..., half_size:]
    cos_grid = cos_table[:, None, :]
    sin_grid = sine_table[:, None, :]
    return jnp.concatenate(
        [
            front_half * cos_grid - back_half * sin_grid,
            front_half * sin_grid + back_half * cos_grid,
        ],
        axis=-1,
    )


def rotate_back(vectors, cos_table, sine_table):
    half_size = vectors.shape[-1] // 2
    front_half = vectors[..., :half_size]
    back_half = vectors[..., half_size:]
    cos_grid = cos_table[:, None, :]
    sin_grid = sine_table[:, None, :]
    return jnp.concatenate(
        [
            front_half * cos_grid + back_half * sin_grid,
            back_half * cos_grid - front_half * sin_grid,
        ],
        axis=-1,
    )


def gelu_value(hidden):
    return 0.5 * hidden * (1.0 + lax.erf(hidden * root_half))


def gelu_slope(hidden):
    return (
        0.5 * (1.0 + lax.erf(hidden * root_half))
        + hidden * jnp.exp(-0.5 * hidden * hidden) * gauss_norm
    )


def project_qkv(gathered, qkv_weight, qkv_bias, cos_table, sine_table, seq_count, length):
    heads_here = qkv_weight.shape[2] // HEAD
    qkv_pre = (
        jnp.einsum("sd,tde->tse", gathered, qkv_weight, preferred_element_type=jnp.float32)
        + qkv_bias[:, None, :]
    )
    shaped = qkv_pre.reshape(3, seq_count, length, heads_here, HEAD)
    query = rotate(shaped[0], cos_table, sine_table).astype(jnp.bfloat16)
    key_rows = rotate(shaped[1], cos_table, sine_table).astype(jnp.bfloat16)
    values = shaped[2].astype(jnp.bfloat16)
    return (query, key_rows, values)


def block_scores(query, key_rows, block_start, block_rows):
    key_stop = block_start + block_rows
    query_block = query[:, block_start:key_stop]
    key_block = key_rows[:, :key_stop]
    scores = jnp.einsum(
        "bqhd,bkhd->bhqk", query_block, key_block, preferred_element_type=jnp.float32
    ) * (1.0 / math.sqrt(HEAD))
    query_pos = block_start + jnp.arange(block_rows)
    key_pos = jnp.arange(key_stop)
    allowed = key_pos[None, :] <= query_pos[:, None]
    return (jnp.where(allowed[None, None], scores, masked_score), query_block, key_block)


def attend_forward(query, key_rows, values, block_rows):
    length = query.shape[1]
    outputs = []
    totals = []
    for block_start in range(0, length, block_rows):
        key_stop = block_start + block_rows
        scores, query_block, key_block = block_scores(query, key_rows, block_start, block_rows)
        row_max = jnp.max(scores, axis=-1, keepdims=True)
        log_total = row_max + jnp.log(jnp.sum(jnp.exp(scores - row_max), axis=-1, keepdims=True))
        probs_low = jnp.exp(scores - log_total).astype(jnp.bfloat16)
        outputs.append(
            jnp.einsum(
                "bhqk,bkhd->bqhd",
                probs_low,
                values[:, :key_stop],
                preferred_element_type=jnp.float32,
            )
        )
        totals.append(log_total)
    return (jnp.concatenate(outputs, axis=1), totals)


def attend_backward(query, key_rows, values, attn_grad, totals, block_rows):
    length = query.shape[1]
    score_scale = 1.0 / math.sqrt(HEAD)
    keys_grad = jnp.zeros(key_rows.shape, jnp.float32)
    values_grad = jnp.zeros(values.shape, jnp.float32)
    query_grads = []
    for block_number, block_start in enumerate(range(0, length, block_rows)):
        key_stop = block_start + block_rows
        scores, query_block, key_block = block_scores(query, key_rows, block_start, block_rows)
        value_block = values[:, :key_stop]
        grad_block = attn_grad[:, block_start:key_stop]
        probs_full = jnp.exp(scores - totals[block_number])
        probs_low = probs_full.astype(jnp.bfloat16)
        probs_grad = jnp.einsum(
            "bqhd,bkhd->bhqk", grad_block, value_block, preferred_element_type=jnp.float32
        )
        row_dot = jnp.sum(probs_full * probs_grad, axis=-1, keepdims=True)
        scores_grad = (probs_full * (probs_grad - row_dot)).astype(jnp.bfloat16)
        query_grads.append(
            jnp.einsum(
                "bhqk,bkhd->bqhd", scores_grad, key_block, preferred_element_type=jnp.float32
            )
            * score_scale
        )
        pad_rows = ((0, 0), (0, length - key_stop), (0, 0), (0, 0))
        keys_grad = keys_grad + jnp.pad(
            jnp.einsum(
                "bhqk,bqhd->bkhd", scores_grad, query_block, preferred_element_type=jnp.float32
            )
            * score_scale,
            pad_rows,
        )
        values_grad = values_grad + jnp.pad(
            jnp.einsum(
                "bhqk,bqhd->bkhd", probs_low, grad_block, preferred_element_type=jnp.float32
            ),
            pad_rows,
        )
    return (
        jnp.concatenate(query_grads, axis=1),
        keys_grad,
        values_grad,
    )


def swap_cores(block):
    count = lax.axis_size("wide")
    return lax.ppermute(block, "wide", [(index, index ^ 1) for index in range(count)])


def gather_mine(shard, core, split_axis, gather_axis):
    half = shard.shape[split_axis] // 2
    mine = lax.dynamic_slice_in_dim(shard, core * half, half, axis=split_axis)
    return lax.all_gather(mine, "narrow", axis=gather_axis, tiled=True)


def gather_halves(shard, core, split_axis, gather_axis):
    return join_halves(gather_mine(shard, core, split_axis, gather_axis), core, split_axis)


def join_halves(gathered, core, split_axis):
    partner = swap_cores(gathered)
    first = jnp.where(core == 0, gathered, partner)
    second = jnp.where(core == 0, partner, gathered)
    return jnp.concatenate([first, second], axis=split_axis)


def reduce_halves(rows, core, split_axis, scatter_axis):
    half = rows.shape[split_axis] // 2
    mine = lax.dynamic_slice_in_dim(rows, core * half, half, axis=split_axis)
    other = lax.dynamic_slice_in_dim(rows, (1 - core) * half, half, axis=split_axis)
    chip_sum = mine + swap_cores(other.astype(jnp.bfloat16)).astype(jnp.float32)
    part = lax.psum_scatter(
        chip_sum.astype(jnp.bfloat16), "narrow", scatter_dimension=scatter_axis, tiled=True
    )
    empty = jnp.zeros_like(part)
    return jnp.stack(
        [jnp.where(core == 0, part, empty), jnp.where(core == 0, empty, part)], axis=split_axis
    )


def reduce_column_halves(mats, core):
    count = lax.axis_size("narrow")
    pieces = []
    for rows in mats:
        half = rows.shape[1] // 2
        mine = lax.dynamic_slice_in_dim(rows, core * half, half, axis=1)
        other = lax.dynamic_slice_in_dim(rows, (1 - core) * half, half, axis=1)
        chip_sum = mine + swap_cores(other.astype(jnp.bfloat16)).astype(jnp.float32)
        pieces.append(chip_sum.astype(jnp.bfloat16).reshape(count, -1, half))
    joined = lax.psum_scatter(
        jnp.concatenate(pieces, axis=1), "narrow", scatter_dimension=0, tiled=True
    )[0]
    results = []
    start = 0
    for piece in pieces:
        part = joined[start : start + piece.shape[1]]
        start += piece.shape[1]
        empty = jnp.zeros_like(part)
        results.append(
            jnp.stack([jnp.where(core == 0, part, empty), jnp.where(core == 0, empty, part)], axis=1)
        )
    return results


def merge_slots(slots, split_axis):
    shape = list(slots.shape)
    shape[split_axis : split_axis + 2] = [shape[split_axis] * shape[split_axis + 1]]
    return slots.reshape(shape)


def shards(
    tokens,
    cotangent,
    corpus_ids,
    corpus_weights,
    qkv_weight,
    qkv_bias,
    out_weight,
    out_bias,
    up_weight,
    up_bias,
    down_weight,
    down_bias,
    norm_gains,
    norm_biases,
):
    shard_rows = tokens.shape[0]
    group_rows = shard_rows * lax.axis_size("narrow")
    seq_count = corpus_ids.shape[0]
    length = group_rows // seq_count
    block_rows = min(512, length)
    inner = qkv_weight.shape[2]
    first_row = lax.axis_index("narrow") * shard_rows
    cos_table, sine_table = rotary_tables(length, HEAD)
    layer_in = tokens.astype(jnp.float32)
    normed_first, inverse_first = norm_stats(layer_in)
    low_first = (normed_first * norm_gains[0] + norm_biases[0]).astype(jnp.bfloat16)
    core = lax.axis_index("wide") % 2
    model = layer_in.shape[1]
    heads_here = inner // HEAD
    bias_flat = jnp.concatenate([qkv_bias.reshape(-1), up_bias])
    bias_full = lax.all_gather(bias_flat, "narrow", axis=0)
    gathered_first = lax.all_gather(low_first, "narrow", axis=0, tiled=True)
    gathered_first, out_weight, bias_full = lax.optimization_barrier(
        (gathered_first, out_weight, bias_full)
    )
    out_gathered = gather_mine(out_weight, core, 1, 0)
    out_gathered, up_weight, down_weight = lax.optimization_barrier(
        (out_gathered, up_weight, down_weight)
    )
    up_bias_full = bias_full[:, 3 * inner :].reshape(-1)
    query, key_rows, values = project_qkv(
        gathered_first, qkv_weight, qkv_bias, cos_table, sine_table, seq_count, length
    )
    attn_heads, totals = attend_forward(query, key_rows, values, block_rows)
    attn_low = attn_heads.reshape(group_rows, inner).astype(jnp.bfloat16)
    attn_rows = lax.all_to_all(attn_low, "narrow", 0, 1, tiled=True)
    out_full = join_halves(out_gathered, core, 1)
    pre_attn = jnp.dot(attn_rows, out_full, preferred_element_type=jnp.float32) + out_bias
    normed_second, inverse_second = norm_stats(pre_attn)
    residual = layer_in + normed_second * norm_gains[1] + norm_biases[1]
    normed_third, inverse_third = norm_stats(residual)
    low_third = (normed_third * norm_gains[2] + norm_biases[2]).astype(jnp.bfloat16)
    up_full = gather_halves(up_weight, core, 0, 1)
    down_full = gather_halves(down_weight, core, 1, 0)
    hidden = jnp.dot(low_third, up_full, preferred_element_type=jnp.float32) + up_bias_full
    act_low = gelu_value(hidden).astype(jnp.bfloat16)
    act_low, qkv_late = lax.optimization_barrier((act_low, qkv_weight))
    qkv_full = join_halves(gather_mine(qkv_late, core, 1, 2), core, 1)
    pre_mlp = jnp.dot(act_low, down_full, preferred_element_type=jnp.float32) + down_bias
    normed_fourth, inverse_fourth = norm_stats(pre_mlp)
    final_sum = residual + normed_fourth * norm_gains[3] + norm_biases[3]
    layer_out = final_sum.astype(jnp.bfloat16)
    row_sequence = (first_row + jnp.arange(shard_rows, dtype=jnp.int32)) // length
    row_corpus = jnp.sum(
        jnp.where(
            row_sequence[:, None] == jnp.arange(seq_count, dtype=jnp.int32)[None, :],
            corpus_ids[None, :],
            0,
        ),
        axis=1,
    )
    row_weight = jnp.sum(
        jnp.where(
            row_corpus[:, None] == jnp.arange(corpus_weights.shape[0], dtype=jnp.int32)[None, :],
            corpus_weights[None, :],
            0.0,
        ),
        axis=1,
    )
    upstream = cotangent.astype(jnp.float32) * row_weight[:, None]
    mlp_grad = norm_back(normed_fourth, inverse_fourth, norm_gains[3], upstream).astype(
        jnp.bfloat16
    )
    down_wgrad_rows = lax.dot_general(
        act_low, mlp_grad, (((0,), (0,)), ((), ())), preferred_element_type=jnp.float32
    )
    act_grad = lax.dot_general(
        mlp_grad, down_full, (((1,), (1,)), ((), ())), preferred_element_type=jnp.float32
    )
    hidden_grad = (act_grad * gelu_slope(hidden)).astype(jnp.bfloat16)
    up_bgrad_rows = jnp.sum(hidden_grad.astype(jnp.float32), axis=0)
    up_wgrad_rows = lax.dot_general(
        low_third, hidden_grad, (((0,), (0,)), ((), ())), preferred_element_type=jnp.float32
    )
    third_grad = lax.dot_general(
        hidden_grad, up_full, (((1,), (1,)), ((), ())), preferred_element_type=jnp.float32
    )
    up_slots = reduce_halves(up_wgrad_rows, core, 0, 1)
    residual_grad = upstream + norm_back(normed_third, inverse_third, norm_gains[2], third_grad)
    branch_grad = norm_back(normed_second, inverse_second, norm_gains[1], residual_grad).astype(
        jnp.bfloat16
    )
    attn_grad_rows = lax.dot_general(
        branch_grad, out_full, (((1,), (1,)), ((), ())), preferred_element_type=jnp.float32
    ).astype(jnp.bfloat16)
    attn_grad = lax.all_to_all(attn_grad_rows, "narrow", 1, 0, tiled=True)
    attn_grad = attn_grad.reshape(query.shape)
    query_grad, keys_grad, values_grad = attend_backward(
        query, key_rows, values, attn_grad, totals, block_rows
    )
    out_wgrad_rows = lax.dot_general(
        attn_rows, branch_grad, (((0,), (0,)), ((), ())), preferred_element_type=jnp.float32
    )
    down_slots, out_slots = reduce_column_halves((down_wgrad_rows, out_wgrad_rows), core)
    qkv_grad = jnp.stack(
        [
            rotate_back(query_grad, cos_table, sine_table),
            rotate_back(keys_grad, cos_table, sine_table),
            values_grad,
        ]
    )
    qkv_grad = qkv_grad.reshape(3, group_rows, inner).astype(jnp.bfloat16)
    qkv_bgrad = jnp.sum(qkv_grad.astype(jnp.float32), axis=1)
    qkv_grad_rows = lax.all_to_all(
        qkv_grad.reshape(3, group_rows, heads_here, HEAD), "narrow", 1, 2, tiled=True
    ).reshape(3, shard_rows, model)
    qkv_wgrad = jnp.einsum(
        "sd,tse->tde", gathered_first, qkv_grad, preferred_element_type=jnp.float32
    )
    first_grad = jnp.einsum(
        "tse,tde->sd", qkv_grad_rows, qkv_full, preferred_element_type=jnp.float32
    )
    input_grad = (
        residual_grad + norm_back(normed_first, inverse_first, norm_gains[0], first_grad)
    ).astype(jnp.bfloat16)
    gain_local = jnp.stack(
        [
            jnp.sum(first_grad * normed_first, axis=0),
            jnp.sum(residual_grad * normed_second, axis=0),
            jnp.sum(third_grad * normed_third, axis=0),
            jnp.sum(upstream * normed_fourth, axis=0),
        ]
    )
    bias_local = jnp.stack(
        [
            jnp.sum(first_grad, axis=0),
            jnp.sum(residual_grad, axis=0),
            jnp.sum(third_grad, axis=0),
            jnp.sum(upstream, axis=0),
        ]
    )
    out_blocal = jnp.sum(branch_grad.astype(jnp.float32), axis=0)
    down_blocal = jnp.sum(mlp_grad.astype(jnp.float32), axis=0)
    weight_sums = (
        lax.psum(qkv_wgrad.astype(jnp.bfloat16), "wide").astype(jnp.float32),
        lax.psum(qkv_bgrad.astype(jnp.bfloat16), "wide").astype(jnp.float32),
        lax.psum(out_slots, "wide").astype(jnp.float32),
        lax.psum(up_slots, "wide").astype(jnp.float32),
        None,
        lax.psum(down_slots, "wide").astype(jnp.float32),
    )
    small_sums = lax.psum(
        (gain_local, bias_local, out_blocal, down_blocal, up_bgrad_rows), ("wide", "narrow")
    )
    units = up_bias.shape[0]
    up_bgrad = lax.dynamic_slice_in_dim(small_sums[4], lax.axis_index("narrow") * units, units)
    up_wgrad = merge_slots(weight_sums[3], 0)
    down_wgrad = merge_slots(weight_sums[5], 1)
    out_wgrad = merge_slots(weight_sums[2], 1)
    qkv_wgrad = weight_sums[0]
    return (
        layer_out,
        input_grad,
        qkv_wgrad,
        weight_sums[1],
        out_wgrad,
        small_sums[2],
        up_wgrad,
        up_bgrad,
        down_wgrad,
        small_sums[3],
        small_sums[0],
        small_sums[1],
    )


def solution(mesh):
    return jax.shard_map(
        shards,
        mesh=mesh,
        in_specs=(
            P(("wide", "narrow"), None),
            P(("wide", "narrow"), None),
            P("wide"),
            P(),
            P(None, None, "narrow"),
            P(None, "narrow"),
            P("narrow", None),
            P(),
            P(None, "narrow"),
            P("narrow"),
            P("narrow", None),
            P(),
            P(),
            P(),
        ),
        out_specs=(
            P(("wide", "narrow"), None),
            P(("wide", "narrow"), None),
            P(None, None, "narrow"),
            P(None, "narrow"),
            P("narrow", None),
            P(),
            P(None, "narrow"),
            P("narrow"),
            P("narrow", None),
            P(),
            P(),
            P(),
        ),
        check_vma=False,
    )
```

```python
import math

import jax
import jax.numpy as jnp
from jax import lax
from jax.sharding import PartitionSpec as P

HEAD = 64


epsilon = 1e-05
root_half = 0.7071067811865476
gauss_norm = 0.3989422804014327
masked_score = -1e30


def norm_stats(vec_in):
    center = vec_in - jnp.mean(vec_in, axis=-1, keepdims=True)
    inverse = lax.rsqrt(jnp.mean(center * center, axis=-1, keepdims=True) + epsilon)
    return (center * inverse, inverse)


def norm_back(normed, inverse, gain_row, upstream):
    scaled = upstream * gain_row
    return inverse * (
        scaled
        - jnp.mean(scaled, axis=-1, keepdims=True)
        - normed * jnp.mean(scaled * normed, axis=-1, keepdims=True)
    )


def rotary_tables(length, head_size):
    half_size = head_size // 2
    inv_freq = jnp.exp(jnp.arange(half_size, dtype=jnp.float32) * (-math.log(10000.0) / half_size))
    angles = jnp.arange(length, dtype=jnp.float32)[:, None] * inv_freq[None, :]
    return (jnp.cos(angles), jnp.sin(angles))


def rotate(vectors, cos_table, sine_table):
    half_size = vectors.shape[-1] // 2
    front_half = vectors[..., :half_size]
    back_half = vectors[..., half_size:]
    cos_grid = cos_table[:, None, :]
    sin_grid = sine_table[:, None, :]
    return jnp.concatenate(
        [
            front_half * cos_grid - back_half * sin_grid,
            front_half * sin_grid + back_half * cos_grid,
        ],
        axis=-1,
    )


def rotate_back(vectors, cos_table, sine_table):
    half_size = vectors.shape[-1] // 2
    front_half = vectors[..., :half_size]
    back_half = vectors[..., half_size:]
    cos_grid = cos_table[:, None, :]
    sin_grid = sine_table[:, None, :]
    return jnp.concatenate(
        [
            front_half * cos_grid + back_half * sin_grid,
            back_half * cos_grid - front_half * sin_grid,
        ],
        axis=-1,
    )


def gelu_value(hidden):
    return 0.5 * hidden * (1.0 + lax.erf(hidden * root_half))


def gelu_slope(hidden):
    return (
        0.5 * (1.0 + lax.erf(hidden * root_half))
        + hidden * jnp.exp(-0.5 * hidden * hidden) * gauss_norm
    )


def project_qkv(gathered, qkv_weight, qkv_bias, cos_table, sine_table, seq_count, length):
    heads_here = qkv_weight.shape[2] // HEAD
    qkv_pre = (
        jnp.einsum("sd,tde->tse", gathered, qkv_weight, preferred_element_type=jnp.float32)
        + qkv_bias[:, None, :]
    )
    shaped = qkv_pre.reshape(3, seq_count, length, heads_here, HEAD)
    query = rotate(shaped[0], cos_table, sine_table).astype(jnp.bfloat16)
    key_rows = rotate(shaped[1], cos_table, sine_table).astype(jnp.bfloat16)
    values = shaped[2].astype(jnp.bfloat16)
    return (query, key_rows, values)


def block_scores(query, key_rows, block_start, block_rows):
    key_stop = block_start + block_rows
    query_block = query[:, block_start:key_stop]
    key_block = key_rows[:, :key_stop]
    scores = jnp.einsum(
        "bqhd,bkhd->bhqk", query_block, key_block, preferred_element_type=jnp.float32
    ) * (1.0 / math.sqrt(HEAD))
    query_pos = block_start + jnp.arange(block_rows)
    key_pos = jnp.arange(key_stop)
    allowed = key_pos[None, :] <= query_pos[:, None]
    return (jnp.where(allowed[None, None], scores, masked_score), query_block, key_block)


def attend_forward(query, key_rows, values, block_rows):
    length = query.shape[1]
    outputs = []
    totals = []
    for block_start in range(0, length, block_rows):
        key_stop = block_start + block_rows
        scores, query_block, key_block = block_scores(query, key_rows, block_start, block_rows)
        row_max = jnp.max(scores, axis=-1, keepdims=True)
        log_total = row_max + jnp.log(jnp.sum(jnp.exp(scores - row_max), axis=-1, keepdims=True))
        probs_low = jnp.exp(scores - log_total).astype(jnp.bfloat16)
        outputs.append(
            jnp.einsum(
                "bhqk,bkhd->bqhd",
                probs_low,
                values[:, :key_stop],
                preferred_element_type=jnp.float32,
            )
        )
        totals.append(log_total)
    return (jnp.concatenate(outputs, axis=1), totals)


def attend_backward(query, key_rows, values, attn_grad, totals, block_rows):
    length = query.shape[1]
    score_scale = 1.0 / math.sqrt(HEAD)
    keys_grad = jnp.zeros(key_rows.shape, jnp.float32)
    values_grad = jnp.zeros(values.shape, jnp.float32)
    query_grads = []
    for block_number, block_start in enumerate(range(0, length, block_rows)):
        key_stop = block_start + block_rows
        scores, query_block, key_block = block_scores(query, key_rows, block_start, block_rows)
        value_block = values[:, :key_stop]
        grad_block = attn_grad[:, block_start:key_stop]
        probs_full = jnp.exp(scores - totals[block_number])
        probs_low = probs_full.astype(jnp.bfloat16)
        probs_grad = jnp.einsum(
            "bqhd,bkhd->bhqk", grad_block, value_block, preferred_element_type=jnp.float32
        )
        row_dot = jnp.sum(probs_full * probs_grad, axis=-1, keepdims=True)
        scores_grad = (probs_full * (probs_grad - row_dot)).astype(jnp.bfloat16)
        query_grads.append(
            jnp.einsum(
                "bhqk,bkhd->bqhd", scores_grad, key_block, preferred_element_type=jnp.float32
            )
            * score_scale
        )
        pad_rows = ((0, 0), (0, length - key_stop), (0, 0), (0, 0))
        keys_grad = keys_grad + jnp.pad(
            jnp.einsum(
                "bhqk,bqhd->bkhd", scores_grad, query_block, preferred_element_type=jnp.float32
            )
            * score_scale,
            pad_rows,
        )
        values_grad = values_grad + jnp.pad(
            jnp.einsum(
                "bhqk,bqhd->bkhd", probs_low, grad_block, preferred_element_type=jnp.float32
            ),
            pad_rows,
        )
    return (
        jnp.concatenate(query_grads, axis=1),
        keys_grad,
        values_grad,
    )


def swap_cores(block):
    count = lax.axis_size("wide")
    return lax.ppermute(block, "wide", [(index, index ^ 1) for index in range(count)])


def gather_mine(shard, core, split_axis, gather_axis):
    half = shard.shape[split_axis] // 2
    mine = lax.dynamic_slice_in_dim(shard, core * half, half, axis=split_axis)
    return lax.all_gather(mine, "narrow", axis=gather_axis, tiled=True)


def gather_halves(shard, core, split_axis, gather_axis):
    return join_halves(gather_mine(shard, core, split_axis, gather_axis), core, split_axis)


def join_halves(gathered, core, split_axis):
    partner = swap_cores(gathered)
    first = jnp.where(core == 0, gathered, partner)
    second = jnp.where(core == 0, partner, gathered)
    return jnp.concatenate([first, second], axis=split_axis)


def reduce_halves(rows, core, split_axis, scatter_axis):
    half = rows.shape[split_axis] // 2
    mine = lax.dynamic_slice_in_dim(rows, core * half, half, axis=split_axis)
    other = lax.dynamic_slice_in_dim(rows, (1 - core) * half, half, axis=split_axis)
    chip_sum = mine + swap_cores(other.astype(jnp.bfloat16)).astype(jnp.float32)
    part = lax.psum_scatter(
        chip_sum.astype(jnp.bfloat16), "narrow", scatter_dimension=scatter_axis, tiled=True
    )
    empty = jnp.zeros_like(part)
    return jnp.stack(
        [jnp.where(core == 0, part, empty), jnp.where(core == 0, empty, part)], axis=split_axis
    )


def reduce_column_halves(mats, core):
    count = lax.axis_size("narrow")
    pieces = []
    for rows in mats:
        half = rows.shape[1] // 2
        mine = lax.dynamic_slice_in_dim(rows, core * half, half, axis=1)
        other = lax.dynamic_slice_in_dim(rows, (1 - core) * half, half, axis=1)
        chip_sum = mine + swap_cores(other.astype(jnp.bfloat16)).astype(jnp.float32)
        pieces.append(chip_sum.astype(jnp.bfloat16).reshape(count, -1, half))
    joined = lax.psum_scatter(
        jnp.concatenate(pieces, axis=1), "narrow", scatter_dimension=0, tiled=True
    )[0]
    results = []
    start = 0
    for piece in pieces:
        part = joined[start : start + piece.shape[1]]
        start += piece.shape[1]
        empty = jnp.zeros_like(part)
        results.append(
            jnp.stack([jnp.where(core == 0, part, empty), jnp.where(core == 0, empty, part)], axis=1)
        )
    return results


def merge_slots(slots, split_axis):
    shape = list(slots.shape)
    shape[split_axis : split_axis + 2] = [shape[split_axis] * shape[split_axis + 1]]
    return slots.reshape(shape)


def shards(
    tokens,
    cotangent,
    corpus_ids,
    corpus_weights,
    qkv_weight,
    qkv_bias,
    out_weight,
    out_bias,
    up_weight,
    up_bias,
    down_weight,
    down_bias,
    norm_gains,
    norm_biases,
):
    shard_rows = tokens.shape[0]
    group_rows = shard_rows * lax.axis_size("narrow")
    seq_count = corpus_ids.shape[0]
    length = group_rows // seq_count
    block_rows = min(512, length)
    inner = qkv_weight.shape[2]
    first_row = lax.axis_index("narrow") * shard_rows
    cos_table, sine_table = rotary_tables(length, HEAD)
    layer_in = tokens.astype(jnp.float32)
    normed_first, inverse_first = norm_stats(layer_in)
    low_first = (normed_first * norm_gains[0] + norm_biases[0]).astype(jnp.bfloat16)
    core = lax.axis_index("wide") % 2
    model = layer_in.shape[1]
    heads_here = inner // HEAD
    bias_flat = jnp.concatenate([qkv_bias.reshape(-1), up_bias])
    bias_full = lax.all_gather(bias_flat, "narrow", axis=0)
    gathered_first = lax.all_gather(low_first, "narrow", axis=0, tiled=True)
    gathered_first, up_weight, down_weight, bias_full = lax.optimization_barrier(
        (gathered_first, up_weight, down_weight, bias_full)
    )
    up_bias_full = bias_full[:, 3 * inner :].reshape(-1)
    query, key_rows, values = project_qkv(
        gathered_first, qkv_weight, qkv_bias, cos_table, sine_table, seq_count, length
    )
    attn_heads, totals = attend_forward(query, key_rows, values, block_rows)
    attn_heads, qkv_late = lax.optimization_barrier((attn_heads, qkv_weight))
    qkv_full = join_halves(gather_mine(qkv_late, core, 1, 2), core, 1)
    attn_low = attn_heads.reshape(group_rows, inner).astype(jnp.bfloat16)
    attn_rows = lax.all_to_all(attn_low, "narrow", 0, 1, tiled=True)
    out_full = lax.all_gather(out_weight, "narrow", axis=0, tiled=True)
    pre_attn = jnp.dot(attn_rows, out_full, preferred_element_type=jnp.float32) + out_bias
    normed_second, inverse_second = norm_stats(pre_attn)
    residual = layer_in + normed_second * norm_gains[1] + norm_biases[1]
    normed_third, inverse_third = norm_stats(residual)
    low_third = (normed_third * norm_gains[2] + norm_biases[2]).astype(jnp.bfloat16)
    up_full = gather_halves(up_weight, core, 0, 1)
    down_full = gather_halves(down_weight, core, 1, 0)
    hidden = jnp.dot(low_third, up_full, preferred_element_type=jnp.float32) + up_bias_full
    act_low = gelu_value(hidden).astype(jnp.bfloat16)
    pre_mlp = jnp.dot(act_low, down_full, preferred_element_type=jnp.float32) + down_bias
    normed_fourth, inverse_fourth = norm_stats(pre_mlp)
    final_sum = residual + normed_fourth * norm_gains[3] + norm_biases[3]
    layer_out = final_sum.astype(jnp.bfloat16)
    row_sequence = (first_row + jnp.arange(shard_rows, dtype=jnp.int32)) // length
    row_corpus = jnp.sum(
        jnp.where(
            row_sequence[:, None] == jnp.arange(seq_count, dtype=jnp.int32)[None, :],
            corpus_ids[None, :],
            0,
        ),
        axis=1,
    )
    row_weight = jnp.sum(
        jnp.where(
            row_corpus[:, None] == jnp.arange(corpus_weights.shape[0], dtype=jnp.int32)[None, :],
            corpus_weights[None, :],
            0.0,
        ),
        axis=1,
    )
    upstream = cotangent.astype(jnp.float32) * row_weight[:, None]
    mlp_grad = norm_back(normed_fourth, inverse_fourth, norm_gains[3], upstream).astype(
        jnp.bfloat16
    )
    down_wgrad_rows = lax.dot_general(
        act_low, mlp_grad, (((0,), (0,)), ((), ())), preferred_element_type=jnp.float32
    )
    act_grad = lax.dot_general(
        mlp_grad, down_full, (((1,), (1,)), ((), ())), preferred_element_type=jnp.float32
    )
    hidden_grad = (act_grad * gelu_slope(hidden)).astype(jnp.bfloat16)
    up_bgrad_rows = jnp.sum(hidden_grad.astype(jnp.float32), axis=0)
    up_wgrad_rows = lax.dot_general(
        low_third, hidden_grad, (((0,), (0,)), ((), ())), preferred_element_type=jnp.float32
    )
    third_grad = lax.dot_general(
        hidden_grad, up_full, (((1,), (1,)), ((), ())), preferred_element_type=jnp.float32
    )
    up_slots = reduce_halves(up_wgrad_rows, core, 0, 1)
    residual_grad = upstream + norm_back(normed_third, inverse_third, norm_gains[2], third_grad)
    branch_grad = norm_back(normed_second, inverse_second, norm_gains[1], residual_grad).astype(
        jnp.bfloat16
    )
    attn_grad_rows = lax.dot_general(
        branch_grad, out_full, (((1,), (1,)), ((), ())), preferred_element_type=jnp.float32
    ).astype(jnp.bfloat16)
    attn_grad = lax.all_to_all(attn_grad_rows, "narrow", 1, 0, tiled=True)
    attn_grad = attn_grad.reshape(query.shape)
    query_grad, keys_grad, values_grad = attend_backward(
        query, key_rows, values, attn_grad, totals, block_rows
    )
    out_wgrad_rows = lax.dot_general(
        attn_rows, branch_grad, (((0,), (0,)), ((), ())), preferred_element_type=jnp.float32
    )
    down_slots, out_slots = reduce_column_halves((down_wgrad_rows, out_wgrad_rows), core)
    qkv_grad = jnp.stack(
        [
            rotate_back(query_grad, cos_table, sine_table),
            rotate_back(keys_grad, cos_table, sine_table),
            values_grad,
        ]
    )
    qkv_grad = qkv_grad.reshape(3, group_rows, inner).astype(jnp.bfloat16)
    qkv_bgrad = jnp.sum(qkv_grad.astype(jnp.float32), axis=1)
    qkv_grad_rows = lax.all_to_all(
        qkv_grad.reshape(3, group_rows, heads_here, HEAD), "narrow", 1, 2, tiled=True
    ).reshape(3, shard_rows, model)
    qkv_wgrad = jnp.einsum(
        "sd,tse->tde", gathered_first, qkv_grad, preferred_element_type=jnp.float32
    )
    first_grad = jnp.einsum(
        "tse,tde->sd", qkv_grad_rows, qkv_full, preferred_element_type=jnp.float32
    )
    input_grad = (
        residual_grad + norm_back(normed_first, inverse_first, norm_gains[0], first_grad)
    ).astype(jnp.bfloat16)
    gain_local = jnp.stack(
        [
            jnp.sum(first_grad * normed_first, axis=0),
            jnp.sum(residual_grad * normed_second, axis=0),
            jnp.sum(third_grad * normed_third, axis=0),
            jnp.sum(upstream * normed_fourth, axis=0),
        ]
    )
    bias_local = jnp.stack(
        [
            jnp.sum(first_grad, axis=0),
            jnp.sum(residual_grad, axis=0),
            jnp.sum(third_grad, axis=0),
            jnp.sum(upstream, axis=0),
        ]
    )
    out_blocal = jnp.sum(branch_grad.astype(jnp.float32), axis=0)
    down_blocal = jnp.sum(mlp_grad.astype(jnp.float32), axis=0)
    weight_sums = (
        lax.psum(qkv_wgrad.astype(jnp.bfloat16), "wide").astype(jnp.float32),
        lax.psum(qkv_bgrad.astype(jnp.bfloat16), "wide").astype(jnp.float32),
        lax.psum(out_slots, "wide").astype(jnp.float32),
        lax.psum(up_slots, "wide").astype(jnp.float32),
        None,
        lax.psum(down_slots, "wide").astype(jnp.float32),
    )
    small_sums = lax.psum(
        (gain_local, bias_local, out_blocal, down_blocal, up_bgrad_rows), ("wide", "narrow")
    )
    units = up_bias.shape[0]
    up_bgrad = lax.dynamic_slice_in_dim(small_sums[4], lax.axis_index("narrow") * units, units)
    up_wgrad = merge_slots(weight_sums[3], 0)
    down_wgrad = merge_slots(weight_sums[5], 1)
    out_wgrad = merge_slots(weight_sums[2], 1)
    qkv_wgrad = weight_sums[0]
    return (
        layer_out,
        input_grad,
        qkv_wgrad,
        weight_sums[1],
        out_wgrad,
        small_sums[2],
        up_wgrad,
        up_bgrad,
        down_wgrad,
        small_sums[3],
        small_sums[0],
        small_sums[1],
    )


def solution(mesh):
    return jax.shard_map(
        shards,
        mesh=mesh,
        in_specs=(
            P(("wide", "narrow"), None),
            P(("wide", "narrow"), None),
            P("wide"),
            P(),
            P(None, None, "narrow"),
            P(None, "narrow"),
            P("narrow", None),
            P(),
            P(None, "narrow"),
            P("narrow"),
            P("narrow", None),
            P(),
            P(),
            P(),
        ),
        out_specs=(
            P(("wide", "narrow"), None),
            P(("wide", "narrow"), None),
            P(None, None, "narrow"),
            P(None, "narrow"),
            P("narrow", None),
            P(),
            P(None, "narrow"),
            P("narrow"),
            P("narrow", None),
            P(),
            P(),
            P(),
        ),
        check_vma=False,
    )
```
